128 devices in a mesh: outer: 16 (over z_hi, y, core), inner: 8 (over x, z_lo).
Axes of the slice: x: 4, y: 4, z: 4 (z_hi: 2, z_lo: 2; z = z_hi * 2 + z_lo), core: 2. Of those that a mesh axis runs over, the one named last changes fastest.
Arguments:
- q_load: bfloat16 [131072, 512], P(('outer', 'inner')), may hold values from -8 to 8
- kv_load: bfloat16 [131072, 256], P(('outer', 'inner')), may hold values from -8 to 8
- pack_dest: int32 [128, 8], P('outer'), may hold values from -1 to 31, as said below
- counts: int32 [128], P('outer'), may hold values from 0 to 8, as said below
- segment_ids: int32 [65536], P(('outer', 'inner')), may hold values from 0 to 7, never falling along the last dimension, each value on 1 to 16384 neighbouring positions
Outputs:
- attn_out: bfloat16 [65536, 512], P(('outer', 'inner'))
The draws below stay inside these ranges and needn't reach their ends.
Inputs may be any that keep to these rules, and one draw needn't show every extreme that they name: In each group of 8 loader shards that share an outer index the counts add up to 32; some shard of every group holds 8 live blocks and some holds none. `pack_dest`: live entries of a group name every block number 0 to 31 exactly once; block number t goes to the device of inner index t // 4 in the same group, as its block t % 4; a shard sends at most 1 block to one device, and some shard sends exactly 1; entries of slots that are not live are -1. `segment_ids`: never falling along the sequence.
All inputs are finite; a program needn't handle non-finite values.
Results may differ from the reference program's by a relative error of at most 0.0059.
Values may be sent and summed in bfloat16 or wider, within the bound.
No kernel may reach another device: no remote copies, remote signals or barrier semaphores. Data moves between devices by JAX's collectives and lax.ppermute only.
A program may use at most 64 MiB of HBM per device.

```python
import math
import jax
import jax.numpy as jnp
import numpy as np
from jax import lax

HEAD = 128
QH = 4
ROW = 128
DOCS = 8
SLOTS = 4
LOAD_CAP = 8
TOKENS = 65536
DOC_MOST = 16384
N_INNER = 8
DEVICES = 128


def routing_plan(key):
    base_key = jax.random.fold_in(key, 7)
    groups = DEVICES // N_INNER

    def one_group(group_index):
        group_key = jax.random.fold_in(base_key, group_index)
        shuffle = jax.random.permutation(jax.random.fold_in(group_key, 1), N_INNER)
        change = jnp.zeros((N_INNER,), jnp.int32)
        change = change.at[shuffle[0]].add(SLOTS).at[shuffle[1]].add(-SLOTS)
        change = change.at[shuffle[2]].add(SLOTS // 2).at[shuffle[3]].add(-(SLOTS // 2))
        shard_loads = SLOTS + change
        owner_ids = jax.random.permutation(jax.random.fold_in(group_key, 2), N_INNER).astype(jnp.int32)
        rotate = jax.random.randint(jax.random.fold_in(group_key, 3), (), 0, SLOTS)
        starts = jnp.cumsum(shard_loads) - shard_loads
        numbers = starts[:, None] + jnp.arange(LOAD_CAP, dtype=jnp.int32)[None, :]
        owner_of = owner_ids[numbers % N_INNER]
        slot_place = (numbers // N_INNER + rotate) % SLOTS
        live_slot = jnp.arange(LOAD_CAP, dtype=jnp.int32)[None, :] < shard_loads[:, None]
        destinations = jnp.where(live_slot, owner_of * SLOTS + slot_place, -1)
        return (destinations.astype(jnp.int32), shard_loads.astype(jnp.int32))
    destinations, shard_loads = jax.vmap(one_group)(jnp.arange(groups, dtype=jnp.int32))
    return (destinations.reshape(DEVICES, LOAD_CAP), shard_loads.reshape(DEVICES))


def draw_pack_dest(key, part):
    return routing_plan(key)[0]


def draw_counts(key, part):
    return routing_plan(key)[1]


def key_pattern(key):
    row_total = DEVICES * LOAD_CAP * ROW
    base_draw = jax.random.normal(jax.random.fold_in(key, 11), (row_total, HEAD), jnp.float32)
    return base_draw


def draw_kv_load(key, part):
    row_total = DEVICES * LOAD_CAP * ROW
    base_draw = key_pattern(key)
    key_part = jnp.clip(base_draw, -4.0, 4.0)
    value_part = jnp.clip(jax.random.normal(jax.random.fold_in(key, 12), (row_total, HEAD), jnp.float32), -4.0, 4.0)
    return jnp.concatenate([key_part, value_part], axis=1).astype(jnp.bfloat16)


def draw_q_load(key, part):
    row_total = DEVICES * LOAD_CAP * ROW
    queries = jnp.clip(jax.random.normal(jax.random.fold_in(key, 23), (row_total, QH * HEAD), jnp.float32), -4.0, 4.0)
    return queries.astype(jnp.bfloat16)


def length_profile(amount, total, reach, lean):
    portions = [(1 << 20) // math.isqrt(standing ** lean) + 1 for standing in range(2, amount + 1)]
    spare, given = total - reach - (amount - 1), [1] * (amount - 1)
    while spare > 0:
        movable = [i for i in range(amount - 1) if given[i] < reach]
        mass, remaining = sum([portions[i] for i in movable]), spare
        for i in movable:
            extra = min(reach - given[i], max(1, remaining * portions[i] // mass), spare)
            given[i] = given[i] + extra
            spare = spare - extra
    return np.array([reach] + given)


def ragged(key, count, total, limit, skew):
    if count == 2:
        one = jax.random.randint(key, (), max(1, total - limit), min(limit, total - 1) + 1)
        return jnp.stack([one, total - one])
    sizes = jnp.asarray(length_profile(count, total, limit, skew), jnp.int32)
    twos = (count - 1) // 2
    source_of, taker = sizes[1:1 + 2 * twos:2], sizes[2:2 + 2 * twos:2]
    margin = jnp.minimum(source_of - 1, limit - taker)
    shifted = jax.random.randint(jax.random.fold_in(key, 1), (twos,), 0, 1 << 20) % (margin + 1)
    sizes = sizes.at[1:1 + 2 * twos:2].set(source_of - shifted).at[2:2 + 2 * twos:2].set(taker + shifted)
    return sizes[jax.random.permutation(jax.random.fold_in(key, 2), count)]


def setup_inputs(seed: int = 0) -> dict:
    key_of = jax.random.split(jax.random.key(seed), 6)
    return {
        "q_load": draw_q_load(jax.random.fold_in(key_of[5], 71), 0),
        "kv_load": draw_kv_load(jax.random.fold_in(key_of[5], 71), 0),
        "pack_dest": draw_pack_dest(jax.random.fold_in(key_of[5], 71), 0),
        "counts": draw_counts(jax.random.fold_in(key_of[5], 71), 0),
        "segment_ids": jnp.searchsorted(jnp.cumsum(ragged(key_of[4], DOCS, TOKENS, DOC_MOST, 0)), jnp.arange(TOKENS), side="right").astype(jnp.int32),
    }


def place_blocks(loaded, targets, width):
    blocks = loaded.reshape(-1, ROW, width)
    filled = jnp.zeros((TOKENS // ROW, ROW, width), loaded.dtype)
    filled = filled.at[targets].set(blocks, mode='drop')
    return filled.reshape(TOKENS, width)

def reference(q_load, kv_load, pack_dest, counts, segment_ids):
    shard_ids = jnp.arange(pack_dest.shape[0], dtype=jnp.int32)[:, None]
    slot_ids = jnp.arange(pack_dest.shape[1], dtype=jnp.int32)[None, :]
    live_slot = slot_ids < counts[:, None]
    targets = shard_ids // N_INNER * (N_INNER * SLOTS) + pack_dest
    targets = jnp.where(live_slot, targets, TOKENS // ROW).reshape(-1).astype(jnp.int32)
    q_seq = place_blocks(q_load, targets, QH * HEAD)
    kv_seq = place_blocks(kv_load, targets, 2 * HEAD)
    queries = q_seq.astype(jnp.float32).reshape(TOKENS, QH, HEAD)
    key_rows = kv_seq[:, :HEAD].astype(jnp.float32)
    value_rows = kv_seq[:, HEAD:].astype(jnp.float32)
    positions = jnp.arange(TOKENS, dtype=jnp.int32)
    score_scale = 1.0 / math.sqrt(HEAD)
    query_block = 512 if TOKENS % 512 == 0 else TOKENS
    window = min(DOC_MOST + query_block, TOKENS)

    def attend(block_index):
        first_row = block_index * query_block
        block_queries = lax.dynamic_slice_in_dim(queries, first_row, query_block, 0)
        block_positions = first_row + jnp.arange(query_block, dtype=jnp.int32)
        block_segments = lax.dynamic_slice_in_dim(segment_ids, first_row, query_block, 0)
        start = jnp.clip(first_row + query_block - window, 0, TOKENS - window).astype(jnp.int32)
        near_keys = lax.dynamic_slice_in_dim(key_rows, start, window, 0)
        near_values = lax.dynamic_slice_in_dim(value_rows, start, window, 0)
        near_pos = lax.dynamic_slice_in_dim(positions, start, window, 0)
        near_seg = lax.dynamic_slice_in_dim(segment_ids, start, window, 0)
        scores = jnp.einsum('qhd,kd->hqk', block_queries, near_keys, precision=lax.Precision.HIGHEST) * score_scale
        visible = (near_pos[None, :] <= block_positions[:, None]) & (near_seg[None, :] == block_segments[:, None])
        masked = jnp.where(visible[None], scores, -1e+30)
        largest = lax.optimization_barrier(jnp.max(masked, axis=-1, keepdims=True))
        weights = jnp.where(visible[None], jnp.exp(masked - largest), 0.0)
        denominator = lax.optimization_barrier(jnp.sum(weights, axis=-1))
        probabilities = lax.optimization_barrier(weights.astype(jnp.bfloat16)).astype(jnp.float32)
        weighted = jnp.einsum('hqk,kd->qhd', probabilities, near_values, precision=lax.Precision.HIGHEST)
        return (weighted / denominator.T[:, :, None]).reshape(query_block, QH * HEAD).astype(jnp.bfloat16)
    blocks = lax.map(attend, jnp.arange(TOKENS // query_block, dtype=jnp.int32))
    return blocks.reshape(TOKENS, QH * HEAD)
```

```python
import math

import jax
import jax.numpy as jnp
from jax import lax
from jax.sharding import PartitionSpec as P


def shifted(value, axis, steps):
    count = lax.axis_size(axis)
    leading, last = (max(0, -steps), min(count, count - steps))
    return lax.ppermute(value, axis, [(source, source + steps) for source in range(leading, last)])


def select_rows(selector, blocks, pattern):
    return jnp.einsum(
        pattern, selector.astype(jnp.bfloat16), blocks, preferred_element_type=jnp.float32
    ).astype(jnp.bfloat16)


def local(q_load, kv_load, pack_dest, counts, segment_ids):
    group_width = lax.axis_size("inner")
    my_index = lax.axis_index("inner")
    capacity = pack_dest.shape[1]
    slot_count = capacity // 2
    pair_limit = -(-capacity // group_width)
    row_length = q_load.shape[0] // capacity
    query_width = q_load.shape[1]
    pair_width = kv_load.shape[1]
    head_size = pair_width // 2
    head_count = query_width // head_size
    slot_grid = lax.broadcasted_iota(jnp.int32, (group_width, capacity), 1)
    live_all = slot_grid < counts[:, None]
    owner_all = pack_dest // slot_count
    slot_numbers = jnp.arange(capacity, dtype=jnp.int32)
    earlier = slot_numbers[None, :] < slot_numbers[:, None]
    same_owner = owner_all[:, :, None] == owner_all[:, None, :]
    rank_all = jnp.sum(
        (earlier[None] & same_owner & live_all[:, None, :]).astype(jnp.int32), axis=2
    )
    shard_rows = jnp.arange(group_width, dtype=jnp.int32)
    mine_row = (shard_rows == my_index)[:, None]
    my_owner = jnp.sum(jnp.where(mine_row, owner_all, 0), axis=0)
    my_rank = jnp.sum(jnp.where(mine_row, rank_all, 0), axis=0)
    my_live = jnp.any(mine_row & live_all, axis=0)
    pair_ids = jnp.arange(pair_limit, dtype=jnp.int32)
    send_select = (
        my_live[None, None, :]
        & (my_owner[None, None, :] == shard_rows[:, None, None])
        & (my_rank[None, None, :] == pair_ids[None, :, None])
    )
    q_blocks = q_load.reshape(capacity, row_length, query_width)
    kv_blocks = kv_load.reshape(capacity, row_length, pair_width)
    send_q = select_rows(send_select, q_blocks, "jkc,crf->jkrf")
    send_kv = select_rows(send_select, kv_blocks, "jkc,crf->jkrf")
    recv_q, recv_kv = (
        lax.all_to_all(send_q, "inner", split_axis=0, concat_axis=0, tiled=True),
        lax.all_to_all(send_kv, "inner", split_axis=0, concat_axis=0, tiled=True),
    )
    wanted = my_index * slot_count + jnp.arange(slot_count, dtype=jnp.int32)
    take_select = jnp.any(
        live_all[None, :, None, :]
        & (pack_dest[None, :, None, :] == wanted[:, None, None, None])
        & (rank_all[None, :, None, :] == pair_ids[None, None, :, None]),
        axis=3,
    )
    q_seq = select_rows(take_select, recv_q, "srk,rktf->stf").reshape(
        slot_count * row_length, query_width
    )
    kv_seq = select_rows(take_select, recv_kv, "srk,rktf->stf").reshape(
        slot_count * row_length, pair_width
    )
    tok_rows = q_seq.shape[0]
    owner_index = lax.axis_index(("outer", "inner"))
    query_pos = owner_index * tok_rows + jnp.arange(tok_rows, dtype=jnp.int32)
    queries = q_seq.reshape(tok_rows, head_count, head_size)
    score_scale = 1.0 / math.sqrt(head_size)
    last_pos = query_pos[tok_rows - 1]
    first_seg = segment_ids[0]
    last_seg = segment_ids[tok_rows - 1]

    def update(running, key_rows, key_seg, key_pos):
        largest, denominator, weighted = running
        key_part = key_rows[:, :head_size]
        value_part = key_rows[:, head_size:]
        scores = (
            jnp.einsum("qhd,kd->hqk", queries, key_part, preferred_element_type=jnp.float32)
            * score_scale
        )
        visible = (
            (key_pos[None, :] >= 0)
            & (key_pos[None, :] <= query_pos[:, None])
            & (key_seg[None, :] == segment_ids[:, None])
        )
        masked = jnp.where(visible[None], scores, -1e30)
        newest = jnp.maximum(largest, jnp.max(masked, axis=-1))
        factor = jnp.exp(largest - newest)
        weights = jnp.where(visible[None], jnp.exp(masked - newest[:, :, None]), 0.0)
        denominator = denominator * factor + jnp.sum(weights, axis=-1)
        weighted = weighted * factor.T[:, :, None] + jnp.einsum(
            "hqk,kd->qhd",
            weights.astype(jnp.bfloat16),
            value_part,
            preferred_element_type=jnp.float32,
        )
        return (newest, denominator, weighted)

    def absorb(running, pieces, first_row):
        key_rows, key_seg = pieces
        row_total = key_rows.shape[0]
        block_rows = 512

        def one_block(block_index, state):
            offset = block_index * block_rows
            rows_now = key_rows
            seg_now = key_seg
            pos_now = first_row + offset + jnp.arange(block_rows, dtype=jnp.int32)

            def compute(inner_state):
                return update(inner_state, rows_now, seg_now, pos_now)

            def keep(inner_state):
                return inner_state

            needed = (
                (pos_now[0] <= last_pos)
                & (seg_now[block_rows - 1] >= first_seg)
                & (seg_now[0] <= last_seg)
            )
            return lax.cond(needed, compute, keep, state)

        return lax.fori_loop(0, row_total // block_rows, one_block, running)

    all_seg = lax.all_gather(segment_ids, ("outer", "inner"), tiled=True)
    outer_index = lax.axis_index("outer")
    outer_count = lax.axis_size("outer")

    def absorb_chunk(running, chunk, first_device):
        def one_block(block_index, state):
            device = first_device + block_index
            rows_now = chunk[block_index]
            first_key = device * tok_rows
            safe_first = jnp.clip(first_key, 0, all_seg.shape[0] - tok_rows)
            seg_now = lax.dynamic_slice_in_dim(all_seg, safe_first, tok_rows, 0)
            pos_now = first_key + jnp.arange(tok_rows, dtype=jnp.int32)

            def compute(inner_state):
                return update(inner_state, rows_now, seg_now, pos_now)

            def keep(inner_state):
                return inner_state

            needed = (
                (first_key >= 0)
                & (pos_now[0] <= last_pos)
                & (seg_now[tok_rows - 1] >= first_seg)
                & (seg_now[0] <= last_seg)
            )
            return lax.cond(needed, compute, keep, state)

        return lax.fori_loop(0, chunk.shape[0], one_block, running)

    state = (
        jnp.full((head_count, tok_rows), -1e30, jnp.float32),
        jnp.zeros((head_count, tok_rows), jnp.float32),
        jnp.zeros((tok_rows, head_count, head_size), jnp.float32),
    )
    outer_reach = -(-(lax.axis_size("outer") * group_width // 4) // group_width)
    for step in range(outer_reach + 1):
        moved = kv_seq if step == 0 else shifted(kv_seq, "outer", step)
        chunk = lax.all_gather(moved, "inner", tiled=False)
        state = absorb_chunk(state, chunk, (outer_index - step) * group_width)
    largest, denominator, weighted = state
    return (
        (weighted / denominator.T[:, :, None]).reshape(tok_rows, query_width).astype(jnp.bfloat16)
    )


def solution(mesh):
    in_specs = (
        P(("outer", "inner"), None),
        P(("outer", "inner"), None),
        P("outer", None),
        P("outer"),
        P(("outer", "inner")),
    )
    out_specs = P(("outer", "inner"), None)
    return jax.shard_map(local, mesh=mesh, in_specs=in_specs, out_specs=out_specs, check_vma=False)
```

```python
import math

import jax
import jax.numpy as jnp
from jax import lax
from jax.experimental import pallas as pl
from jax.experimental.pallas import tpu as pltpu
from jax.sharding import PartitionSpec as P


def shifted(value, axis, steps):
    count = lax.axis_size(axis)
    leading, last = (max(0, -steps), min(count, count - steps))
    return lax.ppermute(value, axis, [(source, source + steps) for source in range(leading, last)])


def select_rows(selector, blocks, pattern):
    return jnp.einsum(
        pattern, selector.astype(jnp.bfloat16), blocks, preferred_element_type=jnp.float32
    ).astype(jnp.bfloat16)


def local(q_load, kv_load, pack_dest, counts, segment_ids):
    group_width = lax.axis_size("inner")
    my_index = lax.axis_index("inner")
    capacity = pack_dest.shape[1]
    slot_count = capacity // 2
    pair_limit = -(-capacity // group_width)
    row_length = q_load.shape[0] // capacity
    query_width = q_load.shape[1]
    pair_width = kv_load.shape[1]
    head_size = pair_width // 2
    head_count = query_width // head_size
    slot_grid = lax.broadcasted_iota(jnp.int32, (group_width, capacity), 1)
    live_all = slot_grid < counts[:, None]
    owner_all = pack_dest // slot_count
    slot_numbers = jnp.arange(capacity, dtype=jnp.int32)
    earlier = slot_numbers[None, :] < slot_numbers[:, None]
    same_owner = owner_all[:, :, None] == owner_all[:, None, :]
    rank_all = jnp.sum(
        (earlier[None] & same_owner & live_all[:, None, :]).astype(jnp.int32), axis=2
    )
    shard_rows = jnp.arange(group_width, dtype=jnp.int32)
    mine_row = (shard_rows == my_index)[:, None]
    my_owner = jnp.sum(jnp.where(mine_row, owner_all, 0), axis=0)
    my_rank = jnp.sum(jnp.where(mine_row, rank_all, 0), axis=0)
    my_live = jnp.any(mine_row & live_all, axis=0)
    pair_ids = jnp.arange(pair_limit, dtype=jnp.int32)
    send_select = (
        my_live[None, None, :]
        & (my_owner[None, None, :] == shard_rows[:, None, None])
        & (my_rank[None, None, :] == pair_ids[None, :, None])
    )
    q_blocks = q_load.reshape(capacity, row_length, query_width)
    kv_blocks = kv_load.reshape(capacity, row_length, pair_width)
    send_q = select_rows(send_select, q_blocks, "jkc,crf->jkrf")
    send_kv = select_rows(send_select, kv_blocks, "jkc,crf->jkrf")
    recv_q, recv_kv = (
        lax.all_to_all(send_q, "inner", split_axis=0, concat_axis=0, tiled=True),
        lax.all_to_all(send_kv, "inner", split_axis=0, concat_axis=0, tiled=True),
    )
    wanted = my_index * slot_count + jnp.arange(slot_count, dtype=jnp.int32)
    take_select = jnp.any(
        live_all[None, :, None, :]
        & (pack_dest[None, :, None, :] == wanted[:, None, None, None])
        & (rank_all[None, :, None, :] == pair_ids[None, None, :, None]),
        axis=3,
    )
    q_seq = select_rows(take_select, recv_q, "srk,rktf->stf").reshape(
        slot_count * row_length, query_width
    )
    kv_seq = select_rows(take_select, recv_kv, "srk,rktf->stf").reshape(
        slot_count * row_length, pair_width
    )
    tok_rows = q_seq.shape[0]
    owner_index = lax.axis_index(("outer", "inner"))
    outer_index = lax.axis_index("outer")
    score_scale = 1.0 / math.sqrt(head_size)
    extra_rows = 16
    seg_rows = tok_rows // pair_width
    seg_pad = jnp.zeros((extra_rows - seg_rows, pair_width), jnp.bfloat16)
    packed = jnp.concatenate(
        [kv_seq, segment_ids.astype(jnp.bfloat16).reshape(seg_rows, pair_width), seg_pad], axis=0
    )
    outer_reach = -(-(lax.axis_size("outer") * group_width // 4) // group_width)
    moved = [packed] + [shifted(packed, "outer", step) for step in range(1, outer_reach + 1)]
    chunks = lax.all_gather(jnp.stack(moved), "inner", tiled=False)
    chunk_count = outer_reach + 1
    block_count = chunk_count * group_width
    block_ids = jnp.arange(block_count, dtype=jnp.int32)
    key_device = (outer_index - block_ids // group_width) * group_width + block_ids % group_width
    flat_seg = chunks[:, :, tok_rows : tok_rows + seg_rows, :]
    key_first = jnp.transpose(flat_seg[:, :, 0, 0]).reshape(block_count)
    key_last = jnp.transpose(flat_seg[:, :, seg_rows - 1, pair_width - 1]).reshape(block_count)
    first_seg = segment_ids[0].astype(jnp.bfloat16)
    last_seg = segment_ids[tok_rows - 1].astype(jnp.bfloat16)
    needed = (
        (key_device >= 0)
        & (key_device <= owner_index)
        & (key_last >= first_seg)
        & (key_first <= last_seg)
    ).astype(jnp.int32)
    meta = jnp.concatenate([owner_index.reshape(1).astype(jnp.int32), needed])
    query_seg = segment_ids.astype(jnp.float32).reshape(tok_rows, 1)
    return attend(meta, q_seq, query_seg, chunks, head_count, head_size, score_scale)


def attend(meta, q_seq, query_seg, chunks, head_count, head_size, score_scale):
    tok_rows = q_seq.shape[0]
    group_width, chunk_count, packed_rows, pair_width = chunks.shape
    block_count = group_width * chunk_count
    seg_rows = tok_rows // pair_width

    def kernel(meta_ref, q_ref, qseg_ref, kv_ref, out_ref, m_ref, l_ref, acc_ref):
        b = pl.program_id(0)

        @pl.when(b == 0)
        def _():
            m_ref[...] = jnp.full(m_ref.shape, -1e30, jnp.float32)
            l_ref[...] = jnp.zeros(l_ref.shape, jnp.float32)
            acc_ref[...] = jnp.zeros(acc_ref.shape, jnp.float32)

        @pl.when(meta_ref[1 + b] == 1)
        def _():
            own = meta_ref[0]
            chunk = b // group_width
            device = (own // group_width - chunk) * group_width + b % group_width
            seg_parts = [
                kv_ref[0, 0, tok_rows + r : tok_rows + r + 1, :].astype(jnp.float32)
                for r in range(seg_rows)
            ]
            key_seg = jnp.concatenate(seg_parts, axis=1)
            key_pos = device * tok_rows + lax.broadcasted_iota(jnp.int32, (1, tok_rows), 1)
            query_pos = own * tok_rows + lax.broadcasted_iota(jnp.int32, (tok_rows, 1), 0)
            visible = (key_pos <= query_pos) & (key_seg == qseg_ref[...])
            keys = kv_ref[0, 0, :tok_rows, :head_size]
            values = kv_ref[0, 0, :tok_rows, head_size:]
            for h in range(head_count):
                queries = q_ref[:, h * head_size : (h + 1) * head_size]
                scores = lax.dot_general(
                    queries, keys, (((1,), (1,)), ((), ())), preferred_element_type=jnp.float32
                ) * score_scale
                masked = jnp.where(visible, scores, -1e30)
                m_prev = m_ref[h]
                m_next = jnp.maximum(m_prev, jnp.max(masked, axis=1, keepdims=True))
                factor = jnp.exp(m_prev - m_next)
                weights = jnp.where(visible, jnp.exp(masked - m_next[:, :1]), 0.0)
                l_ref[h] = l_ref[h] * factor + jnp.sum(weights, axis=1, keepdims=True)
                acc_ref[h] = acc_ref[h] * factor + jnp.dot(
                    weights.astype(jnp.bfloat16), values, preferred_element_type=jnp.float32
                )
                m_ref[h] = m_next

        @pl.when(b == block_count - 1)
        def _():
            for h in range(head_count):
                out_ref[:, h * head_size : (h + 1) * head_size] = (
                    acc_ref[h] / l_ref[h]
                ).astype(out_ref.dtype)

    grid_spec = pltpu.PrefetchScalarGridSpec(
        num_scalar_prefetch=1,
        grid=(block_count,),
        in_specs=[
            pl.BlockSpec(q_seq.shape, lambda b, meta: (0, 0)),
            pl.BlockSpec(query_seg.shape, lambda b, meta: (0, 0)),
            pl.BlockSpec(
                (1, 1, packed_rows, pair_width),
                lambda b, meta: (b % group_width, b // group_width, 0, 0),
            ),
        ],
        out_specs=pl.BlockSpec(q_seq.shape, lambda b, meta: (0, 0)),
        scratch_shapes=[
            pltpu.VMEM((head_count, tok_rows, head_size), jnp.float32),
            pltpu.VMEM((head_count, tok_rows, head_size), jnp.float32),
            pltpu.VMEM((head_count, tok_rows, head_size), jnp.float32),
        ],
    )
    flops = 4 * block_count * tok_rows * tok_rows * head_size * head_count
    return pl.pallas_call(
        kernel,
        grid_spec=grid_spec,
        out_shape=jax.ShapeDtypeStruct(q_seq.shape, q_seq.dtype),
        compiler_params=pltpu.CompilerParams(dimension_semantics=("arbitrary",)),
        cost_estimate=pl.CostEstimate(
            flops=flops,
            transcendentals=block_count * tok_rows * tok_rows * head_count,
            bytes_accessed=chunks.size * 2 + q_seq.size * 4,
        ),
    )(meta, q_seq, query_seg, chunks)


def solution(mesh):
    in_specs = (
        P(("outer", "inner"), None),
        P(("outer", "inner"), None),
        P("outer", None),
        P("outer"),
        P(("outer", "inner")),
    )
    out_specs = P(("outer", "inner"), None)
    return jax.shard_map(local, mesh=mesh, in_specs=in_specs, out_specs=out_specs, check_vma=False)
```

```python
import math

import jax
import jax.numpy as jnp
from jax import lax
from jax.experimental import pallas as pl
from jax.experimental.pallas import tpu as pltpu
from jax.sharding import PartitionSpec as P


def shifted(value, axis, steps):
    count = lax.axis_size(axis)
    leading, last = (max(0, -steps), min(count, count - steps))
    return lax.ppermute(value, axis, [(source, source + steps) for source in range(leading, last)])


def select_rows(selector, blocks, pattern):
    return jnp.einsum(
        pattern, selector.astype(jnp.bfloat16), blocks, preferred_element_type=jnp.float32
    ).astype(jnp.bfloat16)


def local(q_load, kv_load, pack_dest, counts, segment_ids):
    group_width = lax.axis_size("inner")
    my_index = lax.axis_index("inner")
    capacity = pack_dest.shape[1]
    slot_count = capacity // 2
    pair_limit = -(-capacity // group_width)
    row_length = q_load.shape[0] // capacity
    query_width = q_load.shape[1]
    pair_width = kv_load.shape[1]
    head_size = pair_width // 2
    head_count = query_width // head_size
    slot_grid = lax.broadcasted_iota(jnp.int32, (group_width, capacity), 1)
    live_all = slot_grid < counts[:, None]
    owner_all = pack_dest // slot_count
    slot_numbers = jnp.arange(capacity, dtype=jnp.int32)
    earlier = slot_numbers[None, :] < slot_numbers[:, None]
    same_owner = owner_all[:, :, None] == owner_all[:, None, :]
    rank_all = jnp.sum(
        (earlier[None] & same_owner & live_all[:, None, :]).astype(jnp.int32), axis=2
    )
    shard_rows = jnp.arange(group_width, dtype=jnp.int32)
    mine_row = (shard_rows == my_index)[:, None]
    my_owner = jnp.sum(jnp.where(mine_row, owner_all, 0), axis=0)
    my_rank = jnp.sum(jnp.where(mine_row, rank_all, 0), axis=0)
    my_live = jnp.any(mine_row & live_all, axis=0)
    pair_ids = jnp.arange(pair_limit, dtype=jnp.int32)
    send_select = (
        my_live[None, None, :]
        & (my_owner[None, None, :] == shard_rows[:, None, None])
        & (my_rank[None, None, :] == pair_ids[None, :, None])
    )
    q_blocks = q_load.reshape(capacity, row_length, query_width)
    kv_blocks = kv_load.reshape(capacity, row_length, pair_width)
    send_q = select_rows(send_select, q_blocks, "jkc,crf->jkrf")
    send_kv = select_rows(send_select, kv_blocks, "jkc,crf->jkrf")
    recv_q, recv_kv = (
        lax.all_to_all(send_q, "inner", split_axis=0, concat_axis=0, tiled=True),
        lax.all_to_all(send_kv, "inner", split_axis=0, concat_axis=0, tiled=True),
    )
    wanted = my_index * slot_count + jnp.arange(slot_count, dtype=jnp.int32)
    take_select = jnp.any(
        live_all[None, :, None, :]
        & (pack_dest[None, :, None, :] == wanted[:, None, None, None])
        & (rank_all[None, :, None, :] == pair_ids[None, None, :, None]),
        axis=3,
    )
    q_seq = select_rows(take_select, recv_q, "srk,rktf->stf").reshape(
        slot_count * row_length, query_width
    )
    kv_seq = select_rows(take_select, recv_kv, "srk,rktf->stf").reshape(
        slot_count * row_length, pair_width
    )
    tok_rows = q_seq.shape[0]
    owner_index = lax.axis_index(("outer", "inner"))
    outer_index = lax.axis_index("outer")
    score_scale = 1.0 / math.sqrt(head_size)
    extra_rows = 16
    seg_rows = tok_rows // pair_width
    seg_pad = jnp.zeros((extra_rows - seg_rows, pair_width), jnp.bfloat16)
    packed = jnp.concatenate(
        [kv_seq, segment_ids.astype(jnp.bfloat16).reshape(seg_rows, pair_width), seg_pad], axis=0
    )
    outer_reach = -(-(lax.axis_size("outer") * group_width // 4) // group_width)
    own_steps = list(range(0, outer_reach + 1, 2))
    partner_steps = list(range(1, outer_reach + 1, 2))
    moved = [packed if step == 0 else shifted(packed, "outer", step) for step in own_steps]
    gathered = lax.all_gather(jnp.stack(moved), "inner", tiled=False)
    parity = outer_index % 2
    offer = lax.dynamic_slice_in_dim(gathered, parity, len(partner_steps), axis=1)
    outer_count = lax.axis_size("outer")
    partner_pairs = [(o, o ^ 1) for o in range(outer_count)]
    received = lax.ppermute(offer, "outer", partner_pairs)
    sources = [(gathered, own_steps), (received, partner_steps)]
    key_device, key_first, key_last = [], [], []
    for array, steps in sources:
        for slot, step in enumerate(steps):
            key_device.append(
                (outer_index - step) * group_width + jnp.arange(group_width, dtype=jnp.int32)
            )
            key_first.append(array[:, slot, tok_rows, 0])
            key_last.append(array[:, slot, tok_rows + seg_rows - 1, pair_width - 1])
    key_device = jnp.concatenate(key_device)
    key_first = jnp.concatenate(key_first)
    key_last = jnp.concatenate(key_last)
    first_seg = segment_ids[0].astype(jnp.bfloat16)
    last_seg = segment_ids[tok_rows - 1].astype(jnp.bfloat16)
    needed = (
        (key_device >= 0)
        & (key_device <= owner_index)
        & (key_last >= first_seg)
        & (key_first <= last_seg)
    ).astype(jnp.int32)
    meta = jnp.concatenate([owner_index.reshape(1).astype(jnp.int32), needed, key_device])
    query_seg = segment_ids.astype(jnp.float32).reshape(tok_rows, 1)
    return attend(meta, q_seq, query_seg, gathered, received, head_count, head_size, score_scale)


def attend(meta, q_seq, query_seg, gathered, received, head_count, head_size, score_scale):
    tok_rows = q_seq.shape[0]
    group_width, first_slots, packed_rows, pair_width = gathered.shape
    second_slots = received.shape[1]
    first_count = group_width * first_slots
    block_count = first_count + group_width * second_slots
    seg_rows = tok_rows // pair_width

    def kernel(meta_ref, q_ref, qseg_ref, first_ref, second_ref, out_ref, m_ref, l_ref, acc_ref):
        b = pl.program_id(0)

        @pl.when(b == 0)
        def _():
            m_ref[...] = jnp.full(m_ref.shape, -1e30, jnp.float32)
            l_ref[...] = jnp.zeros(l_ref.shape, jnp.float32)
            acc_ref[...] = jnp.zeros(acc_ref.shape, jnp.float32)

        def absorb(kv_ref):
            own = meta_ref[0]
            device = meta_ref[1 + block_count + b]
            seg_parts = [
                kv_ref[0, 0, tok_rows + r : tok_rows + r + 1, :].astype(jnp.float32)
                for r in range(seg_rows)
            ]
            key_seg = jnp.concatenate(seg_parts, axis=1)
            key_pos = device * tok_rows + lax.broadcasted_iota(jnp.int32, (1, tok_rows), 1)
            query_pos = own * tok_rows + lax.broadcasted_iota(jnp.int32, (tok_rows, 1), 0)
            visible = (key_pos <= query_pos) & (key_seg == qseg_ref[...])
            keys = kv_ref[0, 0, :tok_rows, :head_size]
            values = kv_ref[0, 0, :tok_rows, head_size:]
            for h in range(head_count):
                queries = q_ref[:, h * head_size : (h + 1) * head_size]
                scores = lax.dot_general(
                    queries, keys, (((1,), (1,)), ((), ())), preferred_element_type=jnp.float32
                ) * score_scale
                masked = jnp.where(visible, scores, -1e30)
                m_prev = m_ref[h]
                m_next = jnp.maximum(m_prev, jnp.max(masked, axis=1, keepdims=True))
                factor = jnp.exp(m_prev - m_next)
                weights = jnp.where(visible, jnp.exp(masked - m_next[:, :1]), 0.0)
                l_ref[h] = l_ref[h] * factor + jnp.sum(weights, axis=1, keepdims=True)
                acc_ref[h] = acc_ref[h] * factor + jnp.dot(
                    weights.astype(jnp.bfloat16), values, preferred_element_type=jnp.float32
                )
                m_ref[h] = m_next

        live = meta_ref[1 + b] == 1

        @pl.when(live & (b < first_count))
        def _():
            absorb(first_ref)

        @pl.when(live & (b >= first_count))
        def _():
            absorb(second_ref)

        @pl.when(b == block_count - 1)
        def _():
            for h in range(head_count):
                out_ref[:, h * head_size : (h + 1) * head_size] = (
                    acc_ref[h] / l_ref[h]
                ).astype(out_ref.dtype)

    def first_map(b, meta):
        c = jnp.minimum(b, first_count - 1)
        return (c % group_width, c // group_width, 0, 0)

    def second_map(b, meta):
        c = jnp.maximum(b - first_count, 0)
        return (c % group_width, c // group_width, 0, 0)

    grid_spec = pltpu.PrefetchScalarGridSpec(
        num_scalar_prefetch=1,
        grid=(block_count,),
        in_specs=[
            pl.BlockSpec(q_seq.shape, lambda b, meta: (0, 0)),
            pl.BlockSpec(query_seg.shape, lambda b, meta: (0, 0)),
            pl.BlockSpec((1, 1, packed_rows, pair_width), first_map),
            pl.BlockSpec((1, 1, packed_rows, pair_width), second_map),
        ],
        out_specs=pl.BlockSpec(q_seq.shape, lambda b, meta: (0, 0)),
        scratch_shapes=[
            pltpu.VMEM((head_count, tok_rows, head_size), jnp.float32),
            pltpu.VMEM((head_count, tok_rows, head_size), jnp.float32),
            pltpu.VMEM((head_count, tok_rows, head_size), jnp.float32),
        ],
    )
    flops = 4 * block_count * tok_rows * tok_rows * head_size * head_count
    return pl.pallas_call(
        kernel,
        grid_spec=grid_spec,
        out_shape=jax.ShapeDtypeStruct(q_seq.shape, q_seq.dtype),
        compiler_params=pltpu.CompilerParams(dimension_semantics=("arbitrary",)),
        cost_estimate=pl.CostEstimate(
            flops=flops,
            transcendentals=block_count * tok_rows * tok_rows * head_count,
            bytes_accessed=(gathered.size + received.size) * 2 + q_seq.size * 4,
        ),
    )(meta, q_seq, query_seg, gathered, received)


def solution(mesh):
    in_specs = (
        P(("outer", "inner"), None),
        P(("outer", "inner"), None),
        P("outer", None),
        P("outer"),
        P(("outer", "inner")),
    )
    out_specs = P(("outer", "inner"), None)
    return jax.shard_map(local, mesh=mesh, in_specs=in_specs, out_specs=out_specs, check_vma=False)
```

```python
import math

import jax
import jax.numpy as jnp
from jax import lax
from jax.experimental import pallas as pl
from jax.experimental.pallas import tpu as pltpu
from jax.sharding import PartitionSpec as P


def shifted(value, axis, steps):
    count = lax.axis_size(axis)
    leading, last = (max(0, -steps), min(count, count - steps))
    return lax.ppermute(value, axis, [(source, source + steps) for source in range(leading, last)])


def select_rows(selector, blocks, pattern):
    return jnp.einsum(
        pattern, selector.astype(jnp.bfloat16), blocks, preferred_element_type=jnp.float32
    ).astype(jnp.bfloat16)


def local(q_load, kv_load, pack_dest, counts, segment_ids):
    group_width = lax.axis_size("inner")
    my_index = lax.axis_index("inner")
    capacity = pack_dest.shape[1]
    slot_count = capacity // 2
    pair_limit = -(-capacity // group_width)
    row_length = q_load.shape[0] // capacity
    query_width = q_load.shape[1]
    pair_width = kv_load.shape[1]
    head_size = pair_width // 2
    head_count = query_width // head_size
    slot_grid = lax.broadcasted_iota(jnp.int32, (group_width, capacity), 1)
    live_all = slot_grid < counts[:, None]
    owner_all = pack_dest // slot_count
    slot_numbers = jnp.arange(capacity, dtype=jnp.int32)
    earlier = slot_numbers[None, :] < slot_numbers[:, None]
    same_owner = owner_all[:, :, None] == owner_all[:, None, :]
    rank_all = jnp.sum(
        (earlier[None] & same_owner & live_all[:, None, :]).astype(jnp.int32), axis=2
    )
    shard_rows = jnp.arange(group_width, dtype=jnp.int32)
    mine_row = (shard_rows == my_index)[:, None]
    my_owner = jnp.sum(jnp.where(mine_row, owner_all, 0), axis=0)
    my_rank = jnp.sum(jnp.where(mine_row, rank_all, 0), axis=0)
    my_live = jnp.any(mine_row & live_all, axis=0)
    pair_ids = jnp.arange(pair_limit, dtype=jnp.int32)
    send_select = (
        my_live[None, None, :]
        & (my_owner[None, None, :] == shard_rows[:, None, None])
        & (my_rank[None, None, :] == pair_ids[None, :, None])
    )
    q_blocks = q_load.reshape(capacity, row_length, query_width)
    kv_blocks = kv_load.reshape(capacity, row_length, pair_width)
    send_q = select_rows(send_select, q_blocks, "jkc,crf->jkrf")
    send_kv = select_rows(send_select, kv_blocks, "jkc,crf->jkrf")
    recv_both = lax.all_to_all(
        jnp.concatenate([send_q, send_kv], axis=3), "inner", split_axis=0, concat_axis=0, tiled=True
    )
    recv_q = recv_both[..., :query_width]
    recv_kv = recv_both[..., query_width:]
    wanted = my_index * slot_count + jnp.arange(slot_count, dtype=jnp.int32)
    take_select = jnp.any(
        live_all[None, :, None, :]
        & (pack_dest[None, :, None, :] == wanted[:, None, None, None])
        & (rank_all[None, :, None, :] == pair_ids[None, None, :, None]),
        axis=3,
    )
    q_seq = select_rows(take_select, recv_q, "srk,rktf->stf").reshape(
        slot_count * row_length, query_width
    )
    kv_seq = select_rows(take_select, recv_kv, "srk,rktf->stf").reshape(
        slot_count * row_length, pair_width
    )
    tok_rows = q_seq.shape[0]
    owner_index = lax.axis_index(("outer", "inner"))
    outer_index = lax.axis_index("outer")
    score_scale = 1.0 / math.sqrt(head_size)
    extra_rows = 16
    seg_rows = tok_rows // pair_width
    seg_pad = jnp.zeros((extra_rows - seg_rows, pair_width), jnp.bfloat16)
    packed = jnp.concatenate(
        [kv_seq, segment_ids.astype(jnp.bfloat16).reshape(seg_rows, pair_width), seg_pad], axis=0
    )
    outer_reach = -(-(lax.axis_size("outer") * group_width // 4) // group_width)
    own_steps = list(range(0, outer_reach + 1, 2))
    partner_steps = list(range(1, outer_reach + 1, 2))
    moved = [packed if step == 0 else shifted(packed, "outer", step) for step in own_steps]
    own_stack = jnp.stack(moved)
    inner_shifts = [own_stack] + [
        lax.ppermute(own_stack, "inner", [(i, (i + s) % group_width) for i in range(group_width)])
        for s in range(1, group_width)
    ]
    gathered = jnp.stack(inner_shifts)
    inner_of = (my_index - jnp.arange(group_width, dtype=jnp.int32)) % group_width
    parity = outer_index % 2
    offer = lax.dynamic_slice_in_dim(gathered, parity, len(partner_steps), axis=1)
    outer_count = lax.axis_size("outer")
    partner_pairs = [(o, o ^ 1) for o in range(outer_count)]
    received = lax.ppermute(offer, "outer", partner_pairs)
    sources = [(gathered, own_steps), (received, partner_steps)]
    key_device, key_first, key_last = [], [], []
    for array, steps in sources:
        for slot, step in enumerate(steps):
            key_device.append(
                (outer_index - step) * group_width + inner_of
            )
            key_first.append(array[:, slot, tok_rows, 0])
            key_last.append(array[:, slot, tok_rows + seg_rows - 1, pair_width - 1])
    key_device = jnp.concatenate(key_device)
    key_first = jnp.concatenate(key_first)
    key_last = jnp.concatenate(key_last)
    first_seg = segment_ids[0].astype(jnp.bfloat16)
    last_seg = segment_ids[tok_rows - 1].astype(jnp.bfloat16)
    needed = (
        (key_device >= 0)
        & (key_device <= owner_index)
        & (key_last >= first_seg)
        & (key_first <= last_seg)
    ).astype(jnp.int32)
    meta = jnp.concatenate([owner_index.reshape(1).astype(jnp.int32), needed, key_device])
    query_seg = segment_ids.astype(jnp.float32).reshape(tok_rows, 1)
    return attend(meta, q_seq, query_seg, gathered, received, head_count, head_size, score_scale)


def attend(meta, q_seq, query_seg, gathered, received, head_count, head_size, score_scale):
    tok_rows = q_seq.shape[0]
    group_width, first_slots, packed_rows, pair_width = gathered.shape
    second_slots = received.shape[1]
    first_count = group_width * first_slots
    block_count = first_count + group_width * second_slots
    seg_rows = tok_rows // pair_width

    def kernel(meta_ref, q_ref, qseg_ref, first_ref, second_ref, out_ref, m_ref, l_ref, acc_ref):
        b = pl.program_id(0)

        @pl.when(b == 0)
        def _():
            m_ref[...] = jnp.full(m_ref.shape, -1e30, jnp.float32)
            l_ref[...] = jnp.zeros(l_ref.shape, jnp.float32)
            acc_ref[...] = jnp.zeros(acc_ref.shape, jnp.float32)

        def absorb(kv_ref):
            own = meta_ref[0]
            device = meta_ref[1 + block_count + b]
            seg_parts = [
                kv_ref[0, 0, tok_rows + r : tok_rows + r + 1, :].astype(jnp.float32)
                for r in range(seg_rows)
            ]
            key_seg = jnp.concatenate(seg_parts, axis=1)
            key_pos = device * tok_rows + lax.broadcasted_iota(jnp.int32, (1, tok_rows), 1)
            query_pos = own * tok_rows + lax.broadcasted_iota(jnp.int32, (tok_rows, 1), 0)
            visible = (key_pos <= query_pos) & (key_seg == qseg_ref[...])
            keys = kv_ref[0, 0, :tok_rows, :head_size]
            values = kv_ref[0, 0, :tok_rows, head_size:]
            for h in range(head_count):
                queries = q_ref[:, h * head_size : (h + 1) * head_size]
                scores = lax.dot_general(
                    queries, keys, (((1,), (1,)), ((), ())), preferred_element_type=jnp.float32
                ) * score_scale
                masked = jnp.where(visible, scores, -1e30)
                m_prev = m_ref[h]
                m_next = jnp.maximum(m_prev, jnp.max(masked, axis=1, keepdims=True))
                factor = jnp.exp(m_prev - m_next)
                weights = jnp.where(visible, jnp.exp(masked - m_next[:, :1]), 0.0)
                l_ref[h] = l_ref[h] * factor + jnp.sum(weights, axis=1, keepdims=True)
                acc_ref[h] = acc_ref[h] * factor + jnp.dot(
                    weights.astype(jnp.bfloat16), values, preferred_element_type=jnp.float32
                )
                m_ref[h] = m_next

        live = meta_ref[1 + b] == 1

        @pl.when(live & (b < first_count))
        def _():
            absorb(first_ref)

        @pl.when(live & (b >= first_count))
        def _():
            absorb(second_ref)

        @pl.when(b == block_count - 1)
        def _():
            for h in range(head_count):
                out_ref[:, h * head_size : (h + 1) * head_size] = (
                    acc_ref[h] / l_ref[h]
                ).astype(out_ref.dtype)

    def first_map(b, meta):
        c = jnp.minimum(b, first_count - 1)
        return (c % group_width, c // group_width, 0, 0)

    def second_map(b, meta):
        c = jnp.maximum(b - first_count, 0)
        return (c % group_width, c // group_width, 0, 0)

    grid_spec = pltpu.PrefetchScalarGridSpec(
        num_scalar_prefetch=1,
        grid=(block_count,),
        in_specs=[
            pl.BlockSpec(q_seq.shape, lambda b, meta: (0, 0)),
            pl.BlockSpec(query_seg.shape, lambda b, meta: (0, 0)),
            pl.BlockSpec((1, 1, packed_rows, pair_width), first_map),
            pl.BlockSpec((1, 1, packed_rows, pair_width), second_map),
        ],
        out_specs=pl.BlockSpec(q_seq.shape, lambda b, meta: (0, 0)),
        scratch_shapes=[
            pltpu.VMEM((head_count, tok_rows, head_size), jnp.float32),
            pltpu.VMEM((head_count, tok_rows, head_size), jnp.float32),
            pltpu.VMEM((head_count, tok_rows, head_size), jnp.float32),
        ],
    )
    flops = 4 * block_count * tok_rows * tok_rows * head_size * head_count
    return pl.pallas_call(
        kernel,
        grid_spec=grid_spec,
        out_shape=jax.ShapeDtypeStruct(q_seq.shape, q_seq.dtype),
        compiler_params=pltpu.CompilerParams(dimension_semantics=("arbitrary",)),
        cost_estimate=pl.CostEstimate(
            flops=flops,
            transcendentals=block_count * tok_rows * tok_rows * head_count,
            bytes_accessed=(gathered.size + received.size) * 2 + q_seq.size * 4,
        ),
    )(meta, q_seq, query_seg, gathered, received)


def solution(mesh):
    in_specs = (
        P(("outer", "inner"), None),
        P(("outer", "inner"), None),
        P("outer", None),
        P("outer"),
        P(("outer", "inner")),
    )
    out_specs = P(("outer", "inner"), None)
    return jax.shard_map(local, mesh=mesh, in_specs=in_specs, out_specs=out_specs, check_vma=False)
```

```python
import math

import jax
import jax.numpy as jnp
from jax import lax
from jax.experimental import pallas as pl
from jax.experimental.pallas import tpu as pltpu
from jax.sharding import PartitionSpec as P


def shifted(value, axis, steps):
    count = lax.axis_size(axis)
    leading, last = (max(0, -steps), min(count, count - steps))
    return lax.ppermute(value, axis, [(source, source + steps) for source in range(leading, last)])


def select_rows(selector, blocks, pattern):
    return jnp.einsum(
        pattern, selector.astype(jnp.bfloat16), blocks, preferred_element_type=jnp.float32
    ).astype(jnp.bfloat16)


def local(q_load, kv_load, pack_dest, counts, segment_ids):
    group_width = lax.axis_size("inner")
    my_index = lax.axis_index("inner")
    capacity = pack_dest.shape[1]
    slot_count = capacity // 2
    pair_limit = -(-capacity // group_width)
    row_length = q_load.shape[0] // capacity
    query_width = q_load.shape[1]
    pair_width = kv_load.shape[1]
    head_size = pair_width // 2
    head_count = query_width // head_size
    slot_grid = lax.broadcasted_iota(jnp.int32, (group_width, capacity), 1)
    live_all = slot_grid < counts[:, None]
    owner_all = pack_dest // slot_count
    slot_numbers = jnp.arange(capacity, dtype=jnp.int32)
    earlier = slot_numbers[None, :] < slot_numbers[:, None]
    same_owner = owner_all[:, :, None] == owner_all[:, None, :]
    rank_all = jnp.sum(
        (earlier[None] & same_owner & live_all[:, None, :]).astype(jnp.int32), axis=2
    )
    shard_rows = jnp.arange(group_width, dtype=jnp.int32)
    mine_row = (shard_rows == my_index)[:, None]
    my_owner = jnp.sum(jnp.where(mine_row, owner_all, 0), axis=0)
    my_rank = jnp.sum(jnp.where(mine_row, rank_all, 0), axis=0)
    my_live = jnp.any(mine_row & live_all, axis=0)
    pair_ids = jnp.arange(pair_limit, dtype=jnp.int32)
    send_select = (
        my_live[None, None, :]
        & (my_owner[None, None, :] == shard_rows[:, None, None])
        & (my_rank[None, None, :] == pair_ids[None, :, None])
    )
    q_blocks = q_load.reshape(capacity, row_length, query_width)
    kv_blocks = kv_load.reshape(capacity, row_length, pair_width)
    send_q = select_rows(send_select, q_blocks, "jkc,crf->jkrf")
    send_kv = select_rows(send_select, kv_blocks, "jkc,crf->jkrf")
    recv_both = lax.all_to_all(
        jnp.concatenate([send_q, send_kv], axis=3), "inner", split_axis=0, concat_axis=0, tiled=True
    )
    recv_q = recv_both[..., :query_width]
    recv_kv = recv_both[..., query_width:]
    wanted = my_index * slot_count + jnp.arange(slot_count, dtype=jnp.int32)
    take_select = jnp.any(
        live_all[None, :, None, :]
        & (pack_dest[None, :, None, :] == wanted[:, None, None, None])
        & (rank_all[None, :, None, :] == pair_ids[None, None, :, None]),
        axis=3,
    )
    q_seq = select_rows(take_select, recv_q, "srk,rktf->stf").reshape(
        slot_count * row_length, query_width
    )
    kv_seq = select_rows(take_select, recv_kv, "srk,rktf->stf").reshape(
        slot_count * row_length, pair_width
    )
    tok_rows = q_seq.shape[0]
    owner_index = lax.axis_index(("outer", "inner"))
    outer_index = lax.axis_index("outer")
    score_scale = 1.0 / math.sqrt(head_size)
    extra_rows = 16
    seg_rows = tok_rows // pair_width
    seg_pad = jnp.zeros((extra_rows - seg_rows, pair_width), jnp.bfloat16)
    packed = jnp.concatenate(
        [kv_seq, segment_ids.astype(jnp.bfloat16).reshape(seg_rows, pair_width), seg_pad], axis=0
    )
    outer_reach = -(-(lax.axis_size("outer") * group_width // 4) // group_width)
    own_steps = list(range(0, outer_reach + 1, 2))
    partner_steps = list(range(1, outer_reach + 1, 2))
    moved = [packed if step == 0 else shifted(packed, "outer", step) for step in own_steps]
    own_stack = jnp.stack(moved)
    inner_shifts = [own_stack] + [
        lax.ppermute(own_stack, "inner", [(i, (i + s) % group_width) for i in range(group_width)])
        for s in range(1, group_width)
    ]
    gathered = jnp.stack(inner_shifts)
    inner_of = (my_index - jnp.arange(group_width, dtype=jnp.int32)) % group_width
    parity = outer_index % 2
    offer = lax.dynamic_slice_in_dim(gathered, parity, len(partner_steps), axis=1)
    outer_count = lax.axis_size("outer")
    partner_pairs = [(o, o ^ 1) for o in range(outer_count)]
    received = lax.ppermute(offer, "outer", partner_pairs)
    sources = [(gathered, own_steps), (received, partner_steps)]
    key_device, key_first, key_last = [], [], []
    for array, steps in sources:
        for slot, step in enumerate(steps):
            key_device.append(
                (outer_index - step) * group_width + inner_of
            )
            key_first.append(array[:, slot, tok_rows, 0])
            key_last.append(array[:, slot, tok_rows + seg_rows - 1, pair_width - 1])
    key_device = jnp.concatenate(key_device)
    key_first = jnp.concatenate(key_first)
    key_last = jnp.concatenate(key_last)
    first_seg = segment_ids[0].astype(jnp.bfloat16)
    last_seg = segment_ids[tok_rows - 1].astype(jnp.bfloat16)
    needed = (
        (key_device >= 0)
        & (key_device <= owner_index)
        & (key_last >= first_seg)
        & (key_first <= last_seg)
    )
    whole = (
        (key_device < owner_index)
        & (key_first == key_last)
        & (key_first == first_seg)
        & (first_seg == last_seg)
    )
    needed = jnp.where(needed, jnp.where(whole, 1, 2), 0).astype(jnp.int32)
    meta = jnp.concatenate([owner_index.reshape(1).astype(jnp.int32), needed, key_device])
    query_seg = segment_ids.astype(jnp.float32).reshape(tok_rows, 1)
    return attend(meta, q_seq, query_seg, gathered, received, head_count, head_size, score_scale)


def attend(meta, q_seq, query_seg, gathered, received, head_count, head_size, score_scale):
    tok_rows = q_seq.shape[0]
    group_width, first_slots, packed_rows, pair_width = gathered.shape
    second_slots = received.shape[1]
    first_count = group_width * first_slots
    block_count = first_count + group_width * second_slots
    seg_rows = tok_rows // pair_width

    def kernel(meta_ref, q_ref, qseg_ref, first_ref, second_ref, out_ref, m_ref, l_ref, acc_ref):
        b = pl.program_id(0)

        @pl.when(b == 0)
        def _():
            m_ref[...] = jnp.full(m_ref.shape, -1e30, jnp.float32)
            l_ref[...] = jnp.zeros(l_ref.shape, jnp.float32)
            acc_ref[...] = jnp.zeros(acc_ref.shape, jnp.float32)

        def absorb(kv_ref, masked_block):
            keys = kv_ref[0, 0, :tok_rows, :head_size]
            values = kv_ref[0, 0, :tok_rows, head_size:]
            if masked_block:
                own = meta_ref[0]
                device = meta_ref[1 + block_count + b]
                seg_parts = [
                    kv_ref[0, 0, tok_rows + r : tok_rows + r + 1, :].astype(jnp.float32)
                    for r in range(seg_rows)
                ]
                key_seg = jnp.concatenate(seg_parts, axis=1)
                key_pos = device * tok_rows + lax.broadcasted_iota(jnp.int32, (1, tok_rows), 1)
                query_pos = own * tok_rows + lax.broadcasted_iota(jnp.int32, (tok_rows, 1), 0)
                visible = (key_pos <= query_pos) & (key_seg == qseg_ref[...])
            for h in range(head_count):
                queries = q_ref[:, h * head_size : (h + 1) * head_size]
                scores = lax.dot_general(
                    queries, keys, (((1,), (1,)), ((), ())), preferred_element_type=jnp.float32
                )
                if masked_block:
                    scores = jnp.where(visible, scores, -1e30)
                m_prev = m_ref[h]
                m_next = jnp.maximum(m_prev, jnp.max(scores, axis=1, keepdims=True))
                factor = jnp.exp((m_prev - m_next) * score_scale)
                m_row = m_next[:, :1]
                if masked_block:
                    m_row = jnp.where(m_row == -1e30, 0.0, m_row)
                weights = jnp.exp((scores - m_row) * score_scale)
                l_ref[h] = l_ref[h] * factor + jnp.sum(weights, axis=1, keepdims=True)
                acc_ref[h] = acc_ref[h] * factor + jnp.dot(
                    weights.astype(jnp.bfloat16), values, preferred_element_type=jnp.float32
                )
                m_ref[h] = m_next

        mode = meta_ref[1 + b]
        for ref, in_range in ((first_ref, b < first_count), (second_ref, b >= first_count)):
            for masked_block, code in ((False, 1), (True, 2)):
                @pl.when(in_range & (mode == code))
                def _(ref=ref, masked_block=masked_block):
                    absorb(ref, masked_block)

        @pl.when(b == block_count - 1)
        def _():
            for h in range(head_count):
                out_ref[:, h * head_size : (h + 1) * head_size] = (
                    acc_ref[h] / l_ref[h]
                ).astype(out_ref.dtype)

    def first_map(b, meta):
        c = jnp.minimum(b, first_count - 1)
        return (c % group_width, c // group_width, 0, 0)

    def second_map(b, meta):
        c = jnp.maximum(b - first_count, 0)
        return (c % group_width, c // group_width, 0, 0)

    grid_spec = pltpu.PrefetchScalarGridSpec(
        num_scalar_prefetch=1,
        grid=(block_count,),
        in_specs=[
            pl.BlockSpec(q_seq.shape, lambda b, meta: (0, 0)),
            pl.BlockSpec(query_seg.shape, lambda b, meta: (0, 0)),
            pl.BlockSpec((1, 1, packed_rows, pair_width), first_map),
            pl.BlockSpec((1, 1, packed_rows, pair_width), second_map),
        ],
        out_specs=pl.BlockSpec(q_seq.shape, lambda b, meta: (0, 0)),
        scratch_shapes=[
            pltpu.VMEM((head_count, tok_rows, head_size), jnp.float32),
            pltpu.VMEM((head_count, tok_rows, head_size), jnp.float32),
            pltpu.VMEM((head_count, tok_rows, head_size), jnp.float32),
        ],
    )
    flops = 4 * block_count * tok_rows * tok_rows * head_size * head_count
    return pl.pallas_call(
        kernel,
        grid_spec=grid_spec,
        out_shape=jax.ShapeDtypeStruct(q_seq.shape, q_seq.dtype),
        compiler_params=pltpu.CompilerParams(dimension_semantics=("arbitrary",)),
        cost_estimate=pl.CostEstimate(
            flops=flops,
            transcendentals=block_count * tok_rows * tok_rows * head_count,
            bytes_accessed=(gathered.size + received.size) * 2 + q_seq.size * 4,
        ),
    )(meta, q_seq, query_seg, gathered, received)


def solution(mesh):
    in_specs = (
        P(("outer", "inner"), None),
        P(("outer", "inner"), None),
        P("outer", None),
        P("outer"),
        P(("outer", "inner")),
    )
    out_specs = P(("outer", "inner"), None)
    return jax.shard_map(local, mesh=mesh, in_specs=in_specs, out_specs=out_specs, check_vma=False)
```

```python
import math

import jax
import jax.numpy as jnp
from jax import lax
from jax.experimental import pallas as pl
from jax.experimental.pallas import tpu as pltpu
from jax.sharding import PartitionSpec as P


def shifted(value, axis, steps):
    count = lax.axis_size(axis)
    leading, last = (max(0, -steps), min(count, count - steps))
    return lax.ppermute(value, axis, [(source, source + steps) for source in range(leading, last)])


def select_rows(selector, blocks, pattern):
    return jnp.einsum(
        pattern, selector.astype(jnp.bfloat16), blocks, preferred_element_type=jnp.float32
    ).astype(jnp.bfloat16)


def local(q_load, kv_load, pack_dest, counts, segment_ids):
    group_width = lax.axis_size("inner")
    my_index = lax.axis_index("inner")
    capacity = pack_dest.shape[1]
    slot_count = capacity // 2
    pair_limit = -(-capacity // group_width)
    row_length = q_load.shape[0] // capacity
    query_width = q_load.shape[1]
    pair_width = kv_load.shape[1]
    head_size = pair_width // 2
    head_count = query_width // head_size
    slot_grid = lax.broadcasted_iota(jnp.int32, (group_width, capacity), 1)
    live_all = slot_grid < counts[:, None]
    owner_all = pack_dest // slot_count
    slot_numbers = jnp.arange(capacity, dtype=jnp.int32)
    earlier = slot_numbers[None, :] < slot_numbers[:, None]
    same_owner = owner_all[:, :, None] == owner_all[:, None, :]
    rank_all = jnp.sum(
        (earlier[None] & same_owner & live_all[:, None, :]).astype(jnp.int32), axis=2
    )
    shard_rows = jnp.arange(group_width, dtype=jnp.int32)
    mine_row = (shard_rows == my_index)[:, None]
    my_owner = jnp.sum(jnp.where(mine_row, owner_all, 0), axis=0)
    my_rank = jnp.sum(jnp.where(mine_row, rank_all, 0), axis=0)
    my_live = jnp.any(mine_row & live_all, axis=0)
    pair_ids = jnp.arange(pair_limit, dtype=jnp.int32)
    send_select = (
        my_live[None, None, :]
        & (my_owner[None, None, :] == shard_rows[:, None, None])
        & (my_rank[None, None, :] == pair_ids[None, :, None])
    )
    q_blocks = q_load.reshape(capacity, row_length, query_width)
    kv_blocks = kv_load.reshape(capacity, row_length, pair_width)
    send_q = select_rows(send_select, q_blocks, "jkc,crf->jkrf")
    send_kv = select_rows(send_select, kv_blocks, "jkc,crf->jkrf")
    recv_both = lax.all_to_all(
        jnp.concatenate([send_q, send_kv], axis=3), "inner", split_axis=0, concat_axis=0, tiled=True
    )
    recv_q = recv_both[..., :query_width]
    recv_kv = recv_both[..., query_width:]
    wanted = my_index * slot_count + jnp.arange(slot_count, dtype=jnp.int32)
    take_select = jnp.any(
        live_all[None, :, None, :]
        & (pack_dest[None, :, None, :] == wanted[:, None, None, None])
        & (rank_all[None, :, None, :] == pair_ids[None, None, :, None]),
        axis=3,
    )
    q_seq = select_rows(take_select, recv_q, "srk,rktf->stf").reshape(
        slot_count * row_length, query_width
    )
    kv_seq = select_rows(take_select, recv_kv, "srk,rktf->stf").reshape(
        slot_count * row_length, pair_width
    )
    tok_rows = q_seq.shape[0]
    owner_index = lax.axis_index(("outer", "inner"))
    outer_index = lax.axis_index("outer")
    score_scale = 1.0 / math.sqrt(head_size)
    extra_rows = 16
    seg_rows = tok_rows // pair_width
    seg_pad = jnp.zeros((extra_rows - seg_rows, pair_width), jnp.bfloat16)
    packed = jnp.concatenate(
        [kv_seq, segment_ids.astype(jnp.bfloat16).reshape(seg_rows, pair_width), seg_pad], axis=0
    )
    outer_reach = -(-(lax.axis_size("outer") * group_width // 4) // group_width)
    own_steps = list(range(0, outer_reach + 1, 2))
    partner_steps = list(range(1, outer_reach + 1, 2))
    moved = [packed if step == 0 else shifted(packed, "outer", step) for step in own_steps]
    own_stack = jnp.stack(moved)
    parity = outer_index % 2
    outer_count = lax.axis_size("outer")
    partner_pairs = [(o, o ^ 1) for o in range(outer_count)]
    first_seg = segment_ids[0].astype(jnp.bfloat16)
    last_seg = segment_ids[tok_rows - 1].astype(jnp.bfloat16)
    query_seg = segment_ids.astype(jnp.float32).reshape(tok_rows, 1)
    state = (
        jnp.full((head_count, tok_rows, head_size), -1e30, jnp.float32),
        jnp.zeros((head_count, tok_rows, head_size), jnp.float32),
        jnp.zeros((head_count, tok_rows, head_size), jnp.float32),
    )
    q_heads = jnp.transpose(q_seq.reshape(tok_rows, head_count, head_size), (1, 0, 2))

    def run(state, kv, key_device):
        key_first = kv[:, tok_rows, 0]
        key_last = kv[:, tok_rows + seg_rows - 1, pair_width - 1]
        needed = (
            (key_device >= 0)
            & (key_device <= owner_index)
            & (key_last >= first_seg)
            & (key_first <= last_seg)
        )
        whole = (
            (key_device < owner_index)
            & (key_first == key_last)
            & (key_first == first_seg)
            & (first_seg == last_seg)
        )
        needed = jnp.where(needed, jnp.where(whole, 1, 2), 0).astype(jnp.int32)
        meta = jnp.concatenate([owner_index.reshape(1).astype(jnp.int32), needed, key_device])
        return attend(meta, q_heads, query_seg, kv, state, score_scale)

    own_offsets = jnp.array(own_steps, jnp.int32)
    partner_offsets = jnp.array(partner_steps, jnp.int32)
    pieces = []
    states = []
    lag = 3
    for s in range(group_width):
        if s == 0:
            piece = own_stack
        else:
            source = own_stack
            if s > lag:
                source = lax.optimization_barrier((own_stack, states[s - lag]))[0]
            piece = lax.ppermute(
                source, "inner", [(i, (i + s) % group_width) for i in range(group_width)]
            )
        pieces.append(piece)
        inner_of = (my_index - s) % group_width
        state = run(state, piece, (outer_index - own_offsets) * group_width + inner_of)
        states.append(state[0])
    stacked = jnp.stack(pieces)
    offer = lax.dynamic_slice_in_dim(stacked, parity, len(partner_steps), axis=1)
    received = lax.ppermute(offer, "outer", partner_pairs)
    inner_all = (my_index - jnp.arange(group_width, dtype=jnp.int32)) % group_width
    received_device = (outer_index - partner_offsets[None, :]) * group_width + inner_all[:, None]
    state = run(
        state,
        received.reshape(-1, received.shape[2], pair_width),
        received_device.reshape(-1),
    )
    largest, denominator, weighted = state
    out = weighted / denominator
    return jnp.transpose(out, (1, 0, 2)).reshape(tok_rows, query_width).astype(jnp.bfloat16)


def attend(meta, q_heads, query_seg, blocks, state, score_scale):
    head_count, tok_rows, head_size = q_heads.shape
    block_count, packed_rows, pair_width = blocks.shape
    seg_rows = tok_rows // pair_width

    def kernel(meta_ref, q_ref, qseg_ref, kv_ref, m_in, l_in, acc_in, m_ref, l_ref, acc_ref):
        b = pl.program_id(0)

        @pl.when(b == 0)
        def _():
            m_ref[...] = m_in[...]
            l_ref[...] = l_in[...]
            acc_ref[...] = acc_in[...]

        def absorb(masked_block):
            keys = kv_ref[0, :tok_rows, :head_size]
            values = kv_ref[0, :tok_rows, head_size:]
            if masked_block:
                own = meta_ref[0]
                device = meta_ref[1 + block_count + b]
                seg_parts = [
                    kv_ref[0, tok_rows + r : tok_rows + r + 1, :].astype(jnp.float32)
                    for r in range(seg_rows)
                ]
                key_seg = jnp.concatenate(seg_parts, axis=1)
                key_pos = device * tok_rows + lax.broadcasted_iota(jnp.int32, (1, tok_rows), 1)
                query_pos = own * tok_rows + lax.broadcasted_iota(jnp.int32, (tok_rows, 1), 0)
                visible = (key_pos <= query_pos) & (key_seg == qseg_ref[...])

            def one_head(h, carry):
                scores = lax.dot_general(
                    q_ref[h], keys, (((1,), (1,)), ((), ())), preferred_element_type=jnp.float32
                )
                if masked_block:
                    scores = jnp.where(visible, scores, -1e30)
                m_prev = m_ref[h]
                m_next = jnp.maximum(m_prev, jnp.max(scores, axis=1, keepdims=True))
                factor = jnp.exp((m_prev - m_next) * score_scale)
                m_row = m_next[:, :1]
                if masked_block:
                    m_row = jnp.where(m_row == -1e30, 0.0, m_row)
                weights = jnp.exp((scores - m_row) * score_scale)
                l_ref[h] = l_ref[h] * factor + jnp.sum(weights, axis=1, keepdims=True)
                acc_ref[h] = acc_ref[h] * factor + jnp.dot(
                    weights.astype(jnp.bfloat16), values, preferred_element_type=jnp.float32
                )
                m_ref[h] = m_next
                return carry

            lax.fori_loop(0, head_count, one_head, 0)

        mode = meta_ref[1 + b]
        for masked_block, code in ((False, 1), (True, 2)):
            @pl.when(mode == code)
            def _(masked_block=masked_block):
                absorb(masked_block)

    state_spec = pl.BlockSpec(state[0].shape, lambda b, meta: (0, 0, 0))
    grid_spec = pltpu.PrefetchScalarGridSpec(
        num_scalar_prefetch=1,
        grid=(block_count,),
        in_specs=[
            pl.BlockSpec(q_heads.shape, lambda b, meta: (0, 0, 0)),
            pl.BlockSpec(query_seg.shape, lambda b, meta: (0, 0)),
            pl.BlockSpec((1, packed_rows, pair_width), lambda b, meta: (b, 0, 0)),
            state_spec,
            state_spec,
            state_spec,
        ],
        out_specs=[state_spec, state_spec, state_spec],
    )
    flops = 4 * block_count * tok_rows * tok_rows * head_size * head_count
    state_shape = jax.ShapeDtypeStruct(state[0].shape, jnp.float32)
    return pl.pallas_call(
        kernel,
        grid_spec=grid_spec,
        out_shape=[state_shape, state_shape, state_shape],
        input_output_aliases={4: 0, 5: 1, 6: 2},
        compiler_params=pltpu.CompilerParams(dimension_semantics=("arbitrary",)),
        cost_estimate=pl.CostEstimate(
            flops=flops,
            transcendentals=block_count * tok_rows * tok_rows * head_count,
            bytes_accessed=blocks.size * 2 + q_heads.size * 2 + state[0].size * 24,
        ),
    )(meta, q_heads, query_seg, blocks, *state)


def solution(mesh):
    in_specs = (
        P(("outer", "inner"), None),
        P(("outer", "inner"), None),
        P("outer", None),
        P("outer"),
        P(("outer", "inner")),
    )
    out_specs = P(("outer", "inner"), None)
    return jax.shard_map(local, mesh=mesh, in_specs=in_specs, out_specs=out_specs, check_vma=False)
```

```python
import math

import jax
import jax.numpy as jnp
from jax import lax
from jax.experimental import pallas as pl
from jax.experimental.pallas import tpu as pltpu
from jax.sharding import PartitionSpec as P


def shifted(value, axis, steps):
    count = lax.axis_size(axis)
    leading, last = (max(0, -steps), min(count, count - steps))
    return lax.ppermute(value, axis, [(source, source + steps) for source in range(leading, last)])


def select_rows(selector, blocks, pattern):
    return jnp.einsum(
        pattern, selector.astype(jnp.bfloat16), blocks, preferred_element_type=jnp.float32
    ).astype(jnp.bfloat16)


def local(q_load, kv_load, pack_dest, counts, segment_ids):
    group_width = lax.axis_size("inner")
    my_index = lax.axis_index("inner")
    capacity = pack_dest.shape[1]
    slot_count = capacity // 2
    pair_limit = -(-capacity // group_width)
    row_length = q_load.shape[0] // capacity
    query_width = q_load.shape[1]
    pair_width = kv_load.shape[1]
    head_size = pair_width // 2
    head_count = query_width // head_size
    slot_grid = lax.broadcasted_iota(jnp.int32, (group_width, capacity), 1)
    live_all = slot_grid < counts[:, None]
    owner_all = pack_dest // slot_count
    slot_numbers = jnp.arange(capacity, dtype=jnp.int32)
    earlier = slot_numbers[None, :] < slot_numbers[:, None]
    same_owner = owner_all[:, :, None] == owner_all[:, None, :]
    rank_all = jnp.sum(
        (earlier[None] & same_owner & live_all[:, None, :]).astype(jnp.int32), axis=2
    )
    shard_rows = jnp.arange(group_width, dtype=jnp.int32)
    mine_row = (shard_rows == my_index)[:, None]
    my_owner = jnp.sum(jnp.where(mine_row, owner_all, 0), axis=0)
    my_rank = jnp.sum(jnp.where(mine_row, rank_all, 0), axis=0)
    my_live = jnp.any(mine_row & live_all, axis=0)
    pair_ids = jnp.arange(pair_limit, dtype=jnp.int32)
    send_select = (
        my_live[None, None, :]
        & (my_owner[None, None, :] == shard_rows[:, None, None])
        & (my_rank[None, None, :] == pair_ids[None, :, None])
    )
    q_blocks = q_load.reshape(capacity, row_length, query_width)
    kv_blocks = kv_load.reshape(capacity, row_length, pair_width)
    send_q = select_rows(send_select, q_blocks, "jkc,crf->jkrf")
    send_kv = select_rows(send_select, kv_blocks, "jkc,crf->jkrf")
    recv_both = lax.all_to_all(
        jnp.concatenate([send_q, send_kv], axis=3), "inner", split_axis=0, concat_axis=0, tiled=True
    )
    recv_q = recv_both[..., :query_width]
    recv_kv = recv_both[..., query_width:]
    wanted = my_index * slot_count + jnp.arange(slot_count, dtype=jnp.int32)
    take_select = jnp.any(
        live_all[None, :, None, :]
        & (pack_dest[None, :, None, :] == wanted[:, None, None, None])
        & (rank_all[None, :, None, :] == pair_ids[None, None, :, None]),
        axis=3,
    )
    q_seq = select_rows(take_select, recv_q, "srk,rktf->stf").reshape(
        slot_count * row_length, query_width
    )
    kv_seq = select_rows(take_select, recv_kv, "srk,rktf->stf").reshape(
        slot_count * row_length, pair_width
    )
    tok_rows = q_seq.shape[0]
    owner_index = lax.axis_index(("outer", "inner"))
    outer_index = lax.axis_index("outer")
    score_scale = 1.0 / math.sqrt(head_size)
    extra_rows = 16
    seg_rows = tok_rows // pair_width
    seg_pad = jnp.zeros((extra_rows - seg_rows, pair_width), jnp.bfloat16)
    packed = jnp.concatenate(
        [kv_seq, segment_ids.astype(jnp.bfloat16).reshape(seg_rows, pair_width), seg_pad], axis=0
    )
    outer_reach = -(-(lax.axis_size("outer") * group_width // 4) // group_width)
    own_steps = list(range(0, outer_reach + 1, 2))
    partner_steps = list(range(1, outer_reach + 1, 2))
    moved = [packed if step == 0 else shifted(packed, "outer", step) for step in own_steps]
    own_stack = jnp.stack(moved)
    inner_shifts = [own_stack] + [
        lax.ppermute(own_stack, "inner", [(i, (i + s) % group_width) for i in range(group_width)])
        for s in range(1, group_width)
    ]
    gathered = jnp.stack(inner_shifts)
    inner_of = (my_index - jnp.arange(group_width, dtype=jnp.int32)) % group_width
    parity = outer_index % 2
    offer = lax.dynamic_slice_in_dim(gathered, parity, len(partner_steps), axis=1)
    outer_count = lax.axis_size("outer")
    partner_pairs = [(o, o ^ 1) for o in range(outer_count)]
    received = lax.ppermute(offer, "outer", partner_pairs)
    sources = [(gathered, own_steps), (received, partner_steps)]
    key_device, key_first, key_last = [], [], []
    for array, steps in sources:
        for slot, step in enumerate(steps):
            key_device.append(
                (outer_index - step) * group_width + inner_of
            )
            key_first.append(array[:, slot, tok_rows, 0])
            key_last.append(array[:, slot, tok_rows + seg_rows - 1, pair_width - 1])
    key_device = jnp.concatenate(key_device)
    key_first = jnp.concatenate(key_first)
    key_last = jnp.concatenate(key_last)
    first_seg = segment_ids[0].astype(jnp.bfloat16)
    last_seg = segment_ids[tok_rows - 1].astype(jnp.bfloat16)
    needed = (
        (key_device >= 0)
        & (key_device <= owner_index)
        & (key_last >= first_seg)
        & (key_first <= last_seg)
    )
    whole = (
        (key_device < owner_index)
        & (key_first == key_last)
        & (key_first == first_seg)
        & (first_seg == last_seg)
    )
    needed = jnp.where(needed, jnp.where(whole, 1, 2), 0).astype(jnp.int32)
    meta = jnp.concatenate([owner_index.reshape(1).astype(jnp.int32), needed, key_device])
    query_seg = segment_ids.astype(jnp.float32).reshape(tok_rows, 1)
    return attend(meta, q_seq, query_seg, gathered, received, head_count, head_size, score_scale)


def attend(meta, q_seq, query_seg, gathered, received, head_count, head_size, score_scale):
    tok_rows = q_seq.shape[0]
    group_width, first_slots, packed_rows, pair_width = gathered.shape
    second_slots = received.shape[1]
    first_count = group_width * first_slots
    block_count = first_count + group_width * second_slots
    seg_rows = tok_rows // pair_width

    def kernel(meta_ref, q_ref, qseg_ref, first_ref, second_ref, out_ref, m_ref, l_ref, acc_ref):
        b = pl.program_id(0)

        @pl.when(b == 0)
        def _():
            m_ref[...] = jnp.full(m_ref.shape, -1e30, jnp.float32)
            l_ref[...] = jnp.zeros(l_ref.shape, jnp.float32)
            acc_ref[...] = jnp.zeros(acc_ref.shape, jnp.float32)

        def absorb(kv_ref, masked_block):
            keys = kv_ref[0, 0, :tok_rows, :head_size]
            values = kv_ref[0, 0, :tok_rows, head_size:]
            ones = jnp.ones((tok_rows, head_size), jnp.bfloat16)
            if masked_block:
                own = meta_ref[0]
                device = meta_ref[1 + block_count + b]
                seg_parts = [
                    kv_ref[0, 0, tok_rows + r : tok_rows + r + 1, :].astype(jnp.float32)
                    for r in range(seg_rows)
                ]
                key_seg = jnp.concatenate(seg_parts, axis=1)
                key_pos = device * tok_rows + lax.broadcasted_iota(jnp.int32, (1, tok_rows), 1)
                query_pos = own * tok_rows + lax.broadcasted_iota(jnp.int32, (tok_rows, 1), 0)
                visible = (key_pos <= query_pos) & (key_seg == qseg_ref[...])
            for h in range(head_count):
                queries = q_ref[:, h * head_size : (h + 1) * head_size]
                scores = lax.dot_general(
                    queries, keys, (((1,), (1,)), ((), ())), preferred_element_type=jnp.float32
                )
                if masked_block:
                    scores = jnp.where(visible, scores, -1e30)
                m_prev = m_ref[h]
                m_next = jnp.maximum(m_prev, jnp.max(scores, axis=1, keepdims=True))
                factor = jnp.exp((m_prev - m_next) * score_scale)
                m_row = m_next[:, :1]
                if masked_block:
                    m_row = jnp.where(m_row == -1e30, 0.0, m_row)
                weights = jnp.exp(scores * score_scale - m_row * score_scale).astype(jnp.bfloat16)
                l_ref[h] = l_ref[h] * factor + jnp.dot(
                    weights, ones, preferred_element_type=jnp.float32
                )
                acc_ref[h] = acc_ref[h] * factor + jnp.dot(
                    weights, values, preferred_element_type=jnp.float32
                )
                m_ref[h] = m_next

        mode = meta_ref[1 + b]
        for ref, in_range in ((first_ref, b < first_count), (second_ref, b >= first_count)):
            for masked_block, code in ((False, 1), (True, 2)):
                @pl.when(in_range & (mode == code))
                def _(ref=ref, masked_block=masked_block):
                    absorb(ref, masked_block)

        @pl.when(b == block_count - 1)
        def _():
            for h in range(head_count):
                out_ref[:, h * head_size : (h + 1) * head_size] = (
                    acc_ref[h] / l_ref[h]
                ).astype(out_ref.dtype)

    def first_map(b, meta):
        c = jnp.minimum(b, first_count - 1)
        return (c % group_width, c // group_width, 0, 0)

    def second_map(b, meta):
        c = jnp.maximum(b - first_count, 0)
        return (c % group_width, c // group_width, 0, 0)

    grid_spec = pltpu.PrefetchScalarGridSpec(
        num_scalar_prefetch=1,
        grid=(block_count,),
        in_specs=[
            pl.BlockSpec(q_seq.shape, lambda b, meta: (0, 0)),
            pl.BlockSpec(query_seg.shape, lambda b, meta: (0, 0)),
            pl.BlockSpec((1, 1, packed_rows, pair_width), first_map),
            pl.BlockSpec((1, 1, packed_rows, pair_width), second_map),
        ],
        out_specs=pl.BlockSpec(q_seq.shape, lambda b, meta: (0, 0)),
        scratch_shapes=[
            pltpu.VMEM((head_count, tok_rows, head_size), jnp.float32),
            pltpu.VMEM((head_count, tok_rows, head_size), jnp.float32),
            pltpu.VMEM((head_count, tok_rows, head_size), jnp.float32),
        ],
    )
    flops = 4 * block_count * tok_rows * tok_rows * head_size * head_count
    return pl.pallas_call(
        kernel,
        grid_spec=grid_spec,
        out_shape=jax.ShapeDtypeStruct(q_seq.shape, q_seq.dtype),
        compiler_params=pltpu.CompilerParams(dimension_semantics=("arbitrary",)),
        cost_estimate=pl.CostEstimate(
            flops=flops,
            transcendentals=block_count * tok_rows * tok_rows * head_count,
            bytes_accessed=(gathered.size + received.size) * 2 + q_seq.size * 4,
        ),
    )(meta, q_seq, query_seg, gathered, received)


def solution(mesh):
    in_specs = (
        P(("outer", "inner"), None),
        P(("outer", "inner"), None),
        P("outer", None),
        P("outer"),
        P(("outer", "inner")),
    )
    out_specs = P(("outer", "inner"), None)
    return jax.shard_map(local, mesh=mesh, in_specs=in_specs, out_specs=out_specs, check_vma=False)
```

```python
import math

import jax
import jax.numpy as jnp
from jax import lax
from jax.experimental import pallas as pl
from jax.experimental.pallas import tpu as pltpu
from jax.sharding import PartitionSpec as P


def shifted(value, axis, steps):
    count = lax.axis_size(axis)
    leading, last = (max(0, -steps), min(count, count - steps))
    return lax.ppermute(value, axis, [(source, source + steps) for source in range(leading, last)])


def select_rows(selector, blocks, pattern):
    return jnp.einsum(
        pattern, selector.astype(jnp.bfloat16), blocks, preferred_element_type=jnp.float32
    ).astype(jnp.bfloat16)


def local(q_load, kv_load, pack_dest, counts, segment_ids):
    group_width = lax.axis_size("inner")
    my_index = lax.axis_index("inner")
    capacity = pack_dest.shape[1]
    slot_count = capacity // 2
    pair_limit = -(-capacity // group_width)
    row_length = q_load.shape[0] // capacity
    query_width = q_load.shape[1]
    pair_width = kv_load.shape[1]
    head_size = pair_width // 2
    head_count = query_width // head_size
    slot_grid = lax.broadcasted_iota(jnp.int32, (group_width, capacity), 1)
    live_all = slot_grid < counts[:, None]
    owner_all = pack_dest // slot_count
    slot_numbers = jnp.arange(capacity, dtype=jnp.int32)
    earlier = slot_numbers[None, :] < slot_numbers[:, None]
    same_owner = owner_all[:, :, None] == owner_all[:, None, :]
    rank_all = jnp.sum(
        (earlier[None] & same_owner & live_all[:, None, :]).astype(jnp.int32), axis=2
    )
    shard_rows = jnp.arange(group_width, dtype=jnp.int32)
    mine_row = (shard_rows == my_index)[:, None]
    my_owner = jnp.sum(jnp.where(mine_row, owner_all, 0), axis=0)
    my_rank = jnp.sum(jnp.where(mine_row, rank_all, 0), axis=0)
    my_live = jnp.any(mine_row & live_all, axis=0)
    pair_ids = jnp.arange(pair_limit, dtype=jnp.int32)
    send_select = (
        my_live[None, None, :]
        & (my_owner[None, None, :] == shard_rows[:, None, None])
        & (my_rank[None, None, :] == pair_ids[None, :, None])
    )
    q_blocks = q_load.reshape(capacity, row_length, query_width)
    kv_blocks = kv_load.reshape(capacity, row_length, pair_width)
    send_q = select_rows(send_select, q_blocks, "jkc,crf->jkrf")
    send_kv = select_rows(send_select, kv_blocks, "jkc,crf->jkrf")
    recv_both = lax.all_to_all(
        jnp.concatenate([send_q, send_kv], axis=3), "inner", split_axis=0, concat_axis=0, tiled=True
    )
    recv_q = recv_both[..., :query_width]
    recv_kv = recv_both[..., query_width:]
    wanted = my_index * slot_count + jnp.arange(slot_count, dtype=jnp.int32)
    take_select = jnp.any(
        live_all[None, :, None, :]
        & (pack_dest[None, :, None, :] == wanted[:, None, None, None])
        & (rank_all[None, :, None, :] == pair_ids[None, None, :, None]),
        axis=3,
    )
    q_seq = select_rows(take_select, recv_q, "srk,rktf->stf").reshape(
        slot_count * row_length, query_width
    )
    kv_seq = select_rows(take_select, recv_kv, "srk,rktf->stf").reshape(
        slot_count * row_length, pair_width
    )
    tok_rows = q_seq.shape[0]
    owner_index = lax.axis_index(("outer", "inner"))
    outer_index = lax.axis_index("outer")
    score_scale = 1.0 / math.sqrt(head_size)
    extra_rows = 16
    seg_rows = tok_rows // pair_width
    seg_pad = jnp.zeros((extra_rows - seg_rows, pair_width), jnp.bfloat16)
    packed = jnp.concatenate(
        [kv_seq, segment_ids.astype(jnp.bfloat16).reshape(seg_rows, pair_width), seg_pad], axis=0
    )
    outer_reach = -(-(lax.axis_size("outer") * group_width // 4) // group_width)
    own_steps = list(range(0, outer_reach + 1, 2))
    partner_steps = list(range(1, outer_reach + 1, 2))
    moved = [packed if step == 0 else shifted(packed, "outer", step) for step in own_steps]
    own_stack = jnp.stack(moved)
    parity = outer_index % 2
    outer_count = lax.axis_size("outer")
    partner_pairs = [(o, o ^ 1) for o in range(outer_count)]
    first_seg = segment_ids[0].astype(jnp.bfloat16)
    last_seg = segment_ids[tok_rows - 1].astype(jnp.bfloat16)
    query_seg = segment_ids.astype(jnp.float32).reshape(tok_rows, 1)
    state = (
        jnp.full((head_count, tok_rows, head_size), -1e30, jnp.float32),
        jnp.zeros((head_count, tok_rows, head_size), jnp.float32),
        jnp.zeros((head_count, tok_rows, head_size), jnp.float32),
    )
    q_heads = jnp.transpose(q_seq.reshape(tok_rows, head_count, head_size), (1, 0, 2))

    def run(state, kv, key_device):
        key_first = kv[:, tok_rows, 0]
        key_last = kv[:, tok_rows + seg_rows - 1, pair_width - 1]
        needed = (
            (key_device >= 0)
            & (key_device <= owner_index)
            & (key_last >= first_seg)
            & (key_first <= last_seg)
        )
        whole = (
            (key_device < owner_index)
            & (key_first == key_last)
            & (key_first == first_seg)
            & (first_seg == last_seg)
        )
        needed = jnp.where(needed, jnp.where(whole, 1, 2), 0).astype(jnp.int32)
        meta = jnp.concatenate([owner_index.reshape(1).astype(jnp.int32), needed, key_device])
        return attend(meta, q_heads, query_seg, kv, state, score_scale)

    own_offsets = jnp.array(own_steps, jnp.int32)
    partner_offsets = jnp.array(partner_steps, jnp.int32)
    pieces = []
    states = []
    shift_groups = [[0, 1, 2], [3, 4, 5], [6, 7]]
    for g, shifts in enumerate(shift_groups):
        group_pieces, group_devices = [], []
        for s in shifts:
            if s == 0:
                piece = own_stack
            else:
                source = own_stack
                if g >= 2:
                    source = lax.optimization_barrier((own_stack, states[g - 2]))[0]
                piece = lax.ppermute(
                    source, "inner", [(i, (i + s) % group_width) for i in range(group_width)]
                )
            pieces.append(piece)
            group_pieces.append(piece)
            inner_of = (my_index - s) % group_width
            group_devices.append((outer_index - own_offsets) * group_width + inner_of)
        state = run(state, jnp.concatenate(group_pieces), jnp.concatenate(group_devices))
        states.append(state[0])
    stacked = jnp.stack(pieces)
    offer = lax.dynamic_slice_in_dim(stacked, parity, len(partner_steps), axis=1)
    received = lax.ppermute(offer, "outer", partner_pairs)
    inner_all = (my_index - jnp.arange(group_width, dtype=jnp.int32)) % group_width
    received_device = (outer_index - partner_offsets[None, :]) * group_width + inner_all[:, None]
    state = run(
        state,
        received.reshape(-1, received.shape[2], pair_width),
        received_device.reshape(-1),
    )
    largest, denominator, weighted = state
    out = weighted / denominator
    return jnp.transpose(out, (1, 0, 2)).reshape(tok_rows, query_width).astype(jnp.bfloat16)


def attend(meta, q_heads, query_seg, blocks, state, score_scale):
    head_count, tok_rows, head_size = q_heads.shape
    block_count, packed_rows, pair_width = blocks.shape
    seg_rows = tok_rows // pair_width

    def kernel(meta_ref, q_ref, qseg_ref, kv_ref, m_in, l_in, acc_in, m_ref, l_ref, acc_ref):
        b = pl.program_id(0)

        @pl.when(b == 0)
        def _():
            m_ref[...] = m_in[...]
            l_ref[...] = l_in[...]
            acc_ref[...] = acc_in[...]

        def absorb(masked_block):
            keys = kv_ref[0, :tok_rows, :head_size]
            values = kv_ref[0, :tok_rows, head_size:]
            if masked_block:
                own = meta_ref[0]
                device = meta_ref[1 + block_count + b]
                seg_parts = [
                    kv_ref[0, tok_rows + r : tok_rows + r + 1, :].astype(jnp.float32)
                    for r in range(seg_rows)
                ]
                key_seg = jnp.concatenate(seg_parts, axis=1)
                key_pos = device * tok_rows + lax.broadcasted_iota(jnp.int32, (1, tok_rows), 1)
                query_pos = own * tok_rows + lax.broadcasted_iota(jnp.int32, (tok_rows, 1), 0)
                visible = (key_pos <= query_pos) & (key_seg == qseg_ref[...])

            def one_head(h, carry):
                scores = lax.dot_general(
                    q_ref[h], keys, (((1,), (1,)), ((), ())), preferred_element_type=jnp.float32
                )
                if masked_block:
                    scores = jnp.where(visible, scores, -1e30)
                m_prev = m_ref[h]
                m_next = jnp.maximum(m_prev, jnp.max(scores, axis=1, keepdims=True))
                factor = jnp.exp((m_prev - m_next) * score_scale)
                m_row = m_next[:, :1]
                if masked_block:
                    m_row = jnp.where(m_row == -1e30, 0.0, m_row)
                weights = jnp.exp((scores - m_row) * score_scale)
                l_ref[h] = l_ref[h] * factor + jnp.sum(weights, axis=1, keepdims=True)
                acc_ref[h] = acc_ref[h] * factor + jnp.dot(
                    weights.astype(jnp.bfloat16), values, preferred_element_type=jnp.float32
                )
                m_ref[h] = m_next
                return carry

            lax.fori_loop(0, head_count, one_head, 0)

        mode = meta_ref[1 + b]
        for masked_block, code in ((False, 1), (True, 2)):
            @pl.when(mode == code)
            def _(masked_block=masked_block):
                absorb(masked_block)

    state_spec = pl.BlockSpec(state[0].shape, lambda b, meta: (0, 0, 0))
    grid_spec = pltpu.PrefetchScalarGridSpec(
        num_scalar_prefetch=1,
        grid=(block_count,),
        in_specs=[
            pl.BlockSpec(q_heads.shape, lambda b, meta: (0, 0, 0)),
            pl.BlockSpec(query_seg.shape, lambda b, meta: (0, 0)),
            pl.BlockSpec((1, packed_rows, pair_width), lambda b, meta: (b, 0, 0)),
            state_spec,
            state_spec,
            state_spec,
        ],
        out_specs=[state_spec, state_spec, state_spec],
    )
    flops = 4 * block_count * tok_rows * tok_rows * head_size * head_count
    state_shape = jax.ShapeDtypeStruct(state[0].shape, jnp.float32)
    return pl.pallas_call(
        kernel,
        grid_spec=grid_spec,
        out_shape=[state_shape, state_shape, state_shape],
        input_output_aliases={4: 0, 5: 1, 6: 2},
        compiler_params=pltpu.CompilerParams(dimension_semantics=("arbitrary",)),
        cost_estimate=pl.CostEstimate(
            flops=flops,
            transcendentals=block_count * tok_rows * tok_rows * head_count,
            bytes_accessed=blocks.size * 2 + q_heads.size * 2 + state[0].size * 24,
        ),
    )(meta, q_heads, query_seg, blocks, *state)


def solution(mesh):
    in_specs = (
        P(("outer", "inner"), None),
        P(("outer", "inner"), None),
        P("outer", None),
        P("outer"),
        P(("outer", "inner")),
    )
    out_specs = P(("outer", "inner"), None)
    return jax.shard_map(local, mesh=mesh, in_specs=in_specs, out_specs=out_specs, check_vma=False)
```

```python
import math

import jax
import jax.numpy as jnp
from jax import lax
from jax.experimental import pallas as pl
from jax.experimental.pallas import tpu as pltpu
from jax.sharding import PartitionSpec as P


def shifted(value, axis, steps):
    count = lax.axis_size(axis)
    leading, last = (max(0, -steps), min(count, count - steps))
    return lax.ppermute(value, axis, [(source, source + steps) for source in range(leading, last)])


def select_rows(selector, blocks, pattern):
    return jnp.einsum(
        pattern, selector.astype(jnp.bfloat16), blocks, preferred_element_type=jnp.float32
    ).astype(jnp.bfloat16)


def local(q_load, kv_load, pack_dest, counts, segment_ids):
    group_width = lax.axis_size("inner")
    my_index = lax.axis_index("inner")
    capacity = pack_dest.shape[1]
    slot_count = capacity // 2
    pair_limit = -(-capacity // group_width)
    row_length = q_load.shape[0] // capacity
    query_width = q_load.shape[1]
    pair_width = kv_load.shape[1]
    head_size = pair_width // 2
    head_count = query_width // head_size
    slot_grid = lax.broadcasted_iota(jnp.int32, (group_width, capacity), 1)
    live_all = slot_grid < counts[:, None]
    owner_all = pack_dest // slot_count
    slot_numbers = jnp.arange(capacity, dtype=jnp.int32)
    earlier = slot_numbers[None, :] < slot_numbers[:, None]
    same_owner = owner_all[:, :, None] == owner_all[:, None, :]
    rank_all = jnp.sum(
        (earlier[None] & same_owner & live_all[:, None, :]).astype(jnp.int32), axis=2
    )
    shard_rows = jnp.arange(group_width, dtype=jnp.int32)
    mine_row = (shard_rows == my_index)[:, None]
    my_owner = jnp.sum(jnp.where(mine_row, owner_all, 0), axis=0)
    my_rank = jnp.sum(jnp.where(mine_row, rank_all, 0), axis=0)
    my_live = jnp.any(mine_row & live_all, axis=0)
    pair_ids = jnp.arange(pair_limit, dtype=jnp.int32)
    send_select = (
        my_live[None, None, :]
        & (my_owner[None, None, :] == shard_rows[:, None, None])
        & (my_rank[None, None, :] == pair_ids[None, :, None])
    )
    q_blocks = q_load.reshape(capacity, row_length, query_width)
    kv_blocks = kv_load.reshape(capacity, row_length, pair_width)
    send_q = select_rows(send_select, q_blocks, "jkc,crf->jkrf")
    send_kv = select_rows(send_select, kv_blocks, "jkc,crf->jkrf")
    recv_both = lax.all_to_all(
        jnp.concatenate([send_q, send_kv], axis=3), "inner", split_axis=0, concat_axis=0, tiled=True
    )
    recv_q = recv_both[..., :query_width]
    recv_kv = recv_both[..., query_width:]
    wanted = my_index * slot_count + jnp.arange(slot_count, dtype=jnp.int32)
    take_select = jnp.any(
        live_all[None, :, None, :]
        & (pack_dest[None, :, None, :] == wanted[:, None, None, None])
        & (rank_all[None, :, None, :] == pair_ids[None, None, :, None]),
        axis=3,
    )
    q_seq = select_rows(take_select, recv_q, "srk,rktf->stf").reshape(
        slot_count * row_length, query_width
    )
    kv_seq = select_rows(take_select, recv_kv, "srk,rktf->stf").reshape(
        slot_count * row_length, pair_width
    )
    tok_rows = q_seq.shape[0]
    owner_index = lax.axis_index(("outer", "inner"))
    outer_index = lax.axis_index("outer")
    score_scale = 1.0 / math.sqrt(head_size)
    extra_rows = 16
    seg_rows = tok_rows // pair_width
    seg_pad = jnp.zeros((extra_rows - seg_rows, pair_width), jnp.bfloat16)
    packed = jnp.concatenate(
        [kv_seq, segment_ids.astype(jnp.bfloat16).reshape(seg_rows, pair_width), seg_pad], axis=0
    )
    outer_reach = -(-(lax.axis_size("outer") * group_width // 4) // group_width)
    own_steps = list(range(0, outer_reach + 1, 2))
    partner_steps = list(range(1, outer_reach + 1, 2))
    moved = [packed if step == 0 else shifted(packed, "outer", step) for step in own_steps]
    near_stack = jnp.stack(moved[:2])
    inner_shifts = [near_stack] + [
        lax.ppermute(near_stack, "inner", [(i, (i + s) % group_width) for i in range(group_width)])
        for s in range(1, group_width)
    ]
    near = jnp.stack(inner_shifts)
    far = lax.all_gather(moved[2], "inner", tiled=False)
    parity = outer_index % 2
    shift_ids = jnp.arange(group_width, dtype=jnp.int32)
    inner_of = (my_index - shift_ids) % group_width
    outer_count = lax.axis_size("outer")
    partner_pairs = [(o, o ^ 1) for o in range(outer_count)]
    offer = jnp.stack([near[:, 1], jnp.where(parity == 0, near[:, 0], far)], axis=1)
    received = lax.ppermute(offer, "outer", partner_pairs)
    first = jnp.concatenate([near, far[:, None]], axis=1)
    first_steps = [own_steps[0], own_steps[1], own_steps[2]]
    first_inner = [inner_of, inner_of, shift_ids]
    second_steps = [jnp.where(parity == 1, 3, 1), jnp.where(parity == 1, 1, 3)]
    second_inner = [inner_of, jnp.where(parity == 0, shift_ids, inner_of)]
    sources = [(first, first_steps, first_inner), (received, second_steps, second_inner)]
    key_device, key_first, key_last = [], [], []
    for array, steps, inners in sources:
        for slot in range(len(steps)):
            key_device.append((outer_index - steps[slot]) * group_width + inners[slot])
            key_first.append(array[:, slot, tok_rows, 0])
            key_last.append(array[:, slot, tok_rows + seg_rows - 1, pair_width - 1])
    key_device = jnp.concatenate(key_device)
    key_first = jnp.concatenate(key_first)
    key_last = jnp.concatenate(key_last)
    gathered = first
    first_seg = segment_ids[0].astype(jnp.bfloat16)
    last_seg = segment_ids[tok_rows - 1].astype(jnp.bfloat16)
    needed = (
        (key_device >= 0)
        & (key_device <= owner_index)
        & (key_last >= first_seg)
        & (key_first <= last_seg)
    )
    whole = (
        (key_device < owner_index)
        & (key_first == key_last)
        & (key_first == first_seg)
        & (first_seg == last_seg)
    )
    needed = jnp.where(needed, jnp.where(whole, 1, 2), 0).astype(jnp.int32)
    meta = jnp.concatenate([owner_index.reshape(1).astype(jnp.int32), needed, key_device])
    query_seg = segment_ids.astype(jnp.float32).reshape(tok_rows, 1)
    return attend(meta, q_seq, query_seg, gathered, received, head_count, head_size, score_scale)


def attend(meta, q_seq, query_seg, gathered, received, head_count, head_size, score_scale):
    tok_rows = q_seq.shape[0]
    group_width, first_slots, packed_rows, pair_width = gathered.shape
    second_slots = received.shape[1]
    first_count = group_width * first_slots
    block_count = first_count + group_width * second_slots
    seg_rows = tok_rows // pair_width

    def kernel(meta_ref, q_ref, qseg_ref, first_ref, second_ref, out_ref, m_ref, l_ref, acc_ref):
        b = pl.program_id(0)

        @pl.when(b == 0)
        def _():
            m_ref[...] = jnp.full(m_ref.shape, -1e30, jnp.float32)
            l_ref[...] = jnp.zeros(l_ref.shape, jnp.float32)
            acc_ref[...] = jnp.zeros(acc_ref.shape, jnp.float32)

        def absorb(kv_ref, masked_block):
            keys = kv_ref[0, 0, :tok_rows, :head_size]
            values = kv_ref[0, 0, :tok_rows, head_size:]
            if masked_block:
                own = meta_ref[0]
                device = meta_ref[1 + block_count + b]
                seg_parts = [
                    kv_ref[0, 0, tok_rows + r : tok_rows + r + 1, :].astype(jnp.float32)
                    for r in range(seg_rows)
                ]
                key_seg = jnp.concatenate(seg_parts, axis=1)
                key_pos = device * tok_rows + lax.broadcasted_iota(jnp.int32, (1, tok_rows), 1)
                query_pos = own * tok_rows + lax.broadcasted_iota(jnp.int32, (tok_rows, 1), 0)
                visible = (key_pos <= query_pos) & (key_seg == qseg_ref[...])
            for h in range(head_count):
                queries = q_ref[:, h * head_size : (h + 1) * head_size]
                scores = lax.dot_general(
                    queries, keys, (((1,), (1,)), ((), ())), preferred_element_type=jnp.float32
                )
                if masked_block:
                    scores = jnp.where(visible, scores, -1e30)
                m_prev = m_ref[h]
                m_next = jnp.maximum(m_prev, jnp.max(scores, axis=1, keepdims=True))
                factor = jnp.exp((m_prev - m_next) * score_scale)
                m_row = m_next[:, :1]
                if masked_block:
                    m_row = jnp.where(m_row == -1e30, 0.0, m_row)
                weights = jnp.exp((scores - m_row) * score_scale)
                l_ref[h] = l_ref[h] * factor + jnp.sum(weights, axis=1, keepdims=True)
                acc_ref[h] = acc_ref[h] * factor + jnp.dot(
                    weights.astype(jnp.bfloat16), values, preferred_element_type=jnp.float32
                )
                m_ref[h] = m_next

        mode = meta_ref[1 + b]
        for ref, in_range in ((first_ref, b < first_count), (second_ref, b >= first_count)):
            for masked_block, code in ((False, 1), (True, 2)):
                @pl.when(in_range & (mode == code))
                def _(ref=ref, masked_block=masked_block):
                    absorb(ref, masked_block)

        @pl.when(b == block_count - 1)
        def _():
            for h in range(head_count):
                out_ref[:, h * head_size : (h + 1) * head_size] = (
                    acc_ref[h] / l_ref[h]
                ).astype(out_ref.dtype)

    def first_map(b, meta):
        c = jnp.minimum(b, first_count - 1)
        return (c % group_width, c // group_width, 0, 0)

    def second_map(b, meta):
        c = jnp.maximum(b - first_count, 0)
        return (c % group_width, c // group_width, 0, 0)

    grid_spec = pltpu.PrefetchScalarGridSpec(
        num_scalar_prefetch=1,
        grid=(block_count,),
        in_specs=[
            pl.BlockSpec(q_seq.shape, lambda b, meta: (0, 0)),
            pl.BlockSpec(query_seg.shape, lambda b, meta: (0, 0)),
            pl.BlockSpec((1, 1, packed_rows, pair_width), first_map),
            pl.BlockSpec((1, 1, packed_rows, pair_width), second_map),
        ],
        out_specs=pl.BlockSpec(q_seq.shape, lambda b, meta: (0, 0)),
        scratch_shapes=[
            pltpu.VMEM((head_count, tok_rows, head_size), jnp.float32),
            pltpu.VMEM((head_count, tok_rows, head_size), jnp.float32),
            pltpu.VMEM((head_count, tok_rows, head_size), jnp.float32),
        ],
    )
    flops = 4 * block_count * tok_rows * tok_rows * head_size * head_count
    return pl.pallas_call(
        kernel,
        grid_spec=grid_spec,
        out_shape=jax.ShapeDtypeStruct(q_seq.shape, q_seq.dtype),
        compiler_params=pltpu.CompilerParams(dimension_semantics=("arbitrary",)),
        cost_estimate=pl.CostEstimate(
            flops=flops,
            transcendentals=block_count * tok_rows * tok_rows * head_count,
            bytes_accessed=(gathered.size + received.size) * 2 + q_seq.size * 4,
        ),
    )(meta, q_seq, query_seg, gathered, received)


def solution(mesh):
    in_specs = (
        P(("outer", "inner"), None),
        P(("outer", "inner"), None),
        P("outer", None),
        P("outer"),
        P(("outer", "inner")),
    )
    out_specs = P(("outer", "inner"), None)
    return jax.shard_map(local, mesh=mesh, in_specs=in_specs, out_specs=out_specs, check_vma=False)
```

```python
import math

import jax
import jax.numpy as jnp
from jax import lax
from jax.experimental import pallas as pl
from jax.experimental.pallas import tpu as pltpu
from jax.sharding import PartitionSpec as P


def shifted(value, axis, steps):
    count = lax.axis_size(axis)
    leading, last = (max(0, -steps), min(count, count - steps))
    return lax.ppermute(value, axis, [(source, source + steps) for source in range(leading, last)])


def select_rows(selector, blocks, pattern):
    return jnp.einsum(
        pattern, selector.astype(jnp.bfloat16), blocks, preferred_element_type=jnp.float32
    ).astype(jnp.bfloat16)


def local(q_load, kv_load, pack_dest, counts, segment_ids):
    group_width = lax.axis_size("inner")
    my_index = lax.axis_index("inner")
    capacity = pack_dest.shape[1]
    slot_count = capacity // 2
    pair_limit = -(-capacity // group_width)
    row_length = q_load.shape[0] // capacity
    query_width = q_load.shape[1]
    pair_width = kv_load.shape[1]
    head_size = pair_width // 2
    head_count = query_width // head_size
    slot_grid = lax.broadcasted_iota(jnp.int32, (group_width, capacity), 1)
    live_all = slot_grid < counts[:, None]
    owner_all = pack_dest // slot_count
    slot_numbers = jnp.arange(capacity, dtype=jnp.int32)
    earlier = slot_numbers[None, :] < slot_numbers[:, None]
    same_owner = owner_all[:, :, None] == owner_all[:, None, :]
    rank_all = jnp.sum(
        (earlier[None] & same_owner & live_all[:, None, :]).astype(jnp.int32), axis=2
    )
    shard_rows = jnp.arange(group_width, dtype=jnp.int32)
    mine_row = (shard_rows == my_index)[:, None]
    my_owner = jnp.sum(jnp.where(mine_row, owner_all, 0), axis=0)
    my_rank = jnp.sum(jnp.where(mine_row, rank_all, 0), axis=0)
    my_live = jnp.any(mine_row & live_all, axis=0)
    pair_ids = jnp.arange(pair_limit, dtype=jnp.int32)
    send_select = (
        my_live[None, None, :]
        & (my_owner[None, None, :] == shard_rows[:, None, None])
        & (my_rank[None, None, :] == pair_ids[None, :, None])
    )
    q_blocks = q_load.reshape(capacity, row_length, query_width)
    kv_blocks = kv_load.reshape(capacity, row_length, pair_width)
    send_q = select_rows(send_select, q_blocks, "jkc,crf->jkrf")
    send_kv = select_rows(send_select, kv_blocks, "jkc,crf->jkrf")
    recv_both = lax.all_to_all(
        jnp.concatenate([send_q, send_kv], axis=3), "inner", split_axis=0, concat_axis=0, tiled=True
    )
    recv_q = recv_both[..., :query_width]
    recv_kv = recv_both[..., query_width:]
    wanted = my_index * slot_count + jnp.arange(slot_count, dtype=jnp.int32)
    take_select = jnp.any(
        live_all[None, :, None, :]
        & (pack_dest[None, :, None, :] == wanted[:, None, None, None])
        & (rank_all[None, :, None, :] == pair_ids[None, None, :, None]),
        axis=3,
    )
    q_seq = select_rows(take_select, recv_q, "srk,rktf->stf").reshape(
        slot_count * row_length, query_width
    )
    kv_seq = select_rows(take_select, recv_kv, "srk,rktf->stf").reshape(
        slot_count * row_length, pair_width
    )
    tok_rows = q_seq.shape[0]
    owner_index = lax.axis_index(("outer", "inner"))
    outer_index = lax.axis_index("outer")
    score_scale = 1.0 / math.sqrt(head_size)
    extra_rows = 16
    seg_rows = tok_rows // pair_width
    seg_pad = jnp.zeros((extra_rows - seg_rows, pair_width), jnp.bfloat16)
    packed = jnp.concatenate(
        [kv_seq, segment_ids.astype(jnp.bfloat16).reshape(seg_rows, pair_width), seg_pad], axis=0
    )
    outer_reach = -(-(lax.axis_size("outer") * group_width // 4) // group_width)
    own_steps = list(range(0, outer_reach + 1, 2))
    partner_steps = list(range(1, outer_reach + 1, 2))
    moved = [packed if step == 0 else shifted(packed, "outer", step) for step in own_steps]
    own_stack = jnp.stack(moved)
    pair_mate = lax.ppermute(own_stack, "inner", [(i, i ^ 1) for i in range(group_width)])
    pair = jnp.stack([own_stack, pair_mate])
    pair_shifts = [pair] + [
        lax.ppermute(pair, "inner", [(i, (i + 2 * t) % group_width) for i in range(group_width)])
        for t in range(1, group_width // 2)
    ]
    gathered = jnp.concatenate(pair_shifts)
    entry = jnp.arange(group_width, dtype=jnp.int32)
    inner_of = ((my_index - 2 * (entry // 2)) % group_width) ^ (entry % 2)
    parity = outer_index % 2
    offer = lax.dynamic_slice_in_dim(gathered, parity, len(partner_steps), axis=1)
    outer_count = lax.axis_size("outer")
    partner_pairs = [(o, o ^ 1) for o in range(outer_count)]
    received = lax.ppermute(offer, "outer", partner_pairs)
    sources = [(gathered, own_steps), (received, partner_steps)]
    key_device, key_first, key_last = [], [], []
    for array, steps in sources:
        for slot, step in enumerate(steps):
            key_device.append(
                (outer_index - step) * group_width + inner_of
            )
            key_first.append(array[:, slot, tok_rows, 0])
            key_last.append(array[:, slot, tok_rows + seg_rows - 1, pair_width - 1])
    key_device = jnp.concatenate(key_device)
    key_first = jnp.concatenate(key_first)
    key_last = jnp.concatenate(key_last)
    first_seg = segment_ids[0].astype(jnp.bfloat16)
    last_seg = segment_ids[tok_rows - 1].astype(jnp.bfloat16)
    needed = (
        (key_device >= 0)
        & (key_device <= owner_index)
        & (key_last >= first_seg)
        & (key_first <= last_seg)
    )
    whole = (
        (key_device < owner_index)
        & (key_first == key_last)
        & (key_first == first_seg)
        & (first_seg == last_seg)
    )
    needed = jnp.where(needed, jnp.where(whole, 1, 2), 0).astype(jnp.int32)
    meta = jnp.concatenate([owner_index.reshape(1).astype(jnp.int32), needed, key_device])
    query_seg = segment_ids.astype(jnp.float32).reshape(tok_rows, 1)
    return attend(meta, q_seq, query_seg, gathered, received, head_count, head_size, score_scale)


def attend(meta, q_seq, query_seg, gathered, received, head_count, head_size, score_scale):
    tok_rows = q_seq.shape[0]
    group_width, first_slots, packed_rows, pair_width = gathered.shape
    second_slots = received.shape[1]
    first_count = group_width * first_slots
    block_count = first_count + group_width * second_slots
    seg_rows = tok_rows // pair_width

    def kernel(meta_ref, q_ref, qseg_ref, first_ref, second_ref, out_ref, m_ref, l_ref, acc_ref):
        b = pl.program_id(0)

        @pl.when(b == 0)
        def _():
            m_ref[...] = jnp.full(m_ref.shape, -1e30, jnp.float32)
            l_ref[...] = jnp.zeros(l_ref.shape, jnp.float32)
            acc_ref[...] = jnp.zeros(acc_ref.shape, jnp.float32)

        def absorb(kv_ref, masked_block):
            keys = kv_ref[0, 0, :tok_rows, :head_size]
            values = kv_ref[0, 0, :tok_rows, head_size:]
            if masked_block:
                own = meta_ref[0]
                device = meta_ref[1 + block_count + b]
                seg_parts = [
                    kv_ref[0, 0, tok_rows + r : tok_rows + r + 1, :].astype(jnp.float32)
                    for r in range(seg_rows)
                ]
                key_seg = jnp.concatenate(seg_parts, axis=1)
                key_pos = device * tok_rows + lax.broadcasted_iota(jnp.int32, (1, tok_rows), 1)
                query_pos = own * tok_rows + lax.broadcasted_iota(jnp.int32, (tok_rows, 1), 0)
                visible = (key_pos <= query_pos) & (key_seg == qseg_ref[...])
            for h in range(head_count):
                queries = q_ref[:, h * head_size : (h + 1) * head_size]
                scores = lax.dot_general(
                    queries, keys, (((1,), (1,)), ((), ())), preferred_element_type=jnp.float32
                )
                if masked_block:
                    scores = jnp.where(visible, scores, -1e30)
                m_prev = m_ref[h]
                m_next = jnp.maximum(m_prev, jnp.max(scores, axis=1, keepdims=True))
                factor = jnp.exp((m_prev - m_next) * score_scale)
                m_row = m_next[:, :1]
                if masked_block:
                    m_row = jnp.where(m_row == -1e30, 0.0, m_row)
                weights = jnp.exp((scores - m_row) * score_scale)
                l_ref[h] = l_ref[h] * factor + jnp.sum(weights, axis=1, keepdims=True)
                acc_ref[h] = acc_ref[h] * factor + jnp.dot(
                    weights.astype(jnp.bfloat16), values, preferred_element_type=jnp.float32
                )
                m_ref[h] = m_next

        mode = meta_ref[1 + b]
        for ref, in_range in ((first_ref, b < first_count), (second_ref, b >= first_count)):
            for masked_block, code in ((False, 1), (True, 2)):
                @pl.when(in_range & (mode == code))
                def _(ref=ref, masked_block=masked_block):
                    absorb(ref, masked_block)

        @pl.when(b == block_count - 1)
        def _():
            for h in range(head_count):
                out_ref[:, h * head_size : (h + 1) * head_size] = (
                    acc_ref[h] / l_ref[h]
                ).astype(out_ref.dtype)

    def first_map(b, meta):
        c = jnp.minimum(b, first_count - 1)
        return (c % group_width, c // group_width, 0, 0)

    def second_map(b, meta):
        c = jnp.maximum(b - first_count, 0)
        return (c % group_width, c // group_width, 0, 0)

    grid_spec = pltpu.PrefetchScalarGridSpec(
        num_scalar_prefetch=1,
        grid=(block_count,),
        in_specs=[
            pl.BlockSpec(q_seq.shape, lambda b, meta: (0, 0)),
            pl.BlockSpec(query_seg.shape, lambda b, meta: (0, 0)),
            pl.BlockSpec((1, 1, packed_rows, pair_width), first_map),
            pl.BlockSpec((1, 1, packed_rows, pair_width), second_map),
        ],
        out_specs=pl.BlockSpec(q_seq.shape, lambda b, meta: (0, 0)),
        scratch_shapes=[
            pltpu.VMEM((head_count, tok_rows, head_size), jnp.float32),
            pltpu.VMEM((head_count, tok_rows, head_size), jnp.float32),
            pltpu.VMEM((head_count, tok_rows, head_size), jnp.float32),
        ],
    )
    flops = 4 * block_count * tok_rows * tok_rows * head_size * head_count
    return pl.pallas_call(
        kernel,
        grid_spec=grid_spec,
        out_shape=jax.ShapeDtypeStruct(q_seq.shape, q_seq.dtype),
        compiler_params=pltpu.CompilerParams(dimension_semantics=("arbitrary",)),
        cost_estimate=pl.CostEstimate(
            flops=flops,
            transcendentals=block_count * tok_rows * tok_rows * head_count,
            bytes_accessed=(gathered.size + received.size) * 2 + q_seq.size * 4,
        ),
    )(meta, q_seq, query_seg, gathered, received)


def solution(mesh):
    in_specs = (
        P(("outer", "inner"), None),
        P(("outer", "inner"), None),
        P("outer", None),
        P("outer"),
        P(("outer", "inner")),
    )
    out_specs = P(("outer", "inner"), None)
    return jax.shard_map(local, mesh=mesh, in_specs=in_specs, out_specs=out_specs, check_vma=False)
```

```python
import math

import jax
import jax.numpy as jnp
from jax import lax
from jax.experimental import pallas as pl
from jax.experimental.pallas import tpu as pltpu
from jax.sharding import PartitionSpec as P


def shifted(value, axis, steps):
    count = lax.axis_size(axis)
    leading, last = (max(0, -steps), min(count, count - steps))
    return lax.ppermute(value, axis, [(source, source + steps) for source in range(leading, last)])


def select_rows(selector, blocks, pattern):
    return jnp.einsum(
        pattern, selector.astype(jnp.bfloat16), blocks, preferred_element_type=jnp.float32
    ).astype(jnp.bfloat16)


def local(q_load, kv_load, pack_dest, counts, segment_ids):
    group_width = lax.axis_size("inner")
    my_index = lax.axis_index("inner")
    capacity = pack_dest.shape[1]
    slot_count = capacity // 2
    pair_limit = -(-capacity // group_width)
    row_length = q_load.shape[0] // capacity
    query_width = q_load.shape[1]
    pair_width = kv_load.shape[1]
    head_size = pair_width // 2
    head_count = query_width // head_size
    slot_grid = lax.broadcasted_iota(jnp.int32, (group_width, capacity), 1)
    live_all = slot_grid < counts[:, None]
    owner_all = pack_dest // slot_count
    slot_numbers = jnp.arange(capacity, dtype=jnp.int32)
    earlier = slot_numbers[None, :] < slot_numbers[:, None]
    same_owner = owner_all[:, :, None] == owner_all[:, None, :]
    rank_all = jnp.sum(
        (earlier[None] & same_owner & live_all[:, None, :]).astype(jnp.int32), axis=2
    )
    shard_rows = jnp.arange(group_width, dtype=jnp.int32)
    mine_row = (shard_rows == my_index)[:, None]
    my_owner = jnp.sum(jnp.where(mine_row, owner_all, 0), axis=0)
    my_rank = jnp.sum(jnp.where(mine_row, rank_all, 0), axis=0)
    my_live = jnp.any(mine_row & live_all, axis=0)
    pair_ids = jnp.arange(pair_limit, dtype=jnp.int32)
    send_select = (
        my_live[None, None, :]
        & (my_owner[None, None, :] == shard_rows[:, None, None])
        & (my_rank[None, None, :] == pair_ids[None, :, None])
    )
    q_blocks = q_load.reshape(capacity, row_length, query_width)
    kv_blocks = kv_load.reshape(capacity, row_length, pair_width)
    send_q = select_rows(send_select, q_blocks, "jkc,crf->jkrf")
    send_kv = select_rows(send_select, kv_blocks, "jkc,crf->jkrf")
    recv_both = lax.all_to_all(
        jnp.concatenate([send_q, send_kv], axis=3), "inner", split_axis=0, concat_axis=0, tiled=True
    )
    recv_q = recv_both[..., :query_width]
    recv_kv = recv_both[..., query_width:]
    wanted = my_index * slot_count + jnp.arange(slot_count, dtype=jnp.int32)
    take_select = jnp.any(
        live_all[None, :, None, :]
        & (pack_dest[None, :, None, :] == wanted[:, None, None, None])
        & (rank_all[None, :, None, :] == pair_ids[None, None, :, None]),
        axis=3,
    )
    q_seq = select_rows(take_select, recv_q, "srk,rktf->stf").reshape(
        slot_count * row_length, query_width
    )
    kv_seq = select_rows(take_select, recv_kv, "srk,rktf->stf").reshape(
        slot_count * row_length, pair_width
    )
    tok_rows = q_seq.shape[0]
    owner_index = lax.axis_index(("outer", "inner"))
    outer_index = lax.axis_index("outer")
    score_scale = 1.0 / math.sqrt(head_size)
    extra_rows = 16
    seg_rows = tok_rows // pair_width
    seg_pad = jnp.zeros((extra_rows - seg_rows, pair_width), jnp.bfloat16)
    packed = jnp.concatenate(
        [kv_seq, segment_ids.astype(jnp.bfloat16).reshape(seg_rows, pair_width), seg_pad], axis=0
    )
    outer_reach = -(-(lax.axis_size("outer") * group_width // 4) // group_width)
    own_steps = list(range(0, outer_reach + 1, 2))
    partner_steps = list(range(1, outer_reach + 1, 2))
    moved = [packed if step == 0 else shifted(packed, "outer", step) for step in own_steps]
    own_stack = jnp.stack(moved)
    pair_mate = lax.ppermute(own_stack, "inner", [(i, i ^ 1) for i in range(group_width)])
    pair = jnp.stack([own_stack, pair_mate])
    def step_over(value, hops):
        return lax.ppermute(
            value, "inner", [(i, (i + 2 * hops) % group_width) for i in range(group_width)]
        )

    from_left = step_over(pair, 1)
    from_right = step_over(pair, -1)
    relayed = jnp.stack([step_over(from_left[0], 1), step_over(from_right[1], -1)])
    gathered = jnp.concatenate([pair, from_left, relayed, from_right])
    entry = jnp.arange(group_width, dtype=jnp.int32)
    inner_of = ((my_index - 2 * (entry // 2)) % group_width) ^ (entry % 2)
    parity = outer_index % 2
    offer = lax.dynamic_slice_in_dim(gathered, parity, len(partner_steps), axis=1)
    outer_count = lax.axis_size("outer")
    partner_pairs = [(o, o ^ 1) for o in range(outer_count)]
    received = lax.ppermute(offer, "outer", partner_pairs)
    sources = [(gathered, own_steps), (received, partner_steps)]
    key_device, key_first, key_last = [], [], []
    for array, steps in sources:
        for slot, step in enumerate(steps):
            key_device.append(
                (outer_index - step) * group_width + inner_of
            )
            key_first.append(array[:, slot, tok_rows, 0])
            key_last.append(array[:, slot, tok_rows + seg_rows - 1, pair_width - 1])
    key_device = jnp.concatenate(key_device)
    key_first = jnp.concatenate(key_first)
    key_last = jnp.concatenate(key_last)
    first_seg = segment_ids[0].astype(jnp.bfloat16)
    last_seg = segment_ids[tok_rows - 1].astype(jnp.bfloat16)
    needed = (
        (key_device >= 0)
        & (key_device <= owner_index)
        & (key_last >= first_seg)
        & (key_first <= last_seg)
    )
    whole = (
        (key_device < owner_index)
        & (key_first == key_last)
        & (key_first == first_seg)
        & (first_seg == last_seg)
    )
    needed = jnp.where(needed, jnp.where(whole, 1, 2), 0).astype(jnp.int32)
    meta = jnp.concatenate([owner_index.reshape(1).astype(jnp.int32), needed, key_device])
    query_seg = segment_ids.astype(jnp.float32).reshape(tok_rows, 1)
    return attend(meta, q_seq, query_seg, gathered, received, head_count, head_size, score_scale)


def attend(meta, q_seq, query_seg, gathered, received, head_count, head_size, score_scale):
    tok_rows = q_seq.shape[0]
    group_width, first_slots, packed_rows, pair_width = gathered.shape
    second_slots = received.shape[1]
    first_count = group_width * first_slots
    block_count = first_count + group_width * second_slots
    seg_rows = tok_rows // pair_width

    def kernel(meta_ref, q_ref, qseg_ref, first_ref, second_ref, out_ref, m_ref, l_ref, acc_ref):
        b = pl.program_id(0)

        @pl.when(b == 0)
        def _():
            m_ref[...] = jnp.full(m_ref.shape, -1e30, jnp.float32)
            l_ref[...] = jnp.zeros(l_ref.shape, jnp.float32)
            acc_ref[...] = jnp.zeros(acc_ref.shape, jnp.float32)

        def absorb(kv_ref, masked_block):
            keys = kv_ref[0, 0, :tok_rows, :head_size]
            values = kv_ref[0, 0, :tok_rows, head_size:]
            if masked_block:
                own = meta_ref[0]
                device = meta_ref[1 + block_count + b]
                seg_parts = [
                    kv_ref[0, 0, tok_rows + r : tok_rows + r + 1, :].astype(jnp.float32)
                    for r in range(seg_rows)
                ]
                key_seg = jnp.concatenate(seg_parts, axis=1)
                key_pos = device * tok_rows + lax.broadcasted_iota(jnp.int32, (1, tok_rows), 1)
                query_pos = own * tok_rows + lax.broadcasted_iota(jnp.int32, (tok_rows, 1), 0)
                visible = (key_pos <= query_pos) & (key_seg == qseg_ref[...])
            for h in range(head_count):
                queries = q_ref[:, h * head_size : (h + 1) * head_size]
                scores = lax.dot_general(
                    queries, keys, (((1,), (1,)), ((), ())), preferred_element_type=jnp.float32
                )
                if masked_block:
                    scores = jnp.where(visible, scores, -1e30)
                m_prev = m_ref[h]
                m_next = jnp.maximum(m_prev, jnp.max(scores, axis=1, keepdims=True))
                factor = jnp.exp((m_prev - m_next) * score_scale)
                m_row = m_next[:, :1]
                if masked_block:
                    m_row = jnp.where(m_row == -1e30, 0.0, m_row)
                weights = jnp.exp((scores - m_row) * score_scale)
                l_ref[h] = l_ref[h] * factor + jnp.sum(weights, axis=1, keepdims=True)
                acc_ref[h] = acc_ref[h] * factor + jnp.dot(
                    weights.astype(jnp.bfloat16), values, preferred_element_type=jnp.float32
                )
                m_ref[h] = m_next

        mode = meta_ref[1 + b]
        for ref, in_range in ((first_ref, b < first_count), (second_ref, b >= first_count)):
            for masked_block, code in ((False, 1), (True, 2)):
                @pl.when(in_range & (mode == code))
                def _(ref=ref, masked_block=masked_block):
                    absorb(ref, masked_block)

        @pl.when(b == block_count - 1)
        def _():
            for h in range(head_count):
                out_ref[:, h * head_size : (h + 1) * head_size] = (
                    acc_ref[h] / l_ref[h]
                ).astype(out_ref.dtype)

    def first_map(b, meta):
        c = jnp.minimum(b, first_count - 1)
        return (c % group_width, c // group_width, 0, 0)

    def second_map(b, meta):
        c = jnp.maximum(b - first_count, 0)
        return (c % group_width, c // group_width, 0, 0)

    grid_spec = pltpu.PrefetchScalarGridSpec(
        num_scalar_prefetch=1,
        grid=(block_count,),
        in_specs=[
            pl.BlockSpec(q_seq.shape, lambda b, meta: (0, 0)),
            pl.BlockSpec(query_seg.shape, lambda b, meta: (0, 0)),
            pl.BlockSpec((1, 1, packed_rows, pair_width), first_map),
            pl.BlockSpec((1, 1, packed_rows, pair_width), second_map),
        ],
        out_specs=pl.BlockSpec(q_seq.shape, lambda b, meta: (0, 0)),
        scratch_shapes=[
            pltpu.VMEM((head_count, tok_rows, head_size), jnp.float32),
            pltpu.VMEM((head_count, tok_rows, head_size), jnp.float32),
            pltpu.VMEM((head_count, tok_rows, head_size), jnp.float32),
        ],
    )
    flops = 4 * block_count * tok_rows * tok_rows * head_size * head_count
    return pl.pallas_call(
        kernel,
        grid_spec=grid_spec,
        out_shape=jax.ShapeDtypeStruct(q_seq.shape, q_seq.dtype),
        compiler_params=pltpu.CompilerParams(dimension_semantics=("arbitrary",)),
        cost_estimate=pl.CostEstimate(
            flops=flops,
            transcendentals=block_count * tok_rows * tok_rows * head_count,
            bytes_accessed=(gathered.size + received.size) * 2 + q_seq.size * 4,
        ),
    )(meta, q_seq, query_seg, gathered, received)


def solution(mesh):
    in_specs = (
        P(("outer", "inner"), None),
        P(("outer", "inner"), None),
        P("outer", None),
        P("outer"),
        P(("outer", "inner")),
    )
    out_specs = P(("outer", "inner"), None)
    return jax.shard_map(local, mesh=mesh, in_specs=in_specs, out_specs=out_specs, check_vma=False)
```

```python
import math

import jax
import jax.numpy as jnp
from jax import lax
from jax.experimental import pallas as pl
from jax.experimental.pallas import tpu as pltpu
from jax.sharding import PartitionSpec as P


def shifted(value, axis, steps):
    count = lax.axis_size(axis)
    leading, last = (max(0, -steps), min(count, count - steps))
    return lax.ppermute(value, axis, [(source, source + steps) for source in range(leading, last)])


def select_rows(selector, blocks, pattern):
    return jnp.einsum(
        pattern, selector.astype(jnp.bfloat16), blocks, preferred_element_type=jnp.float32
    ).astype(jnp.bfloat16)


def local(q_load, kv_load, pack_dest, counts, segment_ids):
    group_width = lax.axis_size("inner")
    my_index = lax.axis_index("inner")
    capacity = pack_dest.shape[1]
    slot_count = capacity // 2
    pair_limit = -(-capacity // group_width)
    row_length = q_load.shape[0] // capacity
    query_width = q_load.shape[1]
    pair_width = kv_load.shape[1]
    head_size = pair_width // 2
    head_count = query_width // head_size
    slot_grid = lax.broadcasted_iota(jnp.int32, (group_width, capacity), 1)
    live_all = slot_grid < counts[:, None]
    owner_all = pack_dest // slot_count
    slot_numbers = jnp.arange(capacity, dtype=jnp.int32)
    earlier = slot_numbers[None, :] < slot_numbers[:, None]
    same_owner = owner_all[:, :, None] == owner_all[:, None, :]
    rank_all = jnp.sum(
        (earlier[None] & same_owner & live_all[:, None, :]).astype(jnp.int32), axis=2
    )
    shard_rows = jnp.arange(group_width, dtype=jnp.int32)
    mine_row = (shard_rows == my_index)[:, None]
    my_owner = jnp.sum(jnp.where(mine_row, owner_all, 0), axis=0)
    my_rank = jnp.sum(jnp.where(mine_row, rank_all, 0), axis=0)
    my_live = jnp.any(mine_row & live_all, axis=0)
    pair_ids = jnp.arange(pair_limit, dtype=jnp.int32)
    send_select = (
        my_live[None, None, :]
        & (my_owner[None, None, :] == shard_rows[:, None, None])
        & (my_rank[None, None, :] == pair_ids[None, :, None])
    )
    q_blocks = q_load.reshape(capacity, row_length, query_width)
    kv_blocks = kv_load.reshape(capacity, row_length, pair_width)
    send_q = select_rows(send_select, q_blocks, "jkc,crf->jkrf")
    send_kv = select_rows(send_select, kv_blocks, "jkc,crf->jkrf")
    recv_kv = lax.all_to_all(send_kv, "inner", split_axis=0, concat_axis=0, tiled=True)
    wanted = my_index * slot_count + jnp.arange(slot_count, dtype=jnp.int32)
    take_select = jnp.any(
        live_all[None, :, None, :]
        & (pack_dest[None, :, None, :] == wanted[:, None, None, None])
        & (rank_all[None, :, None, :] == pair_ids[None, None, :, None]),
        axis=3,
    )
    kv_seq = select_rows(take_select, recv_kv, "srk,rktf->stf").reshape(
        slot_count * row_length, pair_width
    )
    tok_rows = slot_count * row_length
    owner_index = lax.axis_index(("outer", "inner"))
    outer_index = lax.axis_index("outer")
    score_scale = 1.0 / math.sqrt(head_size)
    extra_rows = 16
    seg_rows = tok_rows // pair_width
    seg_pad = jnp.zeros((extra_rows - seg_rows, pair_width), jnp.bfloat16)
    packed = jnp.concatenate(
        [kv_seq, segment_ids.astype(jnp.bfloat16).reshape(seg_rows, pair_width), seg_pad], axis=0
    )
    outer_reach = -(-(lax.axis_size("outer") * group_width // 4) // group_width)
    own_steps = list(range(0, outer_reach + 1, 2))
    partner_steps = list(range(1, outer_reach + 1, 2))
    moved = [packed if step == 0 else shifted(packed, "outer", step) for step in own_steps]
    own_stack = jnp.stack(moved)
    pair_mate = lax.ppermute(own_stack, "inner", [(i, i ^ 1) for i in range(group_width)])
    pair = jnp.stack([own_stack, pair_mate])
    send_q = lax.optimization_barrier((send_q, pair_mate))[0]
    recv_q = lax.all_to_all(send_q, "inner", split_axis=0, concat_axis=0, tiled=True)
    q_seq = select_rows(take_select, recv_q, "srk,rktf->stf").reshape(tok_rows, query_width)
    def step_over(value, hops):
        return lax.ppermute(
            value, "inner", [(i, (i + 2 * hops) % group_width) for i in range(group_width)]
        )

    from_left = step_over(pair, 1)
    from_right = step_over(pair, -1)
    relayed = jnp.stack([step_over(from_left[0], 1), step_over(from_right[1], -1)])
    gathered = jnp.concatenate([pair, from_left, relayed, from_right])
    entry = jnp.arange(group_width, dtype=jnp.int32)
    inner_of = ((my_index - 2 * (entry // 2)) % group_width) ^ (entry % 2)
    parity = outer_index % 2
    offer = lax.dynamic_slice_in_dim(gathered, parity, len(partner_steps), axis=1)
    outer_count = lax.axis_size("outer")
    partner_pairs = [(o, o ^ 1) for o in range(outer_count)]
    received = lax.ppermute(offer, "outer", partner_pairs)
    sources = [(gathered, own_steps), (received, partner_steps)]
    key_device, key_first, key_last = [], [], []
    for array, steps in sources:
        for slot, step in enumerate(steps):
            key_device.append(
                (outer_index - step) * group_width + inner_of
            )
            key_first.append(array[:, slot, tok_rows, 0])
            key_last.append(array[:, slot, tok_rows + seg_rows - 1, pair_width - 1])
    key_device = jnp.concatenate(key_device)
    key_first = jnp.concatenate(key_first)
    key_last = jnp.concatenate(key_last)
    first_seg = segment_ids[0].astype(jnp.bfloat16)
    last_seg = segment_ids[tok_rows - 1].astype(jnp.bfloat16)
    needed = (
        (key_device >= 0)
        & (key_device <= owner_index)
        & (key_last >= first_seg)
        & (key_first <= last_seg)
    )
    whole = (
        (key_device < owner_index)
        & (key_first == key_last)
        & (key_first == first_seg)
        & (first_seg == last_seg)
    )
    needed = jnp.where(needed, jnp.where(whole, 1, 2), 0).astype(jnp.int32)
    meta = jnp.concatenate([owner_index.reshape(1).astype(jnp.int32), needed, key_device])
    query_seg = segment_ids.astype(jnp.float32).reshape(tok_rows, 1)
    return attend(meta, q_seq, query_seg, gathered, received, head_count, head_size, score_scale)


def attend(meta, q_seq, query_seg, gathered, received, head_count, head_size, score_scale):
    tok_rows = q_seq.shape[0]
    group_width, first_slots, packed_rows, pair_width = gathered.shape
    second_slots = received.shape[1]
    first_count = group_width * first_slots
    block_count = first_count + group_width * second_slots
    seg_rows = tok_rows // pair_width

    def kernel(meta_ref, q_ref, qseg_ref, first_ref, second_ref, out_ref, m_ref, l_ref, acc_ref):
        b = pl.program_id(0)

        @pl.when(b == 0)
        def _():
            m_ref[...] = jnp.full(m_ref.shape, -1e30, jnp.float32)
            l_ref[...] = jnp.zeros(l_ref.shape, jnp.float32)
            acc_ref[...] = jnp.zeros(acc_ref.shape, jnp.float32)

        def absorb(kv_ref, masked_block):
            keys = kv_ref[0, 0, :tok_rows, :head_size]
            values = kv_ref[0, 0, :tok_rows, head_size:]
            if masked_block:
                own = meta_ref[0]
                device = meta_ref[1 + block_count + b]
                seg_parts = [
                    kv_ref[0, 0, tok_rows + r : tok_rows + r + 1, :].astype(jnp.float32)
                    for r in range(seg_rows)
                ]
                key_seg = jnp.concatenate(seg_parts, axis=1)
                key_pos = device * tok_rows + lax.broadcasted_iota(jnp.int32, (1, tok_rows), 1)
                query_pos = own * tok_rows + lax.broadcasted_iota(jnp.int32, (tok_rows, 1), 0)
                visible = (key_pos <= query_pos) & (key_seg == qseg_ref[...])
            for h in range(head_count):
                queries = q_ref[:, h * head_size : (h + 1) * head_size]
                scores = lax.dot_general(
                    queries, keys, (((1,), (1,)), ((), ())), preferred_element_type=jnp.float32
                )
                if masked_block:
                    scores = jnp.where(visible, scores, -1e30)
                m_prev = m_ref[h]
                m_next = jnp.maximum(m_prev, jnp.max(scores, axis=1, keepdims=True))
                factor = jnp.exp((m_prev - m_next) * score_scale)
                m_row = m_next[:, :1]
                if masked_block:
                    m_row = jnp.where(m_row == -1e30, 0.0, m_row)
                weights = jnp.exp((scores - m_row) * score_scale)
                l_ref[h] = l_ref[h] * factor + jnp.sum(weights, axis=1, keepdims=True)
                acc_ref[h] = acc_ref[h] * factor + jnp.dot(
                    weights.astype(jnp.bfloat16), values, preferred_element_type=jnp.float32
                )
                m_ref[h] = m_next

        mode = meta_ref[1 + b]
        for ref, in_range in ((first_ref, b < first_count), (second_ref, b >= first_count)):
            for masked_block, code in ((False, 1), (True, 2)):
                @pl.when(in_range & (mode == code))
                def _(ref=ref, masked_block=masked_block):
                    absorb(ref, masked_block)

        @pl.when(b == block_count - 1)
        def _():
            for h in range(head_count):
                out_ref[:, h * head_size : (h + 1) * head_size] = (
                    acc_ref[h] / l_ref[h]
                ).astype(out_ref.dtype)

    def first_map(b, meta):
        c = jnp.minimum(b, first_count - 1)
        return (c % group_width, c // group_width, 0, 0)

    def second_map(b, meta):
        c = jnp.maximum(b - first_count, 0)
        return (c % group_width, c // group_width, 0, 0)

    grid_spec = pltpu.PrefetchScalarGridSpec(
        num_scalar_prefetch=1,
        grid=(block_count,),
        in_specs=[
            pl.BlockSpec(q_seq.shape, lambda b, meta: (0, 0)),
            pl.BlockSpec(query_seg.shape, lambda b, meta: (0, 0)),
            pl.BlockSpec((1, 1, packed_rows, pair_width), first_map),
            pl.BlockSpec((1, 1, packed_rows, pair_width), second_map),
        ],
        out_specs=pl.BlockSpec(q_seq.shape, lambda b, meta: (0, 0)),
        scratch_shapes=[
            pltpu.VMEM((head_count, tok_rows, head_size), jnp.float32),
            pltpu.VMEM((head_count, tok_rows, head_size), jnp.float32),
            pltpu.VMEM((head_count, tok_rows, head_size), jnp.float32),
        ],
    )
    flops = 4 * block_count * tok_rows * tok_rows * head_size * head_count
    return pl.pallas_call(
        kernel,
        grid_spec=grid_spec,
        out_shape=jax.ShapeDtypeStruct(q_seq.shape, q_seq.dtype),
        compiler_params=pltpu.CompilerParams(dimension_semantics=("arbitrary",)),
        cost_estimate=pl.CostEstimate(
            flops=flops,
            transcendentals=block_count * tok_rows * tok_rows * head_count,
            bytes_accessed=(gathered.size + received.size) * 2 + q_seq.size * 4,
        ),
    )(meta, q_seq, query_seg, gathered, received)


def solution(mesh):
    in_specs = (
        P(("outer", "inner"), None),
        P(("outer", "inner"), None),
        P("outer", None),
        P("outer"),
        P(("outer", "inner")),
    )
    out_specs = P(("outer", "inner"), None)
    return jax.shard_map(local, mesh=mesh, in_specs=in_specs, out_specs=out_specs, check_vma=False)
```

```python
import math

import jax
import jax.numpy as jnp
from jax import lax
from jax.experimental import pallas as pl
from jax.experimental.pallas import tpu as pltpu
from jax.sharding import PartitionSpec as P


def shifted(value, axis, steps):
    count = lax.axis_size(axis)
    leading, last = (max(0, -steps), min(count, count - steps))
    return lax.ppermute(value, axis, [(source, source + steps) for source in range(leading, last)])


def select_rows(selector, blocks, pattern):
    return jnp.einsum(
        pattern, selector.astype(jnp.bfloat16), blocks, preferred_element_type=jnp.float32
    ).astype(jnp.bfloat16)


def local(q_load, kv_load, pack_dest, counts, segment_ids):
    group_width = lax.axis_size("inner")
    my_index = lax.axis_index("inner")
    capacity = pack_dest.shape[1]
    slot_count = capacity // 2
    pair_limit = -(-capacity // group_width)
    row_length = q_load.shape[0] // capacity
    query_width = q_load.shape[1]
    pair_width = kv_load.shape[1]
    head_size = pair_width // 2
    head_count = query_width // head_size
    slot_grid = lax.broadcasted_iota(jnp.int32, (group_width, capacity), 1)
    live_all = slot_grid < counts[:, None]
    owner_all = pack_dest // slot_count
    slot_numbers = jnp.arange(capacity, dtype=jnp.int32)
    earlier = slot_numbers[None, :] < slot_numbers[:, None]
    same_owner = owner_all[:, :, None] == owner_all[:, None, :]
    rank_all = jnp.sum(
        (earlier[None] & same_owner & live_all[:, None, :]).astype(jnp.int32), axis=2
    )
    shard_rows = jnp.arange(group_width, dtype=jnp.int32)
    mine_row = (shard_rows == my_index)[:, None]
    my_owner = jnp.sum(jnp.where(mine_row, owner_all, 0), axis=0)
    my_rank = jnp.sum(jnp.where(mine_row, rank_all, 0), axis=0)
    my_live = jnp.any(mine_row & live_all, axis=0)
    pair_ids = jnp.arange(pair_limit, dtype=jnp.int32)
    send_select = (
        my_live[None, None, :]
        & (my_owner[None, None, :] == shard_rows[:, None, None])
        & (my_rank[None, None, :] == pair_ids[None, :, None])
    )
    q_blocks = q_load.reshape(capacity, row_length, query_width)
    kv_blocks = kv_load.reshape(capacity, row_length, pair_width)
    send_q = select_rows(send_select, q_blocks, "jkc,crf->jkrf")
    send_kv = select_rows(send_select, kv_blocks, "jkc,crf->jkrf")
    recv_kv = lax.all_to_all(send_kv, "inner", split_axis=0, concat_axis=0, tiled=True)
    wanted = my_index * slot_count + jnp.arange(slot_count, dtype=jnp.int32)
    take_select = jnp.any(
        live_all[None, :, None, :]
        & (pack_dest[None, :, None, :] == wanted[:, None, None, None])
        & (rank_all[None, :, None, :] == pair_ids[None, None, :, None]),
        axis=3,
    )
    kv_seq = select_rows(take_select, recv_kv, "srk,rktf->stf").reshape(
        slot_count * row_length, pair_width
    )
    tok_rows = slot_count * row_length
    owner_index = lax.axis_index(("outer", "inner"))
    outer_index = lax.axis_index("outer")
    score_scale = 1.0 / math.sqrt(head_size)
    extra_rows = 16
    seg_rows = tok_rows // pair_width
    seg_pad = jnp.zeros((extra_rows - seg_rows, pair_width), jnp.bfloat16)
    packed = jnp.concatenate(
        [kv_seq, segment_ids.astype(jnp.bfloat16).reshape(seg_rows, pair_width), seg_pad], axis=0
    )
    outer_reach = -(-(lax.axis_size("outer") * group_width // 4) // group_width)
    own_steps = list(range(0, outer_reach + 1, 2))
    partner_steps = list(range(1, outer_reach + 1, 2))
    moved = [packed if step == 0 else shifted(packed, "outer", step) for step in own_steps]
    own_stack = jnp.stack(moved)
    outer_total = lax.axis_size("outer")
    mate_moved = []
    for step in own_steps:
        mate_pairs = [
            (o * group_width + i, (o + step) * group_width + (i ^ 1))
            for o in range(outer_total - step)
            for i in range(group_width)
        ]
        mate_moved.append(lax.ppermute(packed, ("outer", "inner"), mate_pairs))
    pair_mate = jnp.stack(mate_moved)
    pair = jnp.stack([own_stack, pair_mate])
    send_q = lax.optimization_barrier((send_q, pair_mate))[0]
    recv_q = lax.all_to_all(send_q, "inner", split_axis=0, concat_axis=0, tiled=True)
    q_seq = select_rows(take_select, recv_q, "srk,rktf->stf").reshape(tok_rows, query_width)
    def step_over(value, hops):
        return lax.ppermute(
            value, "inner", [(i, (i + 2 * hops) % group_width) for i in range(group_width)]
        )

    from_left = step_over(pair, 1)
    from_right = step_over(pair, -1)
    relayed = jnp.stack([step_over(from_left[0], 1), step_over(from_right[1], -1)])
    gathered = jnp.concatenate([pair, from_left, relayed, from_right])
    entry = jnp.arange(group_width, dtype=jnp.int32)
    inner_of = ((my_index - 2 * (entry // 2)) % group_width) ^ (entry % 2)
    parity = outer_index % 2
    offer = lax.dynamic_slice_in_dim(gathered, parity, len(partner_steps), axis=1)
    outer_count = lax.axis_size("outer")
    partner_pairs = [(o, o ^ 1) for o in range(outer_count)]
    received = lax.ppermute(offer, "outer", partner_pairs)
    sources = [(gathered, own_steps), (received, partner_steps)]
    key_device, key_first, key_last = [], [], []
    for array, steps in sources:
        for slot, step in enumerate(steps):
            key_device.append(
                (outer_index - step) * group_width + inner_of
            )
            key_first.append(array[:, slot, tok_rows, 0])
            key_last.append(array[:, slot, tok_rows + seg_rows - 1, pair_width - 1])
    key_device = jnp.concatenate(key_device)
    key_first = jnp.concatenate(key_first)
    key_last = jnp.concatenate(key_last)
    first_seg = segment_ids[0].astype(jnp.bfloat16)
    last_seg = segment_ids[tok_rows - 1].astype(jnp.bfloat16)
    needed = (
        (key_device >= 0)
        & (key_device <= owner_index)
        & (key_last >= first_seg)
        & (key_first <= last_seg)
    )
    whole = (
        (key_device < owner_index)
        & (key_first == key_last)
        & (key_first == first_seg)
        & (first_seg == last_seg)
    )
    needed = jnp.where(needed, jnp.where(whole, 1, 2), 0).astype(jnp.int32)
    meta = jnp.concatenate([owner_index.reshape(1).astype(jnp.int32), needed, key_device])
    query_seg = segment_ids.astype(jnp.float32).reshape(tok_rows, 1)
    return attend(meta, q_seq, query_seg, gathered, received, head_count, head_size, score_scale)


def attend(meta, q_seq, query_seg, gathered, received, head_count, head_size, score_scale):
    tok_rows = q_seq.shape[0]
    group_width, first_slots, packed_rows, pair_width = gathered.shape
    second_slots = received.shape[1]
    first_count = group_width * first_slots
    block_count = first_count + group_width * second_slots
    seg_rows = tok_rows // pair_width

    def kernel(meta_ref, q_ref, qseg_ref, first_ref, second_ref, out_ref, m_ref, l_ref, acc_ref):
        b = pl.program_id(0)

        @pl.when(b == 0)
        def _():
            m_ref[...] = jnp.full(m_ref.shape, -1e30, jnp.float32)
            l_ref[...] = jnp.zeros(l_ref.shape, jnp.float32)
            acc_ref[...] = jnp.zeros(acc_ref.shape, jnp.float32)

        def absorb(kv_ref, masked_block):
            keys = kv_ref[0, 0, :tok_rows, :head_size]
            values = kv_ref[0, 0, :tok_rows, head_size:]
            if masked_block:
                own = meta_ref[0]
                device = meta_ref[1 + block_count + b]
                seg_parts = [
                    kv_ref[0, 0, tok_rows + r : tok_rows + r + 1, :].astype(jnp.float32)
                    for r in range(seg_rows)
                ]
                key_seg = jnp.concatenate(seg_parts, axis=1)
                key_pos = device * tok_rows + lax.broadcasted_iota(jnp.int32, (1, tok_rows), 1)
                query_pos = own * tok_rows + lax.broadcasted_iota(jnp.int32, (tok_rows, 1), 0)
                visible = (key_pos <= query_pos) & (key_seg == qseg_ref[...])
            for h in range(head_count):
                queries = q_ref[:, h * head_size : (h + 1) * head_size]
                scores = lax.dot_general(
                    queries, keys, (((1,), (1,)), ((), ())), preferred_element_type=jnp.float32
                )
                if masked_block:
                    scores = jnp.where(visible, scores, -1e30)
                m_prev = m_ref[h]
                m_next = jnp.maximum(m_prev, jnp.max(scores, axis=1, keepdims=True))
                factor = jnp.exp((m_prev - m_next) * score_scale)
                m_row = m_next[:, :1]
                if masked_block:
                    m_row = jnp.where(m_row == -1e30, 0.0, m_row)
                weights = jnp.exp((scores - m_row) * score_scale)
                l_ref[h] = l_ref[h] * factor + jnp.sum(weights, axis=1, keepdims=True)
                acc_ref[h] = acc_ref[h] * factor + jnp.dot(
                    weights.astype(jnp.bfloat16), values, preferred_element_type=jnp.float32
                )
                m_ref[h] = m_next

        mode = meta_ref[1 + b]
        for ref, in_range in ((first_ref, b < first_count), (second_ref, b >= first_count)):
            for masked_block, code in ((False, 1), (True, 2)):
                @pl.when(in_range & (mode == code))
                def _(ref=ref, masked_block=masked_block):
                    absorb(ref, masked_block)

        @pl.when(b == block_count - 1)
        def _():
            for h in range(head_count):
                out_ref[:, h * head_size : (h + 1) * head_size] = (
                    acc_ref[h] / l_ref[h]
                ).astype(out_ref.dtype)

    def first_map(b, meta):
        c = jnp.minimum(b, first_count - 1)
        return (c % group_width, c // group_width, 0, 0)

    def second_map(b, meta):
        c = jnp.maximum(b - first_count, 0)
        return (c % group_width, c // group_width, 0, 0)

    grid_spec = pltpu.PrefetchScalarGridSpec(
        num_scalar_prefetch=1,
        grid=(block_count,),
        in_specs=[
            pl.BlockSpec(q_seq.shape, lambda b, meta: (0, 0)),
            pl.BlockSpec(query_seg.shape, lambda b, meta: (0, 0)),
            pl.BlockSpec((1, 1, packed_rows, pair_width), first_map),
            pl.BlockSpec((1, 1, packed_rows, pair_width), second_map),
        ],
        out_specs=pl.BlockSpec(q_seq.shape, lambda b, meta: (0, 0)),
        scratch_shapes=[
            pltpu.VMEM((head_count, tok_rows, head_size), jnp.float32),
            pltpu.VMEM((head_count, tok_rows, head_size), jnp.float32),
            pltpu.VMEM((head_count, tok_rows, head_size), jnp.float32),
        ],
    )
    flops = 4 * block_count * tok_rows * tok_rows * head_size * head_count
    return pl.pallas_call(
        kernel,
        grid_spec=grid_spec,
        out_shape=jax.ShapeDtypeStruct(q_seq.shape, q_seq.dtype),
        compiler_params=pltpu.CompilerParams(dimension_semantics=("arbitrary",)),
        cost_estimate=pl.CostEstimate(
            flops=flops,
            transcendentals=block_count * tok_rows * tok_rows * head_count,
            bytes_accessed=(gathered.size + received.size) * 2 + q_seq.size * 4,
        ),
    )(meta, q_seq, query_seg, gathered, received)


def solution(mesh):
    in_specs = (
        P(("outer", "inner"), None),
        P(("outer", "inner"), None),
        P("outer", None),
        P("outer"),
        P(("outer", "inner")),
    )
    out_specs = P(("outer", "inner"), None)
    return jax.shard_map(local, mesh=mesh, in_specs=in_specs, out_specs=out_specs, check_vma=False)
```

```python
import math

import jax
import jax.numpy as jnp
from jax import lax
from jax.experimental import pallas as pl
from jax.experimental.pallas import tpu as pltpu
from jax.sharding import PartitionSpec as P


def shifted(value, axis, steps):
    count = lax.axis_size(axis)
    leading, last = (max(0, -steps), min(count, count - steps))
    return lax.ppermute(value, axis, [(source, source + steps) for source in range(leading, last)])


def select_rows(selector, blocks, pattern):
    return jnp.einsum(
        pattern, selector.astype(jnp.bfloat16), blocks, preferred_element_type=jnp.float32
    ).astype(jnp.bfloat16)


def local(q_load, kv_load, pack_dest, counts, segment_ids):
    group_width = lax.axis_size("inner")
    my_index = lax.axis_index("inner")
    capacity = pack_dest.shape[1]
    slot_count = capacity // 2
    pair_limit = -(-capacity // group_width)
    row_length = q_load.shape[0] // capacity
    query_width = q_load.shape[1]
    pair_width = kv_load.shape[1]
    head_size = pair_width // 2
    head_count = query_width // head_size
    slot_grid = lax.broadcasted_iota(jnp.int32, (group_width, capacity), 1)
    live_all = slot_grid < counts[:, None]
    owner_all = pack_dest // slot_count
    slot_numbers = jnp.arange(capacity, dtype=jnp.int32)
    earlier = slot_numbers[None, :] < slot_numbers[:, None]
    same_owner = owner_all[:, :, None] == owner_all[:, None, :]
    rank_all = jnp.sum(
        (earlier[None] & same_owner & live_all[:, None, :]).astype(jnp.int32), axis=2
    )
    shard_rows = jnp.arange(group_width, dtype=jnp.int32)
    mine_row = (shard_rows == my_index)[:, None]
    my_owner = jnp.sum(jnp.where(mine_row, owner_all, 0), axis=0)
    my_rank = jnp.sum(jnp.where(mine_row, rank_all, 0), axis=0)
    my_live = jnp.any(mine_row & live_all, axis=0)
    pair_ids = jnp.arange(pair_limit, dtype=jnp.int32)
    send_select = (
        my_live[None, None, :]
        & (my_owner[None, None, :] == shard_rows[:, None, None])
        & (my_rank[None, None, :] == pair_ids[None, :, None])
    )
    q_blocks = q_load.reshape(capacity, row_length, query_width)
    kv_blocks = kv_load.reshape(capacity, row_length, pair_width)
    send_q = select_rows(send_select, q_blocks, "jkc,crf->jkrf")
    send_kv = select_rows(send_select, kv_blocks, "jkc,crf->jkrf")
    recv_kv = lax.all_to_all(send_kv, "inner", split_axis=0, concat_axis=0, tiled=True)
    wanted = my_index * slot_count + jnp.arange(slot_count, dtype=jnp.int32)
    take_select = jnp.any(
        live_all[None, :, None, :]
        & (pack_dest[None, :, None, :] == wanted[:, None, None, None])
        & (rank_all[None, :, None, :] == pair_ids[None, None, :, None]),
        axis=3,
    )
    kv_seq = select_rows(take_select, recv_kv, "srk,rktf->stf").reshape(
        slot_count * row_length, pair_width
    )
    tok_rows = slot_count * row_length
    owner_index = lax.axis_index(("outer", "inner"))
    outer_index = lax.axis_index("outer")
    score_scale = 1.0 / math.sqrt(head_size)
    extra_rows = 16
    seg_rows = tok_rows // pair_width
    seg_pad = jnp.zeros((extra_rows - seg_rows, pair_width), jnp.bfloat16)
    packed = jnp.concatenate(
        [kv_seq, segment_ids.astype(jnp.bfloat16).reshape(seg_rows, pair_width), seg_pad], axis=0
    )
    outer_reach = -(-(lax.axis_size("outer") * group_width // 4) // group_width)
    own_steps = list(range(0, outer_reach + 1, 2))
    partner_steps = list(range(1, outer_reach + 1, 2))
    moved = [packed if step == 0 else shifted(packed, "outer", step) for step in own_steps]
    own_stack = jnp.stack(moved)
    pair_mate = lax.ppermute(own_stack, "inner", [(i, i ^ 1) for i in range(group_width)])
    pair = jnp.stack([own_stack, pair_mate])
    send_q = lax.optimization_barrier((send_q, pair_mate))[0]
    recv_q = lax.all_to_all(send_q, "inner", split_axis=0, concat_axis=0, tiled=True)
    def step_over(value, hops):
        return lax.ppermute(
            value, "inner", [(i, (i + 2 * hops) % group_width) for i in range(group_width)]
        )

    from_left = step_over(pair, 1)
    from_right = step_over(pair, -1)
    left_half, right_half, recv_q = lax.optimization_barrier((from_left[0], from_right[1], recv_q))
    relayed = jnp.stack([step_over(left_half, 1), step_over(right_half, -1)])
    gathered = jnp.concatenate([pair, from_left, relayed, from_right])
    q_seq = select_rows(take_select, recv_q, "srk,rktf->stf").reshape(tok_rows, query_width)
    entry = jnp.arange(group_width, dtype=jnp.int32)
    inner_of = ((my_index - 2 * (entry // 2)) % group_width) ^ (entry % 2)
    parity = outer_index % 2
    offer = lax.dynamic_slice_in_dim(gathered, parity, len(partner_steps), axis=1)
    outer_count = lax.axis_size("outer")
    partner_pairs = [(o, o ^ 1) for o in range(outer_count)]
    received = lax.ppermute(offer, "outer", partner_pairs)
    sources = [(gathered, own_steps), (received, partner_steps)]
    key_device, key_first, key_last = [], [], []
    for array, steps in sources:
        for slot, step in enumerate(steps):
            key_device.append(
                (outer_index - step) * group_width + inner_of
            )
            key_first.append(array[:, slot, tok_rows, 0])
            key_last.append(array[:, slot, tok_rows + seg_rows - 1, pair_width - 1])
    key_device = jnp.concatenate(key_device)
    key_first = jnp.concatenate(key_first)
    key_last = jnp.concatenate(key_last)
    first_seg = segment_ids[0].astype(jnp.bfloat16)
    last_seg = segment_ids[tok_rows - 1].astype(jnp.bfloat16)
    needed = (
        (key_device >= 0)
        & (key_device <= owner_index)
        & (key_last >= first_seg)
        & (key_first <= last_seg)
    )
    whole = (
        (key_device < owner_index)
        & (key_first == key_last)
        & (key_first == first_seg)
        & (first_seg == last_seg)
    )
    needed = jnp.where(needed, jnp.where(whole, 1, 2), 0).astype(jnp.int32)
    meta = jnp.concatenate([owner_index.reshape(1).astype(jnp.int32), needed, key_device])
    query_seg = segment_ids.astype(jnp.float32).reshape(tok_rows, 1)
    return attend(meta, q_seq, query_seg, gathered, received, head_count, head_size, score_scale)


def attend(meta, q_seq, query_seg, gathered, received, head_count, head_size, score_scale):
    tok_rows = q_seq.shape[0]
    group_width, first_slots, packed_rows, pair_width = gathered.shape
    second_slots = received.shape[1]
    first_count = group_width * first_slots
    block_count = first_count + group_width * second_slots
    seg_rows = tok_rows // pair_width

    def kernel(meta_ref, q_ref, qseg_ref, first_ref, second_ref, out_ref, m_ref, l_ref, acc_ref):
        b = pl.program_id(0)

        @pl.when(b == 0)
        def _():
            m_ref[...] = jnp.full(m_ref.shape, -1e30, jnp.float32)
            l_ref[...] = jnp.zeros(l_ref.shape, jnp.float32)
            acc_ref[...] = jnp.zeros(acc_ref.shape, jnp.float32)

        def absorb(kv_ref, masked_block):
            keys = kv_ref[0, 0, :tok_rows, :head_size]
            values = kv_ref[0, 0, :tok_rows, head_size:]
            if masked_block:
                own = meta_ref[0]
                device = meta_ref[1 + block_count + b]
                seg_parts = [
                    kv_ref[0, 0, tok_rows + r : tok_rows + r + 1, :].astype(jnp.float32)
                    for r in range(seg_rows)
                ]
                key_seg = jnp.concatenate(seg_parts, axis=1)
                key_pos = device * tok_rows + lax.broadcasted_iota(jnp.int32, (1, tok_rows), 1)
                query_pos = own * tok_rows + lax.broadcasted_iota(jnp.int32, (tok_rows, 1), 0)
                visible = (key_pos <= query_pos) & (key_seg == qseg_ref[...])
            for h in range(head_count):
                queries = q_ref[:, h * head_size : (h + 1) * head_size]
                scores = lax.dot_general(
                    queries, keys, (((1,), (1,)), ((), ())), preferred_element_type=jnp.float32
                )
                if masked_block:
                    scores = jnp.where(visible, scores, -1e30)
                m_prev = m_ref[h]
                m_next = jnp.maximum(m_prev, jnp.max(scores, axis=1, keepdims=True))
                factor = jnp.exp((m_prev - m_next) * score_scale)
                m_row = m_next[:, :1]
                if masked_block:
                    m_row = jnp.where(m_row == -1e30, 0.0, m_row)
                weights = jnp.exp((scores - m_row) * score_scale)
                l_ref[h] = l_ref[h] * factor + jnp.sum(weights, axis=1, keepdims=True)
                acc_ref[h] = acc_ref[h] * factor + jnp.dot(
                    weights.astype(jnp.bfloat16), values, preferred_element_type=jnp.float32
                )
                m_ref[h] = m_next

        mode = meta_ref[1 + b]
        for ref, in_range in ((first_ref, b < first_count), (second_ref, b >= first_count)):
            for masked_block, code in ((False, 1), (True, 2)):
                @pl.when(in_range & (mode == code))
                def _(ref=ref, masked_block=masked_block):
                    absorb(ref, masked_block)

        @pl.when(b == block_count - 1)
        def _():
            for h in range(head_count):
                out_ref[:, h * head_size : (h + 1) * head_size] = (
                    acc_ref[h] / l_ref[h]
                ).astype(out_ref.dtype)

    def first_map(b, meta):
        c = jnp.minimum(b, first_count - 1)
        return (c % group_width, c // group_width, 0, 0)

    def second_map(b, meta):
        c = jnp.maximum(b - first_count, 0)
        return (c % group_width, c // group_width, 0, 0)

    grid_spec = pltpu.PrefetchScalarGridSpec(
        num_scalar_prefetch=1,
        grid=(block_count,),
        in_specs=[
            pl.BlockSpec(q_seq.shape, lambda b, meta: (0, 0)),
            pl.BlockSpec(query_seg.shape, lambda b, meta: (0, 0)),
            pl.BlockSpec((1, 1, packed_rows, pair_width), first_map),
            pl.BlockSpec((1, 1, packed_rows, pair_width), second_map),
        ],
        out_specs=pl.BlockSpec(q_seq.shape, lambda b, meta: (0, 0)),
        scratch_shapes=[
            pltpu.VMEM((head_count, tok_rows, head_size), jnp.float32),
            pltpu.VMEM((head_count, tok_rows, head_size), jnp.float32),
            pltpu.VMEM((head_count, tok_rows, head_size), jnp.float32),
        ],
    )
    flops = 4 * block_count * tok_rows * tok_rows * head_size * head_count
    return pl.pallas_call(
        kernel,
        grid_spec=grid_spec,
        out_shape=jax.ShapeDtypeStruct(q_seq.shape, q_seq.dtype),
        compiler_params=pltpu.CompilerParams(dimension_semantics=("arbitrary",)),
        cost_estimate=pl.CostEstimate(
            flops=flops,
            transcendentals=block_count * tok_rows * tok_rows * head_count,
            bytes_accessed=(gathered.size + received.size) * 2 + q_seq.size * 4,
        ),
    )(meta, q_seq, query_seg, gathered, received)


def solution(mesh):
    in_specs = (
        P(("outer", "inner"), None),
        P(("outer", "inner"), None),
        P("outer", None),
        P("outer"),
        P(("outer", "inner")),
    )
    out_specs = P(("outer", "inner"), None)
    return jax.shard_map(local, mesh=mesh, in_specs=in_specs, out_specs=out_specs, check_vma=False)
```

```python
import math

import jax
import jax.numpy as jnp
from jax import lax
from jax.experimental import pallas as pl
from jax.experimental.pallas import tpu as pltpu
from jax.sharding import PartitionSpec as P


def shifted(value, axis, steps):
    count = lax.axis_size(axis)
    leading, last = (max(0, -steps), min(count, count - steps))
    return lax.ppermute(value, axis, [(source, source + steps) for source in range(leading, last)])


def select_rows(selector, blocks, pattern):
    return jnp.einsum(
        pattern, selector.astype(jnp.bfloat16), blocks, preferred_element_type=jnp.float32
    ).astype(jnp.bfloat16)


def local(q_load, kv_load, pack_dest, counts, segment_ids):
    group_width = lax.axis_size("inner")
    my_index = lax.axis_index("inner")
    capacity = pack_dest.shape[1]
    slot_count = capacity // 2
    pair_limit = -(-capacity // group_width)
    row_length = q_load.shape[0] // capacity
    query_width = q_load.shape[1]
    pair_width = kv_load.shape[1]
    head_size = pair_width // 2
    head_count = query_width // head_size
    slot_grid = lax.broadcasted_iota(jnp.int32, (group_width, capacity), 1)
    live_all = slot_grid < counts[:, None]
    owner_all = pack_dest // slot_count
    slot_numbers = jnp.arange(capacity, dtype=jnp.int32)
    earlier = slot_numbers[None, :] < slot_numbers[:, None]
    same_owner = owner_all[:, :, None] == owner_all[:, None, :]
    rank_all = jnp.sum(
        (earlier[None] & same_owner & live_all[:, None, :]).astype(jnp.int32), axis=2
    )
    shard_rows = jnp.arange(group_width, dtype=jnp.int32)
    mine_row = (shard_rows == my_index)[:, None]
    my_owner = jnp.sum(jnp.where(mine_row, owner_all, 0), axis=0)
    my_rank = jnp.sum(jnp.where(mine_row, rank_all, 0), axis=0)
    my_live = jnp.any(mine_row & live_all, axis=0)
    pair_ids = jnp.arange(pair_limit, dtype=jnp.int32)
    send_select = (
        my_live[None, None, :]
        & (my_owner[None, None, :] == shard_rows[:, None, None])
        & (my_rank[None, None, :] == pair_ids[None, :, None])
    )
    q_blocks = q_load.reshape(capacity, row_length, query_width)
    kv_blocks = kv_load.reshape(capacity, row_length, pair_width)
    send_q = select_rows(send_select, q_blocks, "jkc,crf->jkrf")
    send_kv = select_rows(send_select, kv_blocks, "jkc,crf->jkrf")
    recv_kv = lax.all_to_all(send_kv, "inner", split_axis=0, concat_axis=0, tiled=True)
    wanted = my_index * slot_count + jnp.arange(slot_count, dtype=jnp.int32)
    take_select = jnp.any(
        live_all[None, :, None, :]
        & (pack_dest[None, :, None, :] == wanted[:, None, None, None])
        & (rank_all[None, :, None, :] == pair_ids[None, None, :, None]),
        axis=3,
    )
    kv_seq = select_rows(take_select, recv_kv, "srk,rktf->stf").reshape(
        slot_count * row_length, pair_width
    )
    tok_rows = slot_count * row_length
    owner_index = lax.axis_index(("outer", "inner"))
    outer_index = lax.axis_index("outer")
    score_scale = 1.0 / math.sqrt(head_size)
    extra_rows = 16
    seg_rows = tok_rows // pair_width
    seg_pad = jnp.zeros((extra_rows - seg_rows, pair_width), jnp.bfloat16)
    packed = jnp.concatenate(
        [kv_seq, segment_ids.astype(jnp.bfloat16).reshape(seg_rows, pair_width), seg_pad], axis=0
    )
    outer_reach = -(-(lax.axis_size("outer") * group_width // 4) // group_width)
    own_steps = list(range(0, outer_reach + 1, 2))
    partner_steps = list(range(1, outer_reach + 1, 2))
    moved = [packed if step == 0 else shifted(packed, "outer", step) for step in own_steps]
    own_stack = jnp.stack(moved)
    pair_mate = lax.ppermute(own_stack, "inner", [(i, i ^ 1) for i in range(group_width)])
    pair = jnp.stack([own_stack, pair_mate])
    send_q = lax.optimization_barrier((send_q, pair_mate))[0]
    recv_q = lax.all_to_all(send_q, "inner", split_axis=0, concat_axis=0, tiled=True)
    def step_over(value, hops):
        return lax.ppermute(
            value, "inner", [(i, (i + 2 * hops) % group_width) for i in range(group_width)]
        )

    from_left = step_over(pair, 1)
    from_right = step_over(pair, -1)
    left_half, right_half, recv_q = lax.optimization_barrier((from_left[0], from_right[1], recv_q))
    relayed = jnp.stack([step_over(left_half, 1), step_over(right_half, -1)])
    gathered = jnp.concatenate([pair, from_left, relayed, from_right])
    q_seq = select_rows(take_select, recv_q, "srk,rktf->stf").reshape(tok_rows, query_width)
    entry = jnp.arange(group_width, dtype=jnp.int32)
    inner_of = ((my_index - 2 * (entry // 2)) % group_width) ^ (entry % 2)
    parity = outer_index % 2
    outer_count = lax.axis_size("outer")
    partner_pairs = [(o, o ^ 1) for o in range(outer_count)]
    received = jnp.concatenate(
        [
            lax.ppermute(
                lax.dynamic_slice_in_dim(part, parity, len(partner_steps), axis=1),
                "outer",
                partner_pairs,
            )
            for part in (pair, from_left, relayed, from_right)
        ]
    )
    sources = [(gathered, own_steps), (received, partner_steps)]
    key_device, key_first, key_last = [], [], []
    for array, steps in sources:
        for slot, step in enumerate(steps):
            key_device.append(
                (outer_index - step) * group_width + inner_of
            )
            key_first.append(array[:, slot, tok_rows, 0])
            key_last.append(array[:, slot, tok_rows + seg_rows - 1, pair_width - 1])
    key_device = jnp.concatenate(key_device)
    key_first = jnp.concatenate(key_first)
    key_last = jnp.concatenate(key_last)
    first_seg = segment_ids[0].astype(jnp.bfloat16)
    last_seg = segment_ids[tok_rows - 1].astype(jnp.bfloat16)
    needed = (
        (key_device >= 0)
        & (key_device <= owner_index)
        & (key_last >= first_seg)
        & (key_first <= last_seg)
    )
    whole = (
        (key_device < owner_index)
        & (key_first == key_last)
        & (key_first == first_seg)
        & (first_seg == last_seg)
    )
    needed = jnp.where(needed, jnp.where(whole, 1, 2), 0).astype(jnp.int32)
    meta = jnp.concatenate([owner_index.reshape(1).astype(jnp.int32), needed, key_device])
    query_seg = segment_ids.astype(jnp.float32).reshape(tok_rows, 1)
    return attend(meta, q_seq, query_seg, gathered, received, head_count, head_size, score_scale)


def attend(meta, q_seq, query_seg, gathered, received, head_count, head_size, score_scale):
    tok_rows = q_seq.shape[0]
    group_width, first_slots, packed_rows, pair_width = gathered.shape
    second_slots = received.shape[1]
    first_count = group_width * first_slots
    block_count = first_count + group_width * second_slots
    seg_rows = tok_rows // pair_width

    def kernel(meta_ref, q_ref, qseg_ref, first_ref, second_ref, out_ref, m_ref, l_ref, acc_ref):
        b = pl.program_id(0)

        @pl.when(b == 0)
        def _():
            m_ref[...] = jnp.full(m_ref.shape, -1e30, jnp.float32)
            l_ref[...] = jnp.zeros(l_ref.shape, jnp.float32)
            acc_ref[...] = jnp.zeros(acc_ref.shape, jnp.float32)

        def absorb(kv_ref, masked_block):
            keys = kv_ref[0, 0, :tok_rows, :head_size]
            values = kv_ref[0, 0, :tok_rows, head_size:]
            if masked_block:
                own = meta_ref[0]
                device = meta_ref[1 + block_count + b]
                seg_parts = [
                    kv_ref[0, 0, tok_rows + r : tok_rows + r + 1, :].astype(jnp.float32)
                    for r in range(seg_rows)
                ]
                key_seg = jnp.concatenate(seg_parts, axis=1)
                key_pos = device * tok_rows + lax.broadcasted_iota(jnp.int32, (1, tok_rows), 1)
                query_pos = own * tok_rows + lax.broadcasted_iota(jnp.int32, (tok_rows, 1), 0)
                visible = (key_pos <= query_pos) & (key_seg == qseg_ref[...])
            for h in range(head_count):
                queries = q_ref[:, h * head_size : (h + 1) * head_size]
                scores = lax.dot_general(
                    queries, keys, (((1,), (1,)), ((), ())), preferred_element_type=jnp.float32
                )
                if masked_block:
                    scores = jnp.where(visible, scores, -1e30)
                m_prev = m_ref[h]
                m_next = jnp.maximum(m_prev, jnp.max(scores, axis=1, keepdims=True))
                factor = jnp.exp((m_prev - m_next) * score_scale)
                m_row = m_next[:, :1]
                if masked_block:
                    m_row = jnp.where(m_row == -1e30, 0.0, m_row)
                weights = jnp.exp((scores - m_row) * score_scale)
                l_ref[h] = l_ref[h] * factor + jnp.sum(weights, axis=1, keepdims=True)
                acc_ref[h] = acc_ref[h] * factor + jnp.dot(
                    weights.astype(jnp.bfloat16), values, preferred_element_type=jnp.float32
                )
                m_ref[h] = m_next

        mode = meta_ref[1 + b]
        for ref, in_range in ((first_ref, b < first_count), (second_ref, b >= first_count)):
            for masked_block, code in ((False, 1), (True, 2)):
                @pl.when(in_range & (mode == code))
                def _(ref=ref, masked_block=masked_block):
                    absorb(ref, masked_block)

        @pl.when(b == block_count - 1)
        def _():
            for h in range(head_count):
                out_ref[:, h * head_size : (h + 1) * head_size] = (
                    acc_ref[h] / l_ref[h]
                ).astype(out_ref.dtype)

    def first_map(b, meta):
        c = jnp.minimum(b, first_count - 1)
        return (c % group_width, c // group_width, 0, 0)

    def second_map(b, meta):
        c = jnp.maximum(b - first_count, 0)
        return (c % group_width, c // group_width, 0, 0)

    grid_spec = pltpu.PrefetchScalarGridSpec(
        num_scalar_prefetch=1,
        grid=(block_count,),
        in_specs=[
            pl.BlockSpec(q_seq.shape, lambda b, meta: (0, 0)),
            pl.BlockSpec(query_seg.shape, lambda b, meta: (0, 0)),
            pl.BlockSpec((1, 1, packed_rows, pair_width), first_map),
            pl.BlockSpec((1, 1, packed_rows, pair_width), second_map),
        ],
        out_specs=pl.BlockSpec(q_seq.shape, lambda b, meta: (0, 0)),
        scratch_shapes=[
            pltpu.VMEM((head_count, tok_rows, head_size), jnp.float32),
            pltpu.VMEM((head_count, tok_rows, head_size), jnp.float32),
            pltpu.VMEM((head_count, tok_rows, head_size), jnp.float32),
        ],
    )
    flops = 4 * block_count * tok_rows * tok_rows * head_size * head_count
    return pl.pallas_call(
        kernel,
        grid_spec=grid_spec,
        out_shape=jax.ShapeDtypeStruct(q_seq.shape, q_seq.dtype),
        compiler_params=pltpu.CompilerParams(dimension_semantics=("arbitrary",)),
        cost_estimate=pl.CostEstimate(
            flops=flops,
            transcendentals=block_count * tok_rows * tok_rows * head_count,
            bytes_accessed=(gathered.size + received.size) * 2 + q_seq.size * 4,
        ),
    )(meta, q_seq, query_seg, gathered, received)


def solution(mesh):
    in_specs = (
        P(("outer", "inner"), None),
        P(("outer", "inner"), None),
        P("outer", None),
        P("outer"),
        P(("outer", "inner")),
    )
    out_specs = P(("outer", "inner"), None)
    return jax.shard_map(local, mesh=mesh, in_specs=in_specs, out_specs=out_specs, check_vma=False)
```

```python
import math

import jax
import jax.numpy as jnp
from jax import lax
from jax.experimental import pallas as pl
from jax.experimental.pallas import tpu as pltpu
from jax.sharding import PartitionSpec as P


def shifted(value, axis, steps):
    count = lax.axis_size(axis)
    leading, last = (max(0, -steps), min(count, count - steps))
    return lax.ppermute(value, axis, [(source, source + steps) for source in range(leading, last)])


def select_rows(selector, blocks, pattern):
    return jnp.einsum(
        pattern, selector.astype(jnp.bfloat16), blocks, preferred_element_type=jnp.float32
    ).astype(jnp.bfloat16)


def local(q_load, kv_load, pack_dest, counts, segment_ids):
    group_width = lax.axis_size("inner")
    my_index = lax.axis_index("inner")
    capacity = pack_dest.shape[1]
    slot_count = capacity // 2
    pair_limit = -(-capacity // group_width)
    row_length = q_load.shape[0] // capacity
    query_width = q_load.shape[1]
    pair_width = kv_load.shape[1]
    head_size = pair_width // 2
    head_count = query_width // head_size
    slot_grid = lax.broadcasted_iota(jnp.int32, (group_width, capacity), 1)
    live_all = slot_grid < counts[:, None]
    owner_all = pack_dest // slot_count
    slot_numbers = jnp.arange(capacity, dtype=jnp.int32)
    earlier = slot_numbers[None, :] < slot_numbers[:, None]
    same_owner = owner_all[:, :, None] == owner_all[:, None, :]
    rank_all = jnp.sum(
        (earlier[None] & same_owner & live_all[:, None, :]).astype(jnp.int32), axis=2
    )
    shard_rows = jnp.arange(group_width, dtype=jnp.int32)
    mine_row = (shard_rows == my_index)[:, None]
    my_owner = jnp.sum(jnp.where(mine_row, owner_all, 0), axis=0)
    my_rank = jnp.sum(jnp.where(mine_row, rank_all, 0), axis=0)
    my_live = jnp.any(mine_row & live_all, axis=0)
    pair_ids = jnp.arange(pair_limit, dtype=jnp.int32)
    send_select = (
        my_live[None, None, :]
        & (my_owner[None, None, :] == shard_rows[:, None, None])
        & (my_rank[None, None, :] == pair_ids[None, :, None])
    )
    q_blocks = q_load.reshape(capacity, row_length, query_width)
    kv_blocks = kv_load.reshape(capacity, row_length, pair_width)
    send_q = select_rows(send_select, q_blocks, "jkc,crf->jkrf")
    send_kv = select_rows(send_select, kv_blocks, "jkc,crf->jkrf")
    recv_kv = lax.all_to_all(send_kv, "inner", split_axis=0, concat_axis=0, tiled=True)
    wanted = my_index * slot_count + jnp.arange(slot_count, dtype=jnp.int32)
    take_select = jnp.any(
        live_all[None, :, None, :]
        & (pack_dest[None, :, None, :] == wanted[:, None, None, None])
        & (rank_all[None, :, None, :] == pair_ids[None, None, :, None]),
        axis=3,
    )
    kv_seq = select_rows(take_select, recv_kv, "srk,rktf->stf").reshape(
        slot_count * row_length, pair_width
    )
    tok_rows = slot_count * row_length
    owner_index = lax.axis_index(("outer", "inner"))
    outer_index = lax.axis_index("outer")
    score_scale = 1.0 / math.sqrt(head_size)
    extra_rows = 16
    seg_rows = tok_rows // pair_width
    seg_pad = jnp.zeros((extra_rows - seg_rows, pair_width), jnp.bfloat16)
    packed = jnp.concatenate(
        [kv_seq, segment_ids.astype(jnp.bfloat16).reshape(seg_rows, pair_width), seg_pad], axis=0
    )
    outer_reach = -(-(lax.axis_size("outer") * group_width // 4) // group_width)
    own_steps = list(range(0, outer_reach + 1, 2))
    partner_steps = list(range(1, outer_reach + 1, 2))
    moved = [packed if step == 0 else shifted(packed, "outer", step) for step in own_steps]
    own_stack = jnp.stack(moved)
    outer_total = lax.axis_size("outer")
    mate_moved = []
    for step in own_steps:
        mate_pairs = [
            (o * group_width + i, (o + step) * group_width + (i ^ 1))
            for o in range(outer_total - step)
            for i in range(group_width)
        ]
        mate_moved.append(lax.ppermute(packed, ("outer", "inner"), mate_pairs))
    pair_mate = jnp.stack(mate_moved)
    pair = jnp.stack([own_stack, pair_mate])
    send_q = lax.optimization_barrier((send_q, pair_mate))[0]
    recv_q = lax.all_to_all(send_q, "inner", split_axis=0, concat_axis=0, tiled=True)
    def step_over(value, hops):
        return lax.ppermute(
            value, "inner", [(i, (i + 2 * hops) % group_width) for i in range(group_width)]
        )

    from_left = step_over(pair, 1)
    from_right = step_over(pair, -1)
    left_half, right_half, recv_q = lax.optimization_barrier((from_left[0], from_right[1], recv_q))
    relayed = jnp.stack([step_over(left_half, 1), step_over(right_half, -1)])
    gathered = jnp.concatenate([pair, from_left, relayed, from_right])
    q_seq = select_rows(take_select, recv_q, "srk,rktf->stf").reshape(tok_rows, query_width)
    entry = jnp.arange(group_width, dtype=jnp.int32)
    inner_of = ((my_index - 2 * (entry // 2)) % group_width) ^ (entry % 2)
    parity = outer_index % 2
    outer_count = lax.axis_size("outer")
    partner_pairs = [(o, o ^ 1) for o in range(outer_count)]
    received = jnp.concatenate(
        [
            lax.ppermute(
                lax.dynamic_slice_in_dim(part, parity, len(partner_steps), axis=1),
                "outer",
                partner_pairs,
            )
            for part in (pair, from_left, relayed, from_right)
        ]
    )
    sources = [(gathered, own_steps), (received, partner_steps)]
    key_device, key_first, key_last = [], [], []
    for array, steps in sources:
        for slot, step in enumerate(steps):
            key_device.append(
                (outer_index - step) * group_width + inner_of
            )
            key_first.append(array[:, slot, tok_rows, 0])
            key_last.append(array[:, slot, tok_rows + seg_rows - 1, pair_width - 1])
    key_device = jnp.concatenate(key_device)
    key_first = jnp.concatenate(key_first)
    key_last = jnp.concatenate(key_last)
    first_seg = segment_ids[0].astype(jnp.bfloat16)
    last_seg = segment_ids[tok_rows - 1].astype(jnp.bfloat16)
    needed = (
        (key_device >= 0)
        & (key_device <= owner_index)
        & (key_last >= first_seg)
        & (key_first <= last_seg)
    )
    whole = (
        (key_device < owner_index)
        & (key_first == key_last)
        & (key_first == first_seg)
        & (first_seg == last_seg)
    )
    needed = jnp.where(needed, jnp.where(whole, 1, 2), 0).astype(jnp.int32)
    meta = jnp.concatenate([owner_index.reshape(1).astype(jnp.int32), needed, key_device])
    query_seg = segment_ids.astype(jnp.float32).reshape(tok_rows, 1)
    return attend(meta, q_seq, query_seg, gathered, received, head_count, head_size, score_scale)


def attend(meta, q_seq, query_seg, gathered, received, head_count, head_size, score_scale):
    tok_rows = q_seq.shape[0]
    group_width, first_slots, packed_rows, pair_width = gathered.shape
    second_slots = received.shape[1]
    first_count = group_width * first_slots
    block_count = first_count + group_width * second_slots
    seg_rows = tok_rows // pair_width

    def kernel(meta_ref, q_ref, qseg_ref, first_ref, second_ref, out_ref, m_ref, l_ref, acc_ref):
        b = pl.program_id(0)

        @pl.when(b == 0)
        def _():
            m_ref[...] = jnp.full(m_ref.shape, -1e30, jnp.float32)
            l_ref[...] = jnp.zeros(l_ref.shape, jnp.float32)
            acc_ref[...] = jnp.zeros(acc_ref.shape, jnp.float32)

        def absorb(kv_ref, masked_block):
            keys = kv_ref[0, 0, :tok_rows, :head_size]
            values = kv_ref[0, 0, :tok_rows, head_size:]
            if masked_block:
                own = meta_ref[0]
                device = meta_ref[1 + block_count + b]
                seg_parts = [
                    kv_ref[0, 0, tok_rows + r : tok_rows + r + 1, :].astype(jnp.float32)
                    for r in range(seg_rows)
                ]
                key_seg = jnp.concatenate(seg_parts, axis=1)
                key_pos = device * tok_rows + lax.broadcasted_iota(jnp.int32, (1, tok_rows), 1)
                query_pos = own * tok_rows + lax.broadcasted_iota(jnp.int32, (tok_rows, 1), 0)
                visible = (key_pos <= query_pos) & (key_seg == qseg_ref[...])
            for h in range(head_count):
                queries = q_ref[:, h * head_size : (h + 1) * head_size]
                scores = lax.dot_general(
                    queries, keys, (((1,), (1,)), ((), ())), preferred_element_type=jnp.float32
                )
                if masked_block:
                    scores = jnp.where(visible, scores, -1e30)
                m_prev = m_ref[h]
                m_next = jnp.maximum(m_prev, jnp.max(scores, axis=1, keepdims=True))
                factor = jnp.exp((m_prev - m_next) * score_scale)
                m_row = m_next[:, :1]
                if masked_block:
                    m_row = jnp.where(m_row == -1e30, 0.0, m_row)
                weights = jnp.exp((scores - m_row) * score_scale)
                l_ref[h] = l_ref[h] * factor + jnp.sum(weights, axis=1, keepdims=True)
                acc_ref[h] = acc_ref[h] * factor + jnp.dot(
                    weights.astype(jnp.bfloat16), values, preferred_element_type=jnp.float32
                )
                m_ref[h] = m_next

        mode = meta_ref[1 + b]
        for ref, in_range in ((first_ref, b < first_count), (second_ref, b >= first_count)):
            for masked_block, code in ((False, 1), (True, 2)):
                @pl.when(in_range & (mode == code))
                def _(ref=ref, masked_block=masked_block):
                    absorb(ref, masked_block)

        @pl.when(b == block_count - 1)
        def _():
            for h in range(head_count):
                out_ref[:, h * head_size : (h + 1) * head_size] = (
                    acc_ref[h] / l_ref[h]
                ).astype(out_ref.dtype)

    def first_map(b, meta):
        c = jnp.minimum(b, first_count - 1)
        return (c % group_width, c // group_width, 0, 0)

    def second_map(b, meta):
        c = jnp.maximum(b - first_count, 0)
        return (c % group_width, c // group_width, 0, 0)

    grid_spec = pltpu.PrefetchScalarGridSpec(
        num_scalar_prefetch=1,
        grid=(block_count,),
        in_specs=[
            pl.BlockSpec(q_seq.shape, lambda b, meta: (0, 0)),
            pl.BlockSpec(query_seg.shape, lambda b, meta: (0, 0)),
            pl.BlockSpec((1, 1, packed_rows, pair_width), first_map),
            pl.BlockSpec((1, 1, packed_rows, pair_width), second_map),
        ],
        out_specs=pl.BlockSpec(q_seq.shape, lambda b, meta: (0, 0)),
        scratch_shapes=[
            pltpu.VMEM((head_count, tok_rows, head_size), jnp.float32),
            pltpu.VMEM((head_count, tok_rows, head_size), jnp.float32),
            pltpu.VMEM((head_count, tok_rows, head_size), jnp.float32),
        ],
    )
    flops = 4 * block_count * tok_rows * tok_rows * head_size * head_count
    return pl.pallas_call(
        kernel,
        grid_spec=grid_spec,
        out_shape=jax.ShapeDtypeStruct(q_seq.shape, q_seq.dtype),
        compiler_params=pltpu.CompilerParams(dimension_semantics=("arbitrary",)),
        cost_estimate=pl.CostEstimate(
            flops=flops,
            transcendentals=block_count * tok_rows * tok_rows * head_count,
            bytes_accessed=(gathered.size + received.size) * 2 + q_seq.size * 4,
        ),
    )(meta, q_seq, query_seg, gathered, received)


def solution(mesh):
    in_specs = (
        P(("outer", "inner"), None),
        P(("outer", "inner"), None),
        P("outer", None),
        P("outer"),
        P(("outer", "inner")),
    )
    out_specs = P(("outer", "inner"), None)
    return jax.shard_map(local, mesh=mesh, in_specs=in_specs, out_specs=out_specs, check_vma=False)
```

```python
import math

import jax
import jax.numpy as jnp
from jax import lax
from jax.experimental import pallas as pl
from jax.experimental.pallas import tpu as pltpu
from jax.sharding import PartitionSpec as P


def shifted(value, axis, steps):
    count = lax.axis_size(axis)
    leading, last = (max(0, -steps), min(count, count - steps))
    return lax.ppermute(value, axis, [(source, source + steps) for source in range(leading, last)])


def select_rows(selector, blocks, pattern):
    return jnp.einsum(
        pattern, selector.astype(jnp.bfloat16), blocks, preferred_element_type=jnp.float32
    ).astype(jnp.bfloat16)


def local(q_load, kv_load, pack_dest, counts, segment_ids):
    group_width = lax.axis_size("inner")
    my_index = lax.axis_index("inner")
    capacity = pack_dest.shape[1]
    slot_count = capacity // 2
    pair_limit = -(-capacity // group_width)
    row_length = q_load.shape[0] // capacity
    query_width = q_load.shape[1]
    pair_width = kv_load.shape[1]
    head_size = pair_width // 2
    head_count = query_width // head_size
    slot_grid = lax.broadcasted_iota(jnp.int32, (group_width, capacity), 1)
    live_all = slot_grid < counts[:, None]
    owner_all = pack_dest // slot_count
    slot_numbers = jnp.arange(capacity, dtype=jnp.int32)
    earlier = slot_numbers[None, :] < slot_numbers[:, None]
    same_owner = owner_all[:, :, None] == owner_all[:, None, :]
    rank_all = jnp.sum(
        (earlier[None] & same_owner & live_all[:, None, :]).astype(jnp.int32), axis=2
    )
    shard_rows = jnp.arange(group_width, dtype=jnp.int32)
    mine_row = (shard_rows == my_index)[:, None]
    my_owner = jnp.sum(jnp.where(mine_row, owner_all, 0), axis=0)
    my_rank = jnp.sum(jnp.where(mine_row, rank_all, 0), axis=0)
    my_live = jnp.any(mine_row & live_all, axis=0)
    pair_ids = jnp.arange(pair_limit, dtype=jnp.int32)
    send_select = (
        my_live[None, None, :]
        & (my_owner[None, None, :] == shard_rows[:, None, None])
        & (my_rank[None, None, :] == pair_ids[None, :, None])
    )
    q_blocks = q_load.reshape(capacity, row_length, query_width)
    kv_blocks = kv_load.reshape(capacity, row_length, pair_width)
    send_q = select_rows(send_select, q_blocks, "jkc,crf->jkrf")
    send_kv = select_rows(send_select, kv_blocks, "jkc,crf->jkrf")
    recv_kv = lax.all_to_all(send_kv, "inner", split_axis=0, concat_axis=0, tiled=True)
    wanted = my_index * slot_count + jnp.arange(slot_count, dtype=jnp.int32)
    take_select = jnp.any(
        live_all[None, :, None, :]
        & (pack_dest[None, :, None, :] == wanted[:, None, None, None])
        & (rank_all[None, :, None, :] == pair_ids[None, None, :, None]),
        axis=3,
    )
    kv_seq = select_rows(take_select, recv_kv, "srk,rktf->stf").reshape(
        slot_count * row_length, pair_width
    )
    tok_rows = slot_count * row_length
    owner_index = lax.axis_index(("outer", "inner"))
    outer_index = lax.axis_index("outer")
    score_scale = 1.0 / math.sqrt(head_size)
    extra_rows = 16
    seg_rows = tok_rows // pair_width
    seg_pad = jnp.zeros((extra_rows - seg_rows, pair_width), jnp.bfloat16)
    packed = jnp.concatenate(
        [kv_seq, segment_ids.astype(jnp.bfloat16).reshape(seg_rows, pair_width), seg_pad], axis=0
    )
    outer_reach = -(-(lax.axis_size("outer") * group_width // 4) // group_width)
    own_steps = list(range(0, outer_reach + 1, 2))
    partner_steps = list(range(1, outer_reach + 1, 2))
    moved = [packed if step == 0 else shifted(packed, "outer", step) for step in own_steps]
    own_stack = jnp.stack(moved)
    outer_total = lax.axis_size("outer")
    mate_moved = []
    for step in own_steps:
        mate_pairs = [
            (o * group_width + i, (o + step) * group_width + (i ^ 1))
            for o in range(outer_total - step)
            for i in range(group_width)
        ]
        mate_moved.append(lax.ppermute(packed, ("outer", "inner"), mate_pairs))
    pair_mate = jnp.stack(mate_moved)
    pair = jnp.stack([own_stack, pair_mate])
    send_q = lax.optimization_barrier((send_q, pair_mate))[0]
    recv_q = lax.all_to_all(send_q, "inner", split_axis=0, concat_axis=0, tiled=True)
    def step_over(value, hops):
        return lax.ppermute(
            value, "inner", [(i, (i + 2 * hops) % group_width) for i in range(group_width)]
        )

    from_left = step_over(pair, 1)
    from_right = step_over(pair, -1)
    left_half, right_half, recv_q = lax.optimization_barrier((from_left[0], from_right[1], recv_q))
    relayed = jnp.stack([step_over(left_half, 1), step_over(right_half, -1)])
    gathered = jnp.concatenate([pair, from_left, relayed, from_right])
    q_seq = select_rows(take_select, recv_q, "srk,rktf->stf").reshape(tok_rows, query_width)
    entry = jnp.arange(group_width, dtype=jnp.int32)
    inner_of = ((my_index - 2 * (entry // 2)) % group_width) ^ (entry % 2)
    parity = outer_index % 2
    outer_count = lax.axis_size("outer")
    partner_pairs = [(o, o ^ 1) for o in range(outer_count)]
    received = jnp.concatenate(
        [
            lax.ppermute(
                lax.dynamic_slice_in_dim(part, parity, len(partner_steps), axis=1),
                "outer",
                partner_pairs,
            )
            for part in (pair, from_left, relayed, from_right)
        ]
    )
    sources = [(gathered, own_steps), (received, partner_steps)]
    key_device, key_first, key_last = [], [], []
    for array, steps in sources:
        for slot, step in enumerate(steps):
            key_device.append(
                (outer_index - step) * group_width + inner_of
            )
            key_first.append(array[:, slot, tok_rows, 0])
            key_last.append(array[:, slot, tok_rows + seg_rows - 1, pair_width - 1])
    key_device = jnp.concatenate(key_device)
    key_first = jnp.concatenate(key_first)
    key_last = jnp.concatenate(key_last)
    first_seg = segment_ids[0].astype(jnp.bfloat16)
    last_seg = segment_ids[tok_rows - 1].astype(jnp.bfloat16)
    needed = (
        (key_device >= 0)
        & (key_device <= owner_index)
        & (key_last >= first_seg)
        & (key_first <= last_seg)
    )
    whole = (
        (key_device < owner_index)
        & (key_first == key_last)
        & (key_first == first_seg)
        & (first_seg == last_seg)
    )
    needed = jnp.where(needed, jnp.where(whole, 1, 2), 0).astype(jnp.int32)
    step_ids = jnp.arange(needed.shape[0], dtype=jnp.int32)
    first_total = gathered.shape[0] * gathered.shape[1]
    live_step = needed > 0
    fetch_first = lax.cummax(jnp.where(live_step & (step_ids < first_total), step_ids, 0))
    fetch_second = lax.cummax(
        jnp.where(live_step & (step_ids >= first_total), step_ids - first_total, 0)
    )
    meta = jnp.concatenate(
        [owner_index.reshape(1).astype(jnp.int32), needed, key_device, fetch_first, fetch_second]
    )
    query_seg = segment_ids.astype(jnp.float32).reshape(tok_rows, 1)
    return attend(meta, q_seq, query_seg, gathered, received, head_count, head_size, score_scale)


def attend(meta, q_seq, query_seg, gathered, received, head_count, head_size, score_scale):
    tok_rows = q_seq.shape[0]
    group_width, first_slots, packed_rows, pair_width = gathered.shape
    second_slots = received.shape[1]
    first_count = group_width * first_slots
    block_count = first_count + group_width * second_slots
    seg_rows = tok_rows // pair_width

    def kernel(meta_ref, q_ref, qseg_ref, first_ref, second_ref, out_ref, m_ref, l_ref, acc_ref):
        b = pl.program_id(0)

        @pl.when(b == 0)
        def _():
            m_ref[...] = jnp.full(m_ref.shape, -1e30, jnp.float32)
            l_ref[...] = jnp.zeros(l_ref.shape, jnp.float32)
            acc_ref[...] = jnp.zeros(acc_ref.shape, jnp.float32)

        def absorb(kv_ref, masked_block):
            keys = kv_ref[0, 0, :tok_rows, :head_size]
            values = kv_ref[0, 0, :tok_rows, head_size:]
            if masked_block:
                own = meta_ref[0]
                device = meta_ref[1 + block_count + b]
                seg_parts = [
                    kv_ref[0, 0, tok_rows + r : tok_rows + r + 1, :].astype(jnp.float32)
                    for r in range(seg_rows)
                ]
                key_seg = jnp.concatenate(seg_parts, axis=1)
                key_pos = device * tok_rows + lax.broadcasted_iota(jnp.int32, (1, tok_rows), 1)
                query_pos = own * tok_rows + lax.broadcasted_iota(jnp.int32, (tok_rows, 1), 0)
                visible = (key_pos <= query_pos) & (key_seg == qseg_ref[...])
            for h in range(head_count):
                queries = q_ref[:, h * head_size : (h + 1) * head_size]
                scores = lax.dot_general(
                    queries, keys, (((1,), (1,)), ((), ())), preferred_element_type=jnp.float32
                )
                if masked_block:
                    scores = jnp.where(visible, scores, -1e30)
                m_prev = m_ref[h]
                m_next = jnp.maximum(m_prev, jnp.max(scores, axis=1, keepdims=True))
                factor = jnp.exp((m_prev - m_next) * score_scale)
                m_row = m_next[:, :1]
                if masked_block:
                    m_row = jnp.where(m_row == -1e30, 0.0, m_row)
                weights = jnp.exp((scores - m_row) * score_scale)
                l_ref[h] = l_ref[h] * factor + jnp.sum(weights, axis=1, keepdims=True)
                acc_ref[h] = acc_ref[h] * factor + jnp.dot(
                    weights.astype(jnp.bfloat16), values, preferred_element_type=jnp.float32
                )
                m_ref[h] = m_next

        mode = meta_ref[1 + b]
        for ref, in_range in ((first_ref, b < first_count), (second_ref, b >= first_count)):
            for masked_block, code in ((False, 1), (True, 2)):
                @pl.when(in_range & (mode == code))
                def _(ref=ref, masked_block=masked_block):
                    absorb(ref, masked_block)

        @pl.when(b == block_count - 1)
        def _():
            for h in range(head_count):
                out_ref[:, h * head_size : (h + 1) * head_size] = (
                    acc_ref[h] / l_ref[h]
                ).astype(out_ref.dtype)

    def first_map(b, meta):
        c = meta[1 + 2 * block_count + b]
        return (c % group_width, c // group_width, 0, 0)

    def second_map(b, meta):
        c = meta[1 + 3 * block_count + b]
        return (c % group_width, c // group_width, 0, 0)

    grid_spec = pltpu.PrefetchScalarGridSpec(
        num_scalar_prefetch=1,
        grid=(block_count,),
        in_specs=[
            pl.BlockSpec(q_seq.shape, lambda b, meta: (0, 0)),
            pl.BlockSpec(query_seg.shape, lambda b, meta: (0, 0)),
            pl.BlockSpec((1, 1, packed_rows, pair_width), first_map),
            pl.BlockSpec((1, 1, packed_rows, pair_width), second_map),
        ],
        out_specs=pl.BlockSpec(q_seq.shape, lambda b, meta: (0, 0)),
        scratch_shapes=[
            pltpu.VMEM((head_count, tok_rows, head_size), jnp.float32),
            pltpu.VMEM((head_count, tok_rows, head_size), jnp.float32),
            pltpu.VMEM((head_count, tok_rows, head_size), jnp.float32),
        ],
    )
    flops = 4 * block_count * tok_rows * tok_rows * head_size * head_count
    return pl.pallas_call(
        kernel,
        grid_spec=grid_spec,
        out_shape=jax.ShapeDtypeStruct(q_seq.shape, q_seq.dtype),
        compiler_params=pltpu.CompilerParams(dimension_semantics=("arbitrary",)),
        cost_estimate=pl.CostEstimate(
            flops=flops,
            transcendentals=block_count * tok_rows * tok_rows * head_count,
            bytes_accessed=(gathered.size + received.size) * 2 + q_seq.size * 4,
        ),
    )(meta, q_seq, query_seg, gathered, received)


def solution(mesh):
    in_specs = (
        P(("outer", "inner"), None),
        P(("outer", "inner"), None),
        P("outer", None),
        P("outer"),
        P(("outer", "inner")),
    )
    out_specs = P(("outer", "inner"), None)
    return jax.shard_map(local, mesh=mesh, in_specs=in_specs, out_specs=out_specs, check_vma=False)
```
